32 devices in a mesh: dp: 2 (over core), expert: 16 (over z, y, x).
Axes of the slice: x: 2, y: 2, z: 4, core: 2. Of those that a mesh axis runs over, the one named last changes fastest.
Arguments:
- tokens: bfloat16 [1024, 3584], P(('dp', 'expert')), may hold values from -6 to 6
- out_grad: bfloat16 [1024, 3584], P(('dp', 'expert')), may hold values from -6 to 6
- expert_ids: int32 [1024, 8], P(('dp', 'expert')), may hold values from 0 to 15, all different within a row; in each aligned block of 32 rows (0 to 31, 32 to 63, ...) at most 20 rows name the same one
- gate_probs: float32 [1024, 8], P(('dp', 'expert')), may hold values from 0.2 to 1.5
- weights: bfloat16 [16, 3584, 3, 128], P('expert', 'dp'), may hold values from -0.09375 to 0.09375
- first_moment: bfloat16 [16, 3584, 3, 128], P('expert', 'dp'), may hold values from -6 to 6
- second_moment: bfloat16 [16, 3584, 3, 128], P('expert', 'dp'), may hold values from 0.5 to 5
- moving_pairs: int32 [8], replicated, may hold values from 0 to 1, as said below
Outputs:
- token_grad: bfloat16 [1024, 3584], P(('dp', 'expert'))
- prob_grad: bfloat16 [1024, 8], P(('dp', 'expert'))
- moved_weights: bfloat16 [16, 3584, 3, 128], P('expert', 'dp')
- weight_grad: float32 [16, 3584, 3, 128], P('expert', 'dp')
- new_first: bfloat16 [16, 3584, 3, 128], P('expert', 'dp')
- new_second: bfloat16 [16, 3584, 3, 128], P('expert', 'dp')
The draws below stay inside these ranges and needn't reach their ends.
Inputs may be any that keep to these rules, and one draw needn't show every extreme that they name: `expert_ids`: each row names 8 different experts. Among the entries of the 32 rows of one device, no expert is named more than 20 times, a bound that some block reaches. `moving_pairs`: entry p is 1 where devices p and p + 8 of the expert axis exchange their experts. The last entry is always 1.
All inputs are finite; a program needn't handle non-finite values.
Results may differ from the reference program's by a relative error of at most 0.018.
Values may be sent and summed in bfloat16 or wider, within the bound.
No kernel may reach another device: no remote copies, remote signals or barrier semaphores. Data moves between devices by JAX's collectives and lax.ppermute only.
A program may use at most 64 MiB of HBM per device.

```python
import math
import jax
import jax.numpy as jnp
import numpy as np
from jax import lax

D = 3584
HS = 128
TOP = 8
TOK_DEV = 32
EXPERTS = 16
HALF = 8
MOST = 20
SLOTS = 320
TOKENS = 1024
N_DP = 2
N_EXPERT = 16


def draw_moving_pairs(key, part):
    bits = jax.random.randint(jax.random.fold_in(key, 17), (HALF,), 0, 2, dtype=jnp.int32)
    return bits.at[HALF - 1].set(1)


def level_of(own_key, dims, pieces, smallest, top_value):
    def one(dim, shards_of):
        steps = jax.random.uniform(jax.random.fold_in(jax.random.fold_in(own_key, 6), dim), (shards_of,), jnp.float32, smallest / len(pieces), top_value / len(pieces))
        return jnp.repeat(jnp.exp(steps), dims[dim] // shards_of).reshape((-1,) + (1,) * (len(dims) - dim - 1))

    gain = one(*pieces[0])
    for cut in pieces[1:]:
        gain = gain * one(*cut)
    return gain


def shared_out(stream_key, own, number, rows, count, top, reach, lean):
    ranking = jax.random.permutation(stream_key, count)
    packed, usual = load_shares(count, rows * top, reach, lean, True), load_shares(count, rows * top, reach, lean, False)
    places = jnp.arange(count)

    def named(lengths, rotation):
        used = int((lengths > 0).sum())
        fixed = max(1, used // 4)
        moved = fixed + (places - fixed + rotation * (used - fixed)) % max(1, count - fixed)
        return jnp.zeros((count,), jnp.int32).at[ranking[jnp.where(places < fixed, places, moved)]].set(jnp.asarray(lengths, jnp.int32))

    lengths = jnp.where(number % 4 == 0, named(packed, number // 4), named(usual, number - number // 4 - 1))
    mixed = jax.random.permutation(jax.random.fold_in(own, 3), count)
    source_of, receiver = mixed[0:count // 2 * 2:2], mixed[1:count // 2 * 2:2]
    room = jnp.minimum(lengths[source_of] - 1, reach - lengths[receiver]) // 2
    room = jnp.where((source_of == ranking[0]) | (receiver == ranking[0]) | (lengths[receiver] == 0), 0, jnp.maximum(room, 0))
    moved = jax.random.randint(jax.random.fold_in(own, 4), (count // 2,), 0, 1 << 20) % (room + 1)
    lengths = lengths.at[source_of].add(-moved).at[receiver].add(moved)
    members = jnp.searchsorted(jnp.cumsum(lengths), jnp.arange(rows * top), side="right").astype(jnp.int32)
    listing = members.reshape(top, rows).T
    listing = listing[jax.random.permutation(jax.random.fold_in(own, 1), rows)]
    rotation = jax.random.randint(jax.random.fold_in(own, 2), (rows, 1), 0, top)
    return jnp.take_along_axis(listing, (jnp.arange(top)[None, :] + rotation) % top, axis=1)


def load_shares(number_of, total, reach, slope, full):
    portions = [(1 << 20) // math.isqrt(standing ** slope) + 1 for standing in range(1, number_of + 1)]
    largest = reach if full else min(reach, max(-(-total // number_of), total * portions[0] // sum(portions)))
    least = 1 if total - largest >= number_of - 1 else 0
    given, spare = [largest] + [least] * (number_of - 1), total - largest - least * (number_of - 1)
    while spare > 0:
        movable = [i for i in range(1, number_of) if given[i] < largest] or [i for i in range(1, number_of) if given[i] < reach]
        mass, remaining = sum([portions[i] for i in movable]), spare
        for i in movable:
            extra = min(reach - given[i], max(1, remaining * portions[i] // mass), spare)
            given[i] = given[i] + extra
            spare = spare - extra
    return np.array(given)


def centred(key, extent, spread, most, pieces=(), kind=jnp.bfloat16):
    factor_of = level_of(key, extent, pieces, -0.22, 0.18) if pieces else 1.0
    result = jax.random.normal(key, extent, jnp.float32) * spread * factor_of
    return jnp.minimum(jnp.maximum(result, -most), most).astype(kind)


def setup_inputs(seed: int = 0) -> dict:
    streams_of = jax.random.split(jax.random.key(seed), 9)
    tokens = centred(streams_of[0], (TOKENS, D), 1.0, 6.0, ((0, 32),))
    out_grad = centred(streams_of[1], (TOKENS, D), 1.0, 6.0, ((0, 32),))
    expert_ids_keys = jax.random.split(jax.random.fold_in(streams_of[2], 1), TOKENS // TOK_DEV)
    expert_ids_turns = jax.random.permutation(jax.random.fold_in(streams_of[2], 3), TOKENS // TOK_DEV)
    expert_ids = jax.vmap(lambda own, number: shared_out(jax.random.fold_in(streams_of[2], 2), own, number, TOK_DEV, EXPERTS, TOP, MOST, 2))(expert_ids_keys, expert_ids_turns).reshape((TOKENS, TOP))
    gate_probs = jnp.clip(0.2 + 1.3 * jax.random.uniform(streams_of[3], (TOKENS, TOP), jnp.float32) ** level_of(streams_of[3], (TOKENS, TOP), ((0, 32),), -0.2, 0.2), 0.2, 1.5)
    weights = centred(streams_of[4], (EXPERTS, D, 3, HS), D ** -0.5, 0.09375, ((0, 16), (1, 2)))
    first_moment = centred(streams_of[5], (EXPERTS, D, 3, HS), 1.0, 6.0, ((0, 16), (1, 2)))
    second_moment = jnp.clip(jnp.exp(math.log(5.0) - 2.3025851 * jax.random.uniform(streams_of[6], (EXPERTS, D, 3, HS), jnp.float32) ** level_of(streams_of[6], (EXPERTS, D, 3, HS), ((0, 16), (1, 2)), -0.2, 0.2)), 0.5, 5.0).astype(jnp.bfloat16)
    moving_pairs = draw_moving_pairs(jax.random.fold_in(streams_of[8], 71), 0)
    return {"tokens": tokens, "out_grad": out_grad, "expert_ids": expert_ids, "gate_probs": gate_probs, "weights": weights, "first_moment": first_moment, "second_moment": second_moment, "moving_pairs": moving_pairs}


def silu_parts(pre_gate):
    sig = jax.nn.sigmoid(pre_gate)
    return pre_gate * sig, sig * (1.0 + pre_gate * (1.0 - sig))


def expert_pass(rows, grads_in, gates, slab):
    w_gate = slab[:, 0, :]
    w_up = slab[:, 1, :]
    w_down = slab[:, 2, :]
    pre_gate = jnp.dot(rows, w_gate, preferred_element_type=jnp.float32)
    pre_up = jnp.dot(rows, w_up, preferred_element_type=jnp.float32)
    activated, act_slope = silu_parts(pre_gate)
    hidden = (activated * pre_up).astype(jnp.bfloat16)
    expert_out = lax.dot_general(hidden, w_down, (((1,), (1,)), ((), ())), preferred_element_type=jnp.float32)
    gate_rows = jnp.sum(expert_out * grads_in.astype(jnp.float32), axis=1).astype(jnp.bfloat16)
    scaled_grad = (gates[:, None] * grads_in.astype(jnp.float32)).astype(jnp.bfloat16)
    hidden_grad = jnp.dot(scaled_grad, w_down, preferred_element_type=jnp.float32)
    gate_delta = (hidden_grad * pre_up * act_slope).astype(jnp.bfloat16)
    up_delta = (hidden_grad * activated).astype(jnp.bfloat16)
    contract_rows = (((0,), (0,)), ((), ()))
    grad_gate = lax.dot_general(rows, gate_delta, contract_rows, preferred_element_type=jnp.float32)
    grad_up = lax.dot_general(rows, up_delta, contract_rows, preferred_element_type=jnp.float32)
    grad_down = lax.dot_general(scaled_grad, hidden, contract_rows, preferred_element_type=jnp.float32)
    contract_hidden = (((1,), (1,)), ((), ()))
    row_grad = lax.dot_general(gate_delta, w_gate, contract_hidden, preferred_element_type=jnp.float32)
    row_grad = row_grad + lax.dot_general(up_delta, w_up, contract_hidden, preferred_element_type=jnp.float32)
    return row_grad.astype(jnp.bfloat16), gate_rows, jnp.stack([grad_gate, grad_up, grad_down], axis=1)


def reference(tokens, out_grad, expert_ids, gate_probs, weights, first_moment, second_moment, moving_pairs):
    device_count = N_DP * N_EXPERT
    entries = TOK_DEV * TOP
    ids = expert_ids.reshape(device_count, entries)
    id_onehot = (ids[:, :, None] == jnp.arange(N_EXPERT, dtype=jnp.int32)[None, None, :]).astype(jnp.int32)
    id_rank = jnp.sum((jnp.cumsum(id_onehot, axis=1) - id_onehot) * id_onehot, axis=2).astype(jnp.int32)
    device_ids = jnp.arange(device_count, dtype=jnp.int32)[:, None]
    entry_code = device_ids * entries + jnp.arange(entries, dtype=jnp.int32)[None, :]
    group_ids = jnp.broadcast_to(device_ids // N_EXPERT, ids.shape)
    source_dev = jnp.broadcast_to(device_ids % N_EXPERT, ids.shape)
    slot_table = jnp.full((N_DP, N_EXPERT, N_EXPERT, MOST), -1, jnp.int32)
    slot_table = slot_table.at[group_ids, ids, source_dev, id_rank].set(entry_code)
    slot_table = slot_table.reshape(N_DP, N_EXPERT, SLOTS)
    flat_gate = gate_probs.reshape(-1)
    wire_gate = lax.optimization_barrier(flat_gate.astype(jnp.bfloat16)).astype(jnp.float32)

    def per_expert(totals, expert_id):
        token_acc, prob_acc = totals
        slab = weights[expert_id]

        def per_group(state, group_id):
            token_acc, prob_acc, grad_acc = state
            entry_ids = slot_table[group_id, expert_id]
            filled = entry_ids >= 0
            safe_ids = jnp.where(filled, entry_ids, 0)
            token_row = safe_ids // TOP
            rows = jnp.where(filled[:, None], tokens[token_row], jnp.zeros((), jnp.bfloat16))
            grads_in = jnp.where(filled[:, None], out_grad[token_row], jnp.zeros((), jnp.bfloat16))
            gates = jnp.where(filled, wire_gate[safe_ids], jnp.float32(0.0))
            row_grad, gate_rows, part = expert_pass(rows, grads_in, gates, slab)
            target = jnp.where(filled, token_row, TOKENS)
            weight_of = jnp.where(filled, flat_gate[safe_ids], jnp.float32(0.0))
            token_acc = token_acc.at[target].add(weight_of[:, None] * row_grad.astype(jnp.float32))
            prob_acc = prob_acc.at[jnp.where(filled, safe_ids, TOKENS * TOP)].set(gate_rows.astype(jnp.float32))
            grad_acc = grad_acc + lax.optimization_barrier(part.astype(jnp.bfloat16)).astype(jnp.float32)
            return (token_acc, prob_acc, grad_acc), None

        grad_start = jnp.zeros((D, 3, HS), jnp.float32)
        (token_acc, prob_acc, grad_acc), _ = lax.scan(per_group, (token_acc, prob_acc, grad_start), jnp.arange(N_DP, dtype=jnp.int32))
        grad = grad_acc * (1.0 / N_DP)
        first = (0.9 * first_moment[expert_id].astype(jnp.float32) + 0.1 * grad).astype(jnp.bfloat16)
        second = (0.95 * second_moment[expert_id].astype(jnp.float32) + 0.05 * grad * grad).astype(jnp.bfloat16)
        return (token_acc, prob_acc), (grad, first, second)

    start = (jnp.zeros((TOKENS + 1, D), jnp.float32), jnp.zeros((TOKENS * TOP + 1,), jnp.float32))
    (token_acc, prob_acc), (grads, firsts, seconds) = lax.scan(per_expert, start, jnp.arange(N_EXPERT, dtype=jnp.int32))
    slot_ids = jnp.arange(N_EXPERT, dtype=jnp.int32)
    moved = moving_pairs[slot_ids % HALF]
    held = jnp.where(moved == 1, (slot_ids + HALF) % N_EXPERT, slot_ids).astype(jnp.int32)
    token_grad = token_acc[:TOKENS].astype(jnp.bfloat16)
    prob_grad = prob_acc[:TOKENS * TOP].reshape(TOKENS, TOP).astype(jnp.bfloat16)
    return (token_grad, prob_grad, weights[held], grads[held], firsts[held], seconds[held])
```

```python
import jax
import jax.numpy as jnp
from jax import lax
from jax.sharding import PartitionSpec as P


def from_partner(value, axis, bit):
    return lax.ppermute(value, axis, [(i, i ^ 1 << bit) for i in range(lax.axis_size(axis))])


def silu_parts(pre_gate):
    sig = jax.nn.sigmoid(pre_gate)
    return (pre_gate * sig, sig * (1.0 + pre_gate * (1.0 - sig)))


def on_device(
    tokens, out_grad, expert_ids, gate_probs, weights, first_moment, second_moment, moving_pairs
):
    axis_width = lax.axis_size("expert")
    half_axis = axis_width // 2
    swap_bit = half_axis.bit_length() - 1
    groups = lax.axis_size("dp")
    my_index = lax.axis_index("expert")
    tok_rows, route_count = expert_ids.shape
    model_width = tokens.shape[1]
    entry_count = tok_rows * route_count
    slot_cap = 5 * entry_count // (4 * axis_width)
    slot_count = axis_width * slot_cap
    pair_lanes = jnp.arange(half_axis, dtype=jnp.int32)
    my_move = jnp.sum(jnp.where(pair_lanes == my_index % half_axis, moving_pairs, 0))
    swapped = my_move == 1
    held = jnp.where(swapped, (my_index + half_axis) % axis_width, my_index)
    theirs = from_partner((weights, first_moment, second_moment), "expert", swap_bit)
    weights = jnp.where(swapped, theirs[0], weights)
    first_moment = jnp.where(swapped, theirs[1], first_moment)
    second_moment = jnp.where(swapped, theirs[2], second_moment)

    flat_gate = gate_probs.reshape(-1)
    all_rows = lax.all_gather(tokens, "expert", axis=0, tiled=True)
    all_grads = lax.all_gather(out_grad, "expert", axis=0, tiled=True)
    all_ids = lax.all_gather(expert_ids, "expert", axis=0, tiled=True)
    all_gate = lax.all_gather(flat_gate.astype(jnp.bfloat16), "expert", axis=0, tiled=True)

    src_ids = all_ids.reshape(axis_width, entry_count)
    hit = (src_ids == held).astype(jnp.int32)
    pos = jnp.cumsum(hit, axis=1) - hit
    ranks = jnp.arange(slot_cap, dtype=jnp.int32)
    sel = (hit[:, None, :] == 1) & (pos[:, None, :] == ranks[None, :, None])
    filled = jnp.any(sel, axis=2).reshape(slot_count)
    entry_lanes = jnp.arange(entry_count, dtype=jnp.int32)
    slot_entry = jnp.sum(jnp.where(sel, entry_lanes[None, None, :], 0), axis=2)
    src_base = (jnp.arange(axis_width, dtype=jnp.int32) * entry_count)[:, None]
    flat_entry = (slot_entry + src_base).reshape(slot_count)
    token_of = flat_entry // route_count
    rows = all_rows[token_of]
    grads_in = all_grads[token_of]
    gates = jnp.where(filled, all_gate[flat_entry].astype(jnp.float32), 0.0)

    whole = lax.all_gather(weights, "dp", axis=1, tiled=True)[0]
    w_gate = whole[:, 0, :]
    w_up = whole[:, 1, :]
    w_down = whole[:, 2, :]
    w_both = jnp.concatenate([w_gate, w_up], axis=1)
    pre_gate = jnp.dot(rows, w_gate, preferred_element_type=jnp.float32)
    pre_up = jnp.dot(rows, w_up, preferred_element_type=jnp.float32)
    activated, act_slope = silu_parts(pre_gate)
    hidden = (activated * pre_up).astype(jnp.bfloat16)
    contract_hidden = (((1,), (1,)), ((), ()))
    projected = jnp.dot(grads_in, w_down, preferred_element_type=jnp.float32)
    gate_rows = jnp.sum(hidden.astype(jnp.float32) * projected, axis=1).astype(jnp.bfloat16)
    scaled_grad = (gates[:, None] * grads_in.astype(jnp.float32)).astype(jnp.bfloat16)
    hidden_grad = jnp.dot(scaled_grad, w_down, preferred_element_type=jnp.float32)
    gate_delta = (hidden_grad * pre_up * act_slope).astype(jnp.bfloat16)
    up_delta = (hidden_grad * activated).astype(jnp.bfloat16)
    both_delta = jnp.concatenate([gate_delta, up_delta], axis=1)
    row_grad = lax.dot_general(
        both_delta, w_both, contract_hidden, preferred_element_type=jnp.float32
    )
    row_grad = row_grad.astype(jnp.bfloat16)
    back_rows, back_gate = (
        lax.all_to_all(
            row_grad.reshape(axis_width, slot_cap, model_width),
            "expert",
            split_axis=0,
            concat_axis=0,
            tiled=True,
        ),
        lax.all_to_all(
            gate_rows.reshape(axis_width, slot_cap),
            "expert",
            split_axis=0,
            concat_axis=0,
            tiled=True,
        ),
    )
    contract_rows = (((0,), (0,)), ((), ()))
    grad_gate = lax.dot_general(rows, gate_delta, contract_rows, preferred_element_type=jnp.float32)
    grad_up = lax.dot_general(rows, up_delta, contract_rows, preferred_element_type=jnp.float32)
    grad_down = lax.dot_general(
        scaled_grad, hidden, contract_rows, preferred_element_type=jnp.float32
    )
    grad = lax.psum_scatter(
        jnp.stack([grad_gate, grad_up, grad_down], axis=1).astype(jnp.bfloat16),
        "dp",
        scatter_dimension=0,
        tiled=True,
    ).astype(jnp.float32) * (1.0 / groups)
    grad = grad[None]
    new_first = (0.9 * first_moment.astype(jnp.float32) + 0.1 * grad).astype(jnp.bfloat16)
    new_second = (0.95 * second_moment.astype(jnp.float32) + 0.05 * grad * grad).astype(
        jnp.bfloat16
    )

    flat_ids = expert_ids.reshape(-1)
    lane_hit = (flat_ids % half_axis)[:, None] == pair_lanes[None, :]
    moves = jnp.sum(jnp.where(lane_hit, moving_pairs[None, :], 0), axis=1)
    target_dev = jnp.where(moves == 1, (flat_ids + half_axis) % axis_width, flat_ids)
    id_onehot = (flat_ids[:, None] == jnp.arange(axis_width, dtype=jnp.int32)[None, :]).astype(
        jnp.int32
    )
    id_rank = jnp.sum((jnp.cumsum(id_onehot, axis=0) - id_onehot) * id_onehot, axis=1)
    slot_of = target_dev * slot_cap + id_rank
    gathered = back_rows.reshape(slot_count, model_width)[slot_of].astype(jnp.float32)
    token_grad = (
        (gathered * flat_gate[:, None])
        .reshape(tok_rows, route_count, model_width)
        .sum(axis=1)
        .astype(jnp.bfloat16)
    )
    prob_grad = back_gate.reshape(slot_count)[slot_of].reshape(tok_rows, route_count)
    return (token_grad, prob_grad, weights, grad, new_first, new_second)


def solution(mesh):
    in_specs = (
        P(("dp", "expert"), None),
        P(("dp", "expert"), None),
        P(("dp", "expert"), None),
        P(("dp", "expert"), None),
        P("expert", "dp", None, None),
        P("expert", "dp", None, None),
        P("expert", "dp", None, None),
        P(),
    )
    out_specs = (
        P(("dp", "expert"), None),
        P(("dp", "expert"), None),
        P("expert", "dp", None, None),
        P("expert", "dp", None, None),
        P("expert", "dp", None, None),
        P("expert", "dp", None, None),
    )
    return jax.shard_map(
        on_device, mesh=mesh, in_specs=in_specs, out_specs=out_specs, check_vma=False
    )
```

```python
import jax
import jax.numpy as jnp
from jax import lax
from jax.sharding import PartitionSpec as P


def from_partner(value, axis, bit):
    return lax.ppermute(value, axis, [(i, i ^ 1 << bit) for i in range(lax.axis_size(axis))])


def silu_parts(pre_gate):
    sig = jax.nn.sigmoid(pre_gate)
    return (pre_gate * sig, sig * (1.0 + pre_gate * (1.0 - sig)))


def gather_slots(tokens, out_grad, expert_ids, gate_probs, held, slot_cap):
    axis_width = lax.axis_size("expert")
    tok_rows, route_count = expert_ids.shape
    model_width = tokens.shape[1]
    entry_count = tok_rows * route_count
    slot_count = axis_width * slot_cap
    side = jnp.concatenate(
        [
            expert_ids.astype(jnp.bfloat16),
            gate_probs.astype(jnp.bfloat16),
            jnp.zeros((tok_rows, 128 - 2 * route_count), jnp.bfloat16),
        ],
        axis=1,
    )
    packed = jnp.concatenate([tokens, out_grad, side], axis=1)
    all_packed = lax.all_gather(packed, "expert", axis=0, tiled=True)
    side_at = 2 * model_width
    all_ids = all_packed[:, side_at : side_at + route_count].astype(jnp.int32)
    all_gate = all_packed[:, side_at + route_count : side_at + 2 * route_count].reshape(-1)
    src_ids = all_ids.reshape(axis_width, entry_count)
    hit = (src_ids == held).astype(jnp.int32)
    pos = jnp.cumsum(hit, axis=1) - hit
    ranks = jnp.arange(slot_cap, dtype=jnp.int32)
    sel = (hit[:, None, :] == 1) & (pos[:, None, :] == ranks[None, :, None])
    filled = jnp.any(sel, axis=2).reshape(slot_count)
    entry_lanes = jnp.arange(entry_count, dtype=jnp.int32)
    slot_entry = jnp.sum(jnp.where(sel, entry_lanes[None, None, :], 0), axis=2)
    src_base = (jnp.arange(axis_width, dtype=jnp.int32) * entry_count)[:, None]
    flat_entry = (slot_entry + src_base).reshape(slot_count)
    token_of = flat_entry // route_count
    picked = all_packed[token_of]
    rows = picked[:, :model_width]
    grads_in = picked[:, model_width:side_at]
    gates = jnp.where(filled, all_gate[flat_entry].astype(jnp.float32), 0.0)
    return rows, grads_in, gates


def send_slots(tokens, out_grad, flat_gate, slot_of, slot_cap):
    axis_width = lax.axis_size("expert")
    model_width = tokens.shape[1]
    entry_count = flat_gate.shape[0]
    route_count = entry_count // tokens.shape[0]
    slot_count = axis_width * slot_cap
    slot_hit = jnp.arange(slot_count, dtype=jnp.int32)[:, None] == slot_of[None, :]
    filled = jnp.any(slot_hit, axis=1)
    entry_lanes = jnp.arange(entry_count, dtype=jnp.int32)
    slot_entry = jnp.sum(jnp.where(slot_hit, entry_lanes[None, :], 0), axis=1)
    token_of = slot_entry // route_count
    zero_row = jnp.zeros((), jnp.bfloat16)
    send_rows = jnp.where(filled[:, None], tokens[token_of], zero_row)
    send_grads = jnp.where(filled[:, None], out_grad[token_of], zero_row)
    send_gate = jnp.where(filled, flat_gate[slot_entry], 0.0).astype(jnp.bfloat16)
    moved = [
        lax.all_to_all(
            part.reshape((axis_width, slot_cap) + part.shape[1:]),
            "expert",
            split_axis=0,
            concat_axis=0,
            tiled=True,
        )
        for part in (send_rows, send_grads, send_gate)
    ]
    rows = moved[0].reshape(slot_count, model_width)
    grads_in = moved[1].reshape(slot_count, model_width)
    gates = moved[2].reshape(slot_count).astype(jnp.float32)
    return rows, grads_in, gates


def on_device(
    tokens, out_grad, expert_ids, gate_probs, weights, first_moment, second_moment, moving_pairs
):
    axis_width = lax.axis_size("expert")
    half_axis = axis_width // 2
    swap_bit = half_axis.bit_length() - 1
    groups = lax.axis_size("dp")
    my_index = lax.axis_index("expert")
    tok_rows, route_count = expert_ids.shape
    model_width = tokens.shape[1]
    entry_count = tok_rows * route_count
    slot_cap = 5 * entry_count // (4 * axis_width)
    slot_count = axis_width * slot_cap
    pair_lanes = jnp.arange(half_axis, dtype=jnp.int32)
    my_move = jnp.sum(jnp.where(pair_lanes == my_index % half_axis, moving_pairs, 0))
    swapped = my_move == 1
    held = jnp.where(swapped, (my_index + half_axis) % axis_width, my_index)
    their_weights = from_partner(weights, "expert", swap_bit)
    their_moments = from_partner((first_moment, second_moment), "expert", swap_bit)
    weights = jnp.where(swapped, their_weights, weights)

    flat_gate = gate_probs.reshape(-1)
    flat_ids = expert_ids.reshape(-1)
    lane_hit = (flat_ids % half_axis)[:, None] == pair_lanes[None, :]
    moves = jnp.sum(jnp.where(lane_hit, moving_pairs[None, :], 0), axis=1)
    target_dev = jnp.where(moves == 1, (flat_ids + half_axis) % axis_width, flat_ids)
    id_onehot = (flat_ids[:, None] == jnp.arange(axis_width, dtype=jnp.int32)[None, :]).astype(
        jnp.int32
    )
    id_rank = jnp.sum((jnp.cumsum(id_onehot, axis=0) - id_onehot) * id_onehot, axis=1)
    slot_of = target_dev * slot_cap + id_rank
    packed_width = 2 * model_width + 128
    if axis_width * tok_rows * packed_width * 2 <= 16 * 2**20:
        rows, grads_in, gates = gather_slots(
            tokens, out_grad, expert_ids, gate_probs, held, slot_cap
        )
    else:
        rows, grads_in, gates = send_slots(
            tokens, out_grad, flat_gate, slot_of, slot_cap
        )
    whole = lax.all_gather(weights, "dp", axis=1, tiled=True)[0]
    w_gate = whole[:, 0, :]
    w_up = whole[:, 1, :]
    w_down = whole[:, 2, :]
    w_both = jnp.concatenate([w_gate, w_up], axis=1)
    pre_gate = jnp.dot(rows, w_gate, preferred_element_type=jnp.float32)
    pre_up = jnp.dot(rows, w_up, preferred_element_type=jnp.float32)
    activated, act_slope = silu_parts(pre_gate)
    hidden = (activated * pre_up).astype(jnp.bfloat16)
    contract_hidden = (((1,), (1,)), ((), ()))
    projected = jnp.dot(grads_in, w_down, preferred_element_type=jnp.float32)
    gate_rows = jnp.sum(hidden.astype(jnp.float32) * projected, axis=1).astype(jnp.bfloat16)
    scaled_grad = (gates[:, None] * grads_in.astype(jnp.float32)).astype(jnp.bfloat16)
    hidden_grad = jnp.dot(scaled_grad, w_down, preferred_element_type=jnp.float32)
    gate_delta = (hidden_grad * pre_up * act_slope).astype(jnp.bfloat16)
    up_delta = (hidden_grad * activated).astype(jnp.bfloat16)
    both_delta = jnp.concatenate([gate_delta, up_delta], axis=1)
    row_grad = lax.dot_general(
        both_delta, w_both, contract_hidden, preferred_element_type=jnp.float32
    )
    row_grad = row_grad.astype(jnp.bfloat16)
    row_grad, their_moments = lax.optimization_barrier((row_grad, their_moments))
    first_moment = jnp.where(swapped, their_moments[0], first_moment)
    second_moment = jnp.where(swapped, their_moments[1], second_moment)
    back_rows, back_gate = (
        lax.all_to_all(
            row_grad.reshape(axis_width, slot_cap, model_width),
            "expert",
            split_axis=0,
            concat_axis=0,
            tiled=True,
        ),
        lax.all_to_all(
            gate_rows.reshape(axis_width, slot_cap),
            "expert",
            split_axis=0,
            concat_axis=0,
            tiled=True,
        ),
    )
    contract_rows = (((0,), (0,)), ((), ()))
    grad_gate = lax.dot_general(rows, gate_delta, contract_rows, preferred_element_type=jnp.float32)
    grad_up = lax.dot_general(rows, up_delta, contract_rows, preferred_element_type=jnp.float32)
    grad_down = lax.dot_general(
        scaled_grad, hidden, contract_rows, preferred_element_type=jnp.float32
    )
    grad = lax.psum_scatter(
        jnp.stack([grad_gate, grad_up, grad_down], axis=1).astype(jnp.bfloat16),
        "dp",
        scatter_dimension=0,
        tiled=True,
    ).astype(jnp.float32) * (1.0 / groups)
    grad = grad[None]
    new_first = (0.9 * first_moment.astype(jnp.float32) + 0.1 * grad).astype(jnp.bfloat16)
    new_second = (0.95 * second_moment.astype(jnp.float32) + 0.05 * grad * grad).astype(
        jnp.bfloat16
    )

    gathered = back_rows.reshape(slot_count, model_width)[slot_of].astype(jnp.float32)
    token_grad = (
        (gathered * flat_gate[:, None])
        .reshape(tok_rows, route_count, model_width)
        .sum(axis=1)
        .astype(jnp.bfloat16)
    )
    prob_grad = back_gate.reshape(slot_count)[slot_of].reshape(tok_rows, route_count)
    return (token_grad, prob_grad, weights, grad, new_first, new_second)


def solution(mesh):
    in_specs = (
        P(("dp", "expert"), None),
        P(("dp", "expert"), None),
        P(("dp", "expert"), None),
        P(("dp", "expert"), None),
        P("expert", "dp", None, None),
        P("expert", "dp", None, None),
        P("expert", "dp", None, None),
        P(),
    )
    out_specs = (
        P(("dp", "expert"), None),
        P(("dp", "expert"), None),
        P("expert", "dp", None, None),
        P("expert", "dp", None, None),
        P("expert", "dp", None, None),
        P("expert", "dp", None, None),
    )
    return jax.shard_map(
        on_device, mesh=mesh, in_specs=in_specs, out_specs=out_specs, check_vma=False
    )
```

```python
import jax
import jax.numpy as jnp
from jax import lax
from jax.sharding import PartitionSpec as P


def from_partner(value, axis, bit):
    return lax.ppermute(value, axis, [(i, i ^ 1 << bit) for i in range(lax.axis_size(axis))])


def silu_parts(pre_gate):
    sig = jax.nn.sigmoid(pre_gate)
    return (pre_gate * sig, sig * (1.0 + pre_gate * (1.0 - sig)))


def send_slots(tokens, out_grad, flat_gate, slot_of, slot_cap):
    axis_width = lax.axis_size("expert")
    model_width = tokens.shape[1]
    entry_count = flat_gate.shape[0]
    route_count = entry_count // tokens.shape[0]
    slot_count = axis_width * slot_cap
    slot_hit = jnp.arange(slot_count, dtype=jnp.int32)[:, None] == slot_of[None, :]
    filled = jnp.any(slot_hit, axis=1)
    entry_lanes = jnp.arange(entry_count, dtype=jnp.int32)
    slot_entry = jnp.sum(jnp.where(slot_hit, entry_lanes[None, :], 0), axis=1)
    token_of = slot_entry // route_count
    zero_row = jnp.zeros((), jnp.bfloat16)
    send_rows = jnp.where(filled[:, None], tokens[token_of], zero_row)
    send_grads = jnp.where(filled[:, None], out_grad[token_of], zero_row)
    send_gate = jnp.where(filled, flat_gate[slot_entry], 0.0).astype(jnp.bfloat16)
    moved = [
        lax.all_to_all(
            part.reshape((axis_width, slot_cap) + part.shape[1:]),
            "expert",
            split_axis=0,
            concat_axis=0,
            tiled=True,
        )
        for part in (send_rows, send_grads, send_gate)
    ]
    rows = moved[0].reshape(slot_count, model_width)
    grads_in = moved[1].reshape(slot_count, model_width)
    gates = moved[2].reshape(slot_count).astype(jnp.float32)
    return rows, grads_in, gates


def xor_permute(value, mask):
    return lax.ppermute(value, "expert", [(i, i ^ mask) for i in range(lax.axis_size("expert"))])


def entry_ranks(flat_ids, axis_width):
    id_onehot = (flat_ids[:, None] == jnp.arange(axis_width, dtype=jnp.int32)[None, :]).astype(
        jnp.int32
    )
    return jnp.sum((jnp.cumsum(id_onehot, axis=0) - id_onehot) * id_onehot, axis=1)


def on_device(
    tokens, out_grad, expert_ids, gate_probs, weights, first_moment, second_moment, moving_pairs
):
    axis_width = lax.axis_size("expert")
    half_axis = axis_width // 2
    swap_bit = half_axis.bit_length() - 1
    groups = lax.axis_size("dp")
    my_index = lax.axis_index("expert")
    tok_rows, route_count = expert_ids.shape
    model_width = tokens.shape[1]
    entry_count = tok_rows * route_count
    slot_cap = 5 * entry_count // (4 * axis_width)
    slot_count = axis_width * slot_cap
    pair_lanes = jnp.arange(half_axis, dtype=jnp.int32)
    my_move = jnp.sum(jnp.where(pair_lanes == my_index % half_axis, moving_pairs, 0))
    swapped = my_move == 1
    held = jnp.where(swapped, (my_index + half_axis) % axis_width, my_index)
    their_weights = from_partner(weights, "expert", swap_bit)
    their_moments = from_partner((first_moment, second_moment), "expert", swap_bit)
    weights = jnp.where(swapped, their_weights, weights)

    flat_gate = gate_probs.reshape(-1)
    flat_ids = expert_ids.reshape(-1)

    def holder_of(ids):
        lane_hit = (ids % half_axis)[:, None] == pair_lanes[None, :]
        moves = jnp.sum(jnp.where(lane_hit, moving_pairs[None, :], 0), axis=1)
        return jnp.where(moves == 1, (ids + half_axis) % axis_width, ids)

    two_stage = half_axis <= 8
    if two_stage:
        p_tokens, p_grads, p_ids, p_gate = from_partner(
            (tokens, out_grad, expert_ids, gate_probs), "expert", swap_bit
        )
        toks2 = jnp.concatenate([tokens, p_tokens], axis=0)
        grads2 = jnp.concatenate([out_grad, p_grads], axis=0)
        ids2 = jnp.concatenate([flat_ids, p_ids.reshape(-1)])
        gate2 = jnp.concatenate([flat_gate, p_gate.reshape(-1)])
        holder2 = holder_of(ids2)
        rank2 = jnp.concatenate(
            [entry_ranks(flat_ids, axis_width), entry_ranks(p_ids.reshape(-1), axis_width)]
        )
        src2 = jnp.arange(2 * entry_count, dtype=jnp.int32) // entry_count
        in_half = holder2 // half_axis == my_index // half_axis
        lane2 = (holder2 ^ my_index) % half_axis
        chunk = 2 * slot_cap
        slot2 = lane2 * chunk + src2 * slot_cap + rank2
        slot_hit = (
            jnp.arange(half_axis * chunk, dtype=jnp.int32)[:, None] == slot2[None, :]
        ) & in_half[None, :]
        tok_hit = jnp.any(slot_hit.reshape(half_axis * chunk, 2 * tok_rows, route_count), axis=2)
        tok_pick = tok_hit.astype(jnp.bfloat16)
        send_rows = jnp.dot(tok_pick, toks2, preferred_element_type=jnp.float32).astype(
            jnp.bfloat16
        )
        send_grads = jnp.dot(tok_pick, grads2, preferred_element_type=jnp.float32).astype(
            jnp.bfloat16
        )
        wire2 = gate2.astype(jnp.bfloat16).astype(jnp.float32)
        send_gate = jnp.sum(jnp.where(slot_hit, wire2[None, :], 0.0), axis=1)

        def spread(value):
            parts = value.reshape((half_axis, chunk) + value.shape[1:])
            moved = [parts[0]] + [xor_permute(parts[m], m) for m in range(1, half_axis)]
            return jnp.stack(moved).reshape(value.shape)

        rows, grads_in, gates = spread(send_rows), spread(send_grads), spread(send_gate)
    else:
        slot_of = holder_of(flat_ids) * slot_cap + entry_ranks(flat_ids, axis_width)
        rows, grads_in, gates = send_slots(tokens, out_grad, flat_gate, slot_of, slot_cap)
    whole = lax.all_gather(weights, "dp", axis=1, tiled=True)[0]
    w_gate = whole[:, 0, :]
    w_up = whole[:, 1, :]
    w_down = whole[:, 2, :]
    w_both = jnp.concatenate([w_gate, w_up], axis=1)
    pre_gate = jnp.dot(rows, w_gate, preferred_element_type=jnp.float32)
    pre_up = jnp.dot(rows, w_up, preferred_element_type=jnp.float32)
    activated, act_slope = silu_parts(pre_gate)
    hidden = (activated * pre_up).astype(jnp.bfloat16)
    contract_hidden = (((1,), (1,)), ((), ()))
    projected = jnp.dot(grads_in, w_down, preferred_element_type=jnp.float32)
    gate_rows = jnp.sum(hidden.astype(jnp.float32) * projected, axis=1).astype(jnp.bfloat16)
    scaled_grad = (gates[:, None] * grads_in.astype(jnp.float32)).astype(jnp.bfloat16)
    hidden_grad = jnp.dot(scaled_grad, w_down, preferred_element_type=jnp.float32)
    gate_delta = (hidden_grad * pre_up * act_slope).astype(jnp.bfloat16)
    up_delta = (hidden_grad * activated).astype(jnp.bfloat16)
    both_delta = jnp.concatenate([gate_delta, up_delta], axis=1)
    row_grad = lax.dot_general(
        both_delta, w_both, contract_hidden, preferred_element_type=jnp.float32
    )
    row_grad = row_grad.astype(jnp.bfloat16)
    row_grad, their_moments = lax.optimization_barrier((row_grad, their_moments))
    first_moment = jnp.where(swapped, their_moments[0], first_moment)
    second_moment = jnp.where(swapped, their_moments[1], second_moment)
    contract_rows = (((0,), (0,)), ((), ()))
    grad_gate = lax.dot_general(rows, gate_delta, contract_rows, preferred_element_type=jnp.float32)
    grad_up = lax.dot_general(rows, up_delta, contract_rows, preferred_element_type=jnp.float32)
    grad_down = lax.dot_general(
        scaled_grad, hidden, contract_rows, preferred_element_type=jnp.float32
    )
    grad = lax.psum_scatter(
        jnp.stack([grad_gate, grad_up, grad_down], axis=1).astype(jnp.bfloat16),
        "dp",
        scatter_dimension=0,
        tiled=True,
    ).astype(jnp.float32) * (1.0 / groups)
    grad = grad[None]
    new_first = (0.9 * first_moment.astype(jnp.float32) + 0.1 * grad).astype(jnp.bfloat16)
    new_second = (0.95 * second_moment.astype(jnp.float32) + 0.05 * grad * grad).astype(
        jnp.bfloat16
    )

    if two_stage:
        back_rows = spread(row_grad)
        back_gate = spread(gate_rows).astype(jnp.float32)
        weight_of = jnp.where(slot_hit, gate2[None, :], 0.0)
        weight_of = jnp.sum(weight_of.reshape(half_axis * chunk, 2 * tok_rows, route_count), axis=2)
        partial = lax.dot_general(
            weight_of,
            back_rows.astype(jnp.float32),
            (((0,), (0,)), ((), ())),
            precision=lax.Precision.HIGHEST,
            preferred_element_type=jnp.float32,
        )
        prob2 = jnp.sum(jnp.where(slot_hit, back_gate[:, None], 0.0), axis=0)
        p_partial, p_prob = from_partner(
            (partial[tok_rows:], prob2[entry_count:].astype(jnp.bfloat16)), "expert", swap_bit
        )
        token_grad = (partial[:tok_rows] + p_partial).astype(jnp.bfloat16)
        prob_grad = jnp.where(
            in_half[:entry_count], prob2[:entry_count], p_prob.astype(jnp.float32)
        )
        prob_grad = prob_grad.astype(jnp.bfloat16).reshape(tok_rows, route_count)
    else:
        back_rows, back_gate = [
            lax.all_to_all(
                part.reshape((axis_width, slot_cap) + part.shape[1:]),
                "expert",
                split_axis=0,
                concat_axis=0,
                tiled=True,
            )
            for part in (row_grad, gate_rows)
        ]
        gathered = back_rows.reshape(slot_count, model_width)[slot_of].astype(jnp.float32)
        token_grad = (
            (gathered * flat_gate[:, None])
            .reshape(tok_rows, route_count, model_width)
            .sum(axis=1)
            .astype(jnp.bfloat16)
        )
        prob_grad = back_gate.reshape(slot_count)[slot_of].reshape(tok_rows, route_count)
    return (token_grad, prob_grad, weights, grad, new_first, new_second)


def solution(mesh):
    in_specs = (
        P(("dp", "expert"), None),
        P(("dp", "expert"), None),
        P(("dp", "expert"), None),
        P(("dp", "expert"), None),
        P("expert", "dp", None, None),
        P("expert", "dp", None, None),
        P("expert", "dp", None, None),
        P(),
    )
    out_specs = (
        P(("dp", "expert"), None),
        P(("dp", "expert"), None),
        P("expert", "dp", None, None),
        P("expert", "dp", None, None),
        P("expert", "dp", None, None),
        P("expert", "dp", None, None),
    )
    return jax.shard_map(
        on_device, mesh=mesh, in_specs=in_specs, out_specs=out_specs, check_vma=False
    )
```

```python
import jax
import jax.numpy as jnp
from jax import lax
from jax.sharding import PartitionSpec as P


def from_partner(value, axis, bit):
    return lax.ppermute(value, axis, [(i, i ^ 1 << bit) for i in range(lax.axis_size(axis))])


def silu_parts(pre_gate):
    sig = jax.nn.sigmoid(pre_gate)
    return (pre_gate * sig, sig * (1.0 + pre_gate * (1.0 - sig)))


def send_slots(tokens, out_grad, flat_gate, slot_of, slot_cap):
    axis_width = lax.axis_size("expert")
    model_width = tokens.shape[1]
    entry_count = flat_gate.shape[0]
    route_count = entry_count // tokens.shape[0]
    slot_count = axis_width * slot_cap
    slot_hit = jnp.arange(slot_count, dtype=jnp.int32)[:, None] == slot_of[None, :]
    filled = jnp.any(slot_hit, axis=1)
    entry_lanes = jnp.arange(entry_count, dtype=jnp.int32)
    slot_entry = jnp.sum(jnp.where(slot_hit, entry_lanes[None, :], 0), axis=1)
    token_of = slot_entry // route_count
    zero_row = jnp.zeros((), jnp.bfloat16)
    send_rows = jnp.where(filled[:, None], tokens[token_of], zero_row)
    send_grads = jnp.where(filled[:, None], out_grad[token_of], zero_row)
    send_gate = jnp.where(filled, flat_gate[slot_entry], 0.0).astype(jnp.bfloat16)
    moved = [
        lax.all_to_all(
            part.reshape((axis_width, slot_cap) + part.shape[1:]),
            "expert",
            split_axis=0,
            concat_axis=0,
            tiled=True,
        )
        for part in (send_rows, send_grads, send_gate)
    ]
    rows = moved[0].reshape(slot_count, model_width)
    grads_in = moved[1].reshape(slot_count, model_width)
    gates = moved[2].reshape(slot_count).astype(jnp.float32)
    return rows, grads_in, gates


def xor_permute(value, mask):
    return lax.ppermute(value, "expert", [(i, i ^ mask) for i in range(lax.axis_size("expert"))])


def with_tile(column):
    lanes = jnp.arange(128, dtype=jnp.int32)[None, :] == 0
    return jnp.where(lanes, column.astype(jnp.bfloat16)[:, None], jnp.zeros((), jnp.bfloat16))


def entry_ranks(flat_ids, axis_width):
    id_onehot = (flat_ids[:, None] == jnp.arange(axis_width, dtype=jnp.int32)[None, :]).astype(
        jnp.int32
    )
    return jnp.sum((jnp.cumsum(id_onehot, axis=0) - id_onehot) * id_onehot, axis=1)


def on_device(
    tokens, out_grad, expert_ids, gate_probs, weights, first_moment, second_moment, moving_pairs
):
    axis_width = lax.axis_size("expert")
    half_axis = axis_width // 2
    swap_bit = half_axis.bit_length() - 1
    groups = lax.axis_size("dp")
    my_index = lax.axis_index("expert")
    tok_rows, route_count = expert_ids.shape
    model_width = tokens.shape[1]
    entry_count = tok_rows * route_count
    slot_cap = 5 * entry_count // (4 * axis_width)
    slot_count = axis_width * slot_cap
    pair_lanes = jnp.arange(half_axis, dtype=jnp.int32)
    my_move = jnp.sum(jnp.where(pair_lanes == my_index % half_axis, moving_pairs, 0))
    swapped = my_move == 1
    held = jnp.where(swapped, (my_index + half_axis) % axis_width, my_index)

    flat_gate = gate_probs.reshape(-1)
    flat_ids = expert_ids.reshape(-1)

    def holder_of(ids):
        lane_hit = (ids % half_axis)[:, None] == pair_lanes[None, :]
        moves = jnp.sum(jnp.where(lane_hit, moving_pairs[None, :], 0), axis=1)
        return jnp.where(moves == 1, (ids + half_axis) % axis_width, ids)

    two_stage = half_axis <= 8
    if two_stage:
        packed = jnp.concatenate([tokens, out_grad], axis=1)
        p_packed, p_ids, p_gate = from_partner(
            (packed, expert_ids, gate_probs), "expert", swap_bit
        )
        weights, p_packed = lax.optimization_barrier((weights, p_packed))
        both = jnp.concatenate([packed, p_packed], axis=0)
        ids2 = jnp.concatenate([flat_ids, p_ids.reshape(-1)])
        gate2 = jnp.concatenate([flat_gate, p_gate.reshape(-1)])
        holder2 = holder_of(ids2)
        rank2 = jnp.concatenate(
            [entry_ranks(flat_ids, axis_width), entry_ranks(p_ids.reshape(-1), axis_width)]
        )
        src2 = jnp.arange(2 * entry_count, dtype=jnp.int32) // entry_count
        in_half = holder2 // half_axis == my_index // half_axis
        lane2 = (holder2 ^ my_index) % half_axis
        chunk = 2 * slot_cap
        slot2 = lane2 * chunk + src2 * slot_cap + rank2
        slot_hit = (
            jnp.arange(half_axis * chunk, dtype=jnp.int32)[:, None] == slot2[None, :]
        ) & in_half[None, :]
        tok_hit = jnp.any(slot_hit.reshape(half_axis * chunk, 2 * tok_rows, route_count), axis=2)
        tok_pick = tok_hit.astype(jnp.bfloat16)
        send_both = jnp.dot(tok_pick, both, preferred_element_type=jnp.float32).astype(
            jnp.bfloat16
        )
        wire2 = gate2.astype(jnp.bfloat16).astype(jnp.float32)
        send_gate = jnp.sum(jnp.where(slot_hit, wire2[None, :], 0.0), axis=1)
        send_all = jnp.concatenate([send_both, with_tile(send_gate)], axis=1)

        def spread(value):
            parts = value.reshape((half_axis, chunk) + value.shape[1:])
            moved = [parts[0]] + [xor_permute(parts[m], m) for m in range(1, half_axis)]
            return jnp.stack(moved).reshape(value.shape)

        recv_all = spread(send_all)
        rows = recv_all[:, :model_width]
        grads_in = recv_all[:, model_width : 2 * model_width]
        gates = recv_all[:, 2 * model_width].astype(jnp.float32)
    else:
        slot_of = holder_of(flat_ids) * slot_cap + entry_ranks(flat_ids, axis_width)
        rows, grads_in, gates = send_slots(tokens, out_grad, flat_gate, slot_of, slot_cap)
    their_weights = from_partner(weights, "expert", swap_bit)
    first_moment, second_moment, _ = lax.optimization_barrier(
        (first_moment, second_moment, their_weights)
    )
    their_moments = from_partner((first_moment, second_moment), "expert", swap_bit)
    weights = jnp.where(swapped, their_weights, weights)
    whole = lax.all_gather(weights, "dp", axis=1, tiled=True)[0]
    w_gate = whole[:, 0, :]
    w_up = whole[:, 1, :]
    w_down = whole[:, 2, :]
    w_both = jnp.concatenate([w_gate, w_up], axis=1)
    pre_gate = jnp.dot(rows, w_gate, preferred_element_type=jnp.float32)
    pre_up = jnp.dot(rows, w_up, preferred_element_type=jnp.float32)
    activated, act_slope = silu_parts(pre_gate)
    hidden = (activated * pre_up).astype(jnp.bfloat16)
    contract_hidden = (((1,), (1,)), ((), ()))
    projected = jnp.dot(grads_in, w_down, preferred_element_type=jnp.float32)
    gate_rows = jnp.sum(hidden.astype(jnp.float32) * projected, axis=1).astype(jnp.bfloat16)
    scaled_grad = (gates[:, None] * grads_in.astype(jnp.float32)).astype(jnp.bfloat16)
    hidden_grad = jnp.dot(scaled_grad, w_down, preferred_element_type=jnp.float32)
    gate_delta = (hidden_grad * pre_up * act_slope).astype(jnp.bfloat16)
    up_delta = (hidden_grad * activated).astype(jnp.bfloat16)
    both_delta = jnp.concatenate([gate_delta, up_delta], axis=1)
    row_grad = lax.dot_general(
        both_delta, w_both, contract_hidden, preferred_element_type=jnp.float32
    )
    row_grad = row_grad.astype(jnp.bfloat16)
    contract_rows = (((0,), (0,)), ((), ()))
    grad_gate = lax.dot_general(rows, gate_delta, contract_rows, preferred_element_type=jnp.float32)
    grad_up = lax.dot_general(rows, up_delta, contract_rows, preferred_element_type=jnp.float32)
    grad_down = lax.dot_general(
        scaled_grad, hidden, contract_rows, preferred_element_type=jnp.float32
    )
    grad = lax.psum_scatter(
        jnp.stack([grad_gate, grad_up, grad_down], axis=1).astype(jnp.bfloat16),
        "dp",
        scatter_dimension=0,
        tiled=True,
    ).astype(jnp.float32) * (1.0 / groups)
    grad = grad[None]
    first_moment = jnp.where(swapped, their_moments[0], first_moment)
    second_moment = jnp.where(swapped, their_moments[1], second_moment)
    new_first = (0.9 * first_moment.astype(jnp.float32) + 0.1 * grad).astype(jnp.bfloat16)
    new_second = (0.95 * second_moment.astype(jnp.float32) + 0.05 * grad * grad).astype(
        jnp.bfloat16
    )

    if two_stage:
        back_all = spread(jnp.concatenate([row_grad, with_tile(gate_rows)], axis=1))
        back_rows = back_all[:, :model_width]
        back_gate = back_all[:, model_width].astype(jnp.float32)
        weight_of = jnp.where(slot_hit, gate2[None, :], 0.0)
        weight_of = jnp.sum(weight_of.reshape(half_axis * chunk, 2 * tok_rows, route_count), axis=2)
        partial = lax.dot_general(
            weight_of,
            back_rows.astype(jnp.float32),
            (((0,), (0,)), ((), ())),
            precision=lax.Precision.HIGHEST,
            preferred_element_type=jnp.float32,
        )
        prob2 = jnp.sum(jnp.where(slot_hit, back_gate[:, None], 0.0), axis=0)
        send_partial, send_prob, _ = lax.optimization_barrier(
            (partial[tok_rows:], prob2[entry_count:].astype(jnp.bfloat16), their_moments)
        )
        p_partial, p_prob = from_partner((send_partial, send_prob), "expert", swap_bit)
        token_grad = (partial[:tok_rows] + p_partial).astype(jnp.bfloat16)
        prob_grad = jnp.where(
            in_half[:entry_count], prob2[:entry_count], p_prob.astype(jnp.float32)
        )
        prob_grad = prob_grad.astype(jnp.bfloat16).reshape(tok_rows, route_count)
    else:
        back_rows, back_gate = [
            lax.all_to_all(
                part.reshape((axis_width, slot_cap) + part.shape[1:]),
                "expert",
                split_axis=0,
                concat_axis=0,
                tiled=True,
            )
            for part in (row_grad, gate_rows)
        ]
        gathered = back_rows.reshape(slot_count, model_width)[slot_of].astype(jnp.float32)
        token_grad = (
            (gathered * flat_gate[:, None])
            .reshape(tok_rows, route_count, model_width)
            .sum(axis=1)
            .astype(jnp.bfloat16)
        )
        prob_grad = back_gate.reshape(slot_count)[slot_of].reshape(tok_rows, route_count)
    return (token_grad, prob_grad, weights, grad, new_first, new_second)


def solution(mesh):
    in_specs = (
        P(("dp", "expert"), None),
        P(("dp", "expert"), None),
        P(("dp", "expert"), None),
        P(("dp", "expert"), None),
        P("expert", "dp", None, None),
        P("expert", "dp", None, None),
        P("expert", "dp", None, None),
        P(),
    )
    out_specs = (
        P(("dp", "expert"), None),
        P(("dp", "expert"), None),
        P("expert", "dp", None, None),
        P("expert", "dp", None, None),
        P("expert", "dp", None, None),
        P("expert", "dp", None, None),
    )
    return jax.shard_map(
        on_device, mesh=mesh, in_specs=in_specs, out_specs=out_specs, check_vma=False
    )
```

```python
import jax
import jax.numpy as jnp
from jax import lax
from jax.sharding import PartitionSpec as P


def from_partner(value, axis, bit):
    return lax.ppermute(value, axis, [(i, i ^ 1 << bit) for i in range(lax.axis_size(axis))])


def silu_parts(pre_gate):
    sig = jax.nn.sigmoid(pre_gate)
    return (pre_gate * sig, sig * (1.0 + pre_gate * (1.0 - sig)))


def send_slots(tokens, out_grad, flat_gate, slot_of, slot_cap):
    axis_width = lax.axis_size("expert")
    model_width = tokens.shape[1]
    entry_count = flat_gate.shape[0]
    route_count = entry_count // tokens.shape[0]
    slot_count = axis_width * slot_cap
    slot_hit = jnp.arange(slot_count, dtype=jnp.int32)[:, None] == slot_of[None, :]
    filled = jnp.any(slot_hit, axis=1)
    entry_lanes = jnp.arange(entry_count, dtype=jnp.int32)
    slot_entry = jnp.sum(jnp.where(slot_hit, entry_lanes[None, :], 0), axis=1)
    token_of = slot_entry // route_count
    zero_row = jnp.zeros((), jnp.bfloat16)
    send_rows = jnp.where(filled[:, None], tokens[token_of], zero_row)
    send_grads = jnp.where(filled[:, None], out_grad[token_of], zero_row)
    send_gate = jnp.where(filled, flat_gate[slot_entry], 0.0).astype(jnp.bfloat16)
    moved = [
        lax.all_to_all(
            part.reshape((axis_width, slot_cap) + part.shape[1:]),
            "expert",
            split_axis=0,
            concat_axis=0,
            tiled=True,
        )
        for part in (send_rows, send_grads, send_gate)
    ]
    rows = moved[0].reshape(slot_count, model_width)
    grads_in = moved[1].reshape(slot_count, model_width)
    gates = moved[2].reshape(slot_count).astype(jnp.float32)
    return rows, grads_in, gates


def xor_permute(value, mask):
    return lax.ppermute(value, "expert", [(i, i ^ mask) for i in range(lax.axis_size("expert"))])


def with_tile(column):
    lanes = jnp.arange(128, dtype=jnp.int32)[None, :] == 0
    return jnp.where(lanes, column.astype(jnp.bfloat16)[:, None], jnp.zeros((), jnp.bfloat16))


def entry_ranks(flat_ids, axis_width):
    id_onehot = (flat_ids[:, None] == jnp.arange(axis_width, dtype=jnp.int32)[None, :]).astype(
        jnp.int32
    )
    return jnp.sum((jnp.cumsum(id_onehot, axis=0) - id_onehot) * id_onehot, axis=1)


def on_device(
    tokens, out_grad, expert_ids, gate_probs, weights, first_moment, second_moment, moving_pairs
):
    axis_width = lax.axis_size("expert")
    half_axis = axis_width // 2
    swap_bit = half_axis.bit_length() - 1
    groups = lax.axis_size("dp")
    my_index = lax.axis_index("expert")
    tok_rows, route_count = expert_ids.shape
    model_width = tokens.shape[1]
    entry_count = tok_rows * route_count
    slot_cap = 5 * entry_count // (4 * axis_width)
    slot_count = axis_width * slot_cap
    pair_lanes = jnp.arange(half_axis, dtype=jnp.int32)
    my_move = jnp.sum(jnp.where(pair_lanes == my_index % half_axis, moving_pairs, 0))
    swapped = my_move == 1
    held = jnp.where(swapped, (my_index + half_axis) % axis_width, my_index)

    flat_gate = gate_probs.reshape(-1)
    flat_ids = expert_ids.reshape(-1)

    def holder_of(ids):
        lane_hit = (ids % half_axis)[:, None] == pair_lanes[None, :]
        moves = jnp.sum(jnp.where(lane_hit, moving_pairs[None, :], 0), axis=1)
        return jnp.where(moves == 1, (ids + half_axis) % axis_width, ids)

    two_stage = half_axis <= 8
    if two_stage:
        packed = jnp.concatenate([tokens, out_grad], axis=1)
        p_packed, p_ids, p_gate, their_weights = from_partner(
            (packed, expert_ids, gate_probs, weights), "expert", swap_bit
        )
        both = jnp.concatenate([packed, p_packed], axis=0)
        ids2 = jnp.concatenate([flat_ids, p_ids.reshape(-1)])
        gate2 = jnp.concatenate([flat_gate, p_gate.reshape(-1)])
        holder2 = holder_of(ids2)
        rank2 = jnp.concatenate(
            [entry_ranks(flat_ids, axis_width), entry_ranks(p_ids.reshape(-1), axis_width)]
        )
        src2 = jnp.arange(2 * entry_count, dtype=jnp.int32) // entry_count
        in_half = holder2 // half_axis == my_index // half_axis
        lane2 = (holder2 ^ my_index) % half_axis
        chunk = 2 * slot_cap
        slot2 = lane2 * chunk + src2 * slot_cap + rank2
        slot_hit = (
            jnp.arange(half_axis * chunk, dtype=jnp.int32)[:, None] == slot2[None, :]
        ) & in_half[None, :]
        tok_hit = jnp.any(slot_hit.reshape(half_axis * chunk, 2 * tok_rows, route_count), axis=2)
        tok_pick = tok_hit.astype(jnp.bfloat16)
        send_both = jnp.dot(tok_pick, both, preferred_element_type=jnp.float32).astype(
            jnp.bfloat16
        )
        wire2 = gate2.astype(jnp.bfloat16).astype(jnp.float32)
        send_gate = jnp.sum(jnp.where(slot_hit, wire2[None, :], 0.0), axis=1)
        send_all = jnp.concatenate([send_both, with_tile(send_gate)], axis=1)

        def spread(value):
            parts = value.reshape((half_axis, chunk) + value.shape[1:])
            moved = [parts[0]] + [xor_permute(parts[m], m) for m in range(1, half_axis)]
            return jnp.stack(moved).reshape(value.shape)

        recv_all = spread(send_all)
        rows = recv_all[:, :model_width]
        grads_in = recv_all[:, model_width : 2 * model_width]
        gates = recv_all[:, 2 * model_width].astype(jnp.float32)
    else:
        slot_of = holder_of(flat_ids) * slot_cap + entry_ranks(flat_ids, axis_width)
        rows, grads_in, gates = send_slots(tokens, out_grad, flat_gate, slot_of, slot_cap)
    if not two_stage:
        their_weights = from_partner(weights, "expert", swap_bit)
    first_moment, second_moment, _ = lax.optimization_barrier(
        (first_moment, second_moment, their_weights)
    )
    their_moments = from_partner((first_moment, second_moment), "expert", swap_bit)
    weights = jnp.where(swapped, their_weights, weights)
    if groups == 2:
        other = lax.ppermute(weights, "dp", [(0, 1), (1, 0)])
        first_half = lax.axis_index("dp") == 0
        whole = jnp.concatenate(
            [jnp.where(first_half, weights, other), jnp.where(first_half, other, weights)],
            axis=1,
        )[0]
    else:
        whole = lax.all_gather(weights, "dp", axis=1, tiled=True)[0]
    w_gate = whole[:, 0, :]
    w_up = whole[:, 1, :]
    w_down = whole[:, 2, :]
    w_both = jnp.concatenate([w_gate, w_up], axis=1)
    pre_gate = jnp.dot(rows, w_gate, preferred_element_type=jnp.float32)
    pre_up = jnp.dot(rows, w_up, preferred_element_type=jnp.float32)
    activated, act_slope = silu_parts(pre_gate)
    hidden = (activated * pre_up).astype(jnp.bfloat16)
    contract_hidden = (((1,), (1,)), ((), ()))
    projected = jnp.dot(grads_in, w_down, preferred_element_type=jnp.float32)
    gate_rows = jnp.sum(hidden.astype(jnp.float32) * projected, axis=1).astype(jnp.bfloat16)
    scaled_grad = (gates[:, None] * grads_in.astype(jnp.float32)).astype(jnp.bfloat16)
    hidden_grad = jnp.dot(scaled_grad, w_down, preferred_element_type=jnp.float32)
    gate_delta = (hidden_grad * pre_up * act_slope).astype(jnp.bfloat16)
    up_delta = (hidden_grad * activated).astype(jnp.bfloat16)
    both_delta = jnp.concatenate([gate_delta, up_delta], axis=1)
    row_grad = lax.dot_general(
        both_delta, w_both, contract_hidden, preferred_element_type=jnp.float32
    )
    row_grad = row_grad.astype(jnp.bfloat16)
    contract_rows = (((0,), (0,)), ((), ()))
    grad_gate = lax.dot_general(rows, gate_delta, contract_rows, preferred_element_type=jnp.float32)
    grad_up = lax.dot_general(rows, up_delta, contract_rows, preferred_element_type=jnp.float32)
    grad_down = lax.dot_general(
        scaled_grad, hidden, contract_rows, preferred_element_type=jnp.float32
    )
    part = jnp.stack([grad_gate, grad_up, grad_down], axis=1).astype(jnp.bfloat16)
    if groups == 2:
        row_half = part.shape[0] // 2
        first_half = lax.axis_index("dp") == 0
        keep = jnp.where(first_half, part[:row_half], part[row_half:])
        give = jnp.where(first_half, part[row_half:], part[:row_half])
        got = lax.ppermute(give, "dp", [(0, 1), (1, 0)])
        grad = (keep.astype(jnp.float32) + got.astype(jnp.float32)) * (1.0 / groups)
    else:
        grad = lax.psum_scatter(
            part, "dp", scatter_dimension=0, tiled=True
        ).astype(jnp.float32) * (1.0 / groups)
    grad = grad[None]
    first_moment = jnp.where(swapped, their_moments[0], first_moment)
    second_moment = jnp.where(swapped, their_moments[1], second_moment)
    new_first = (0.9 * first_moment.astype(jnp.float32) + 0.1 * grad).astype(jnp.bfloat16)
    new_second = (0.95 * second_moment.astype(jnp.float32) + 0.05 * grad * grad).astype(
        jnp.bfloat16
    )

    if two_stage:
        back_all = spread(jnp.concatenate([row_grad, with_tile(gate_rows)], axis=1))
        back_rows = back_all[:, :model_width]
        back_gate = back_all[:, model_width].astype(jnp.float32)
        weight_of = jnp.where(slot_hit, gate2[None, :], 0.0)
        weight_of = jnp.sum(weight_of.reshape(half_axis * chunk, 2 * tok_rows, route_count), axis=2)
        partial = lax.dot_general(
            weight_of,
            back_rows.astype(jnp.float32),
            (((0,), (0,)), ((), ())),
            precision=lax.Precision.HIGHEST,
            preferred_element_type=jnp.float32,
        )
        prob2 = jnp.sum(jnp.where(slot_hit, back_gate[:, None], 0.0), axis=0)
        send_partial, send_prob, _ = lax.optimization_barrier(
            (partial[tok_rows:], prob2[entry_count:].astype(jnp.bfloat16), their_moments)
        )
        p_partial, p_prob = from_partner((send_partial, send_prob), "expert", swap_bit)
        token_grad = (partial[:tok_rows] + p_partial).astype(jnp.bfloat16)
        prob_grad = jnp.where(
            in_half[:entry_count], prob2[:entry_count], p_prob.astype(jnp.float32)
        )
        prob_grad = prob_grad.astype(jnp.bfloat16).reshape(tok_rows, route_count)
    else:
        back_rows, back_gate = [
            lax.all_to_all(
                part.reshape((axis_width, slot_cap) + part.shape[1:]),
                "expert",
                split_axis=0,
                concat_axis=0,
                tiled=True,
            )
            for part in (row_grad, gate_rows)
        ]
        gathered = back_rows.reshape(slot_count, model_width)[slot_of].astype(jnp.float32)
        token_grad = (
            (gathered * flat_gate[:, None])
            .reshape(tok_rows, route_count, model_width)
            .sum(axis=1)
            .astype(jnp.bfloat16)
        )
        prob_grad = back_gate.reshape(slot_count)[slot_of].reshape(tok_rows, route_count)
    return (token_grad, prob_grad, weights, grad, new_first, new_second)


def solution(mesh):
    in_specs = (
        P(("dp", "expert"), None),
        P(("dp", "expert"), None),
        P(("dp", "expert"), None),
        P(("dp", "expert"), None),
        P("expert", "dp", None, None),
        P("expert", "dp", None, None),
        P("expert", "dp", None, None),
        P(),
    )
    out_specs = (
        P(("dp", "expert"), None),
        P(("dp", "expert"), None),
        P("expert", "dp", None, None),
        P("expert", "dp", None, None),
        P("expert", "dp", None, None),
        P("expert", "dp", None, None),
    )
    return jax.shard_map(
        on_device, mesh=mesh, in_specs=in_specs, out_specs=out_specs, check_vma=False
    )
```

```python
import jax
import jax.numpy as jnp
from jax import lax
from jax.sharding import PartitionSpec as P


def from_partner(value, axis, bit):
    return lax.ppermute(value, axis, [(i, i ^ 1 << bit) for i in range(lax.axis_size(axis))])


def silu_parts(pre_gate):
    sig = jax.nn.sigmoid(pre_gate)
    return (pre_gate * sig, sig * (1.0 + pre_gate * (1.0 - sig)))


def send_slots(tokens, out_grad, flat_gate, slot_of, slot_cap):
    axis_width = lax.axis_size("expert")
    model_width = tokens.shape[1]
    entry_count = flat_gate.shape[0]
    route_count = entry_count // tokens.shape[0]
    slot_count = axis_width * slot_cap
    slot_hit = jnp.arange(slot_count, dtype=jnp.int32)[:, None] == slot_of[None, :]
    filled = jnp.any(slot_hit, axis=1)
    entry_lanes = jnp.arange(entry_count, dtype=jnp.int32)
    slot_entry = jnp.sum(jnp.where(slot_hit, entry_lanes[None, :], 0), axis=1)
    token_of = slot_entry // route_count
    zero_row = jnp.zeros((), jnp.bfloat16)
    send_rows = jnp.where(filled[:, None], tokens[token_of], zero_row)
    send_grads = jnp.where(filled[:, None], out_grad[token_of], zero_row)
    send_gate = jnp.where(filled, flat_gate[slot_entry], 0.0).astype(jnp.bfloat16)
    moved = [
        lax.all_to_all(
            part.reshape((axis_width, slot_cap) + part.shape[1:]),
            "expert",
            split_axis=0,
            concat_axis=0,
            tiled=True,
        )
        for part in (send_rows, send_grads, send_gate)
    ]
    rows = moved[0].reshape(slot_count, model_width)
    grads_in = moved[1].reshape(slot_count, model_width)
    gates = moved[2].reshape(slot_count).astype(jnp.float32)
    return rows, grads_in, gates


def xor_permute(value, mask):
    return lax.ppermute(value, "expert", [(i, i ^ mask) for i in range(lax.axis_size("expert"))])


def with_tile(column):
    lanes = jnp.arange(128, dtype=jnp.int32)[None, :] == 0
    return jnp.where(lanes, column.astype(jnp.bfloat16)[:, None], jnp.zeros((), jnp.bfloat16))


def entry_ranks(flat_ids, axis_width):
    id_onehot = (flat_ids[:, None] == jnp.arange(axis_width, dtype=jnp.int32)[None, :]).astype(
        jnp.int32
    )
    return jnp.sum((jnp.cumsum(id_onehot, axis=0) - id_onehot) * id_onehot, axis=1)


def on_device(
    tokens, out_grad, expert_ids, gate_probs, weights, first_moment, second_moment, moving_pairs
):
    axis_width = lax.axis_size("expert")
    half_axis = axis_width // 2
    swap_bit = half_axis.bit_length() - 1
    groups = lax.axis_size("dp")
    my_index = lax.axis_index("expert")
    tok_rows, route_count = expert_ids.shape
    model_width = tokens.shape[1]
    entry_count = tok_rows * route_count
    slot_cap = 5 * entry_count // (4 * axis_width)
    slot_count = axis_width * slot_cap
    pair_lanes = jnp.arange(half_axis, dtype=jnp.int32)
    my_move = jnp.sum(jnp.where(pair_lanes == my_index % half_axis, moving_pairs, 0))
    swapped = my_move == 1
    held = jnp.where(swapped, (my_index + half_axis) % axis_width, my_index)

    flat_gate = gate_probs.reshape(-1)
    flat_ids = expert_ids.reshape(-1)

    def holder_of(ids):
        lane_hit = (ids % half_axis)[:, None] == pair_lanes[None, :]
        moves = jnp.sum(jnp.where(lane_hit, moving_pairs[None, :], 0), axis=1)
        return jnp.where(moves == 1, (ids + half_axis) % axis_width, ids)

    two_stage = half_axis <= 8
    if two_stage:
        packed = jnp.concatenate([tokens, out_grad], axis=1)
        p_packed, p_ids, p_gate, their_weights = from_partner(
            (packed, expert_ids, gate_probs, weights), "expert", swap_bit
        )
        both = jnp.concatenate([packed, p_packed], axis=0)
        ids2 = jnp.concatenate([flat_ids, p_ids.reshape(-1)])
        gate2 = jnp.concatenate([flat_gate, p_gate.reshape(-1)])
        holder2 = holder_of(ids2)
        rank2 = jnp.concatenate(
            [entry_ranks(flat_ids, axis_width), entry_ranks(p_ids.reshape(-1), axis_width)]
        )
        src2 = jnp.arange(2 * entry_count, dtype=jnp.int32) // entry_count
        in_half = holder2 // half_axis == my_index // half_axis
        lane2 = (holder2 ^ my_index) % half_axis
        chunk = 2 * slot_cap
        slot2 = lane2 * chunk + src2 * slot_cap + rank2
        slot_hit = (
            jnp.arange(half_axis * chunk, dtype=jnp.int32)[:, None] == slot2[None, :]
        ) & in_half[None, :]
        tok_hit = jnp.any(slot_hit.reshape(half_axis * chunk, 2 * tok_rows, route_count), axis=2)
        tok_pick = tok_hit.astype(jnp.bfloat16)
        send_both = jnp.dot(tok_pick, both, preferred_element_type=jnp.float32).astype(
            jnp.bfloat16
        )
        wire2 = gate2.astype(jnp.bfloat16).astype(jnp.float32)
        send_gate = jnp.sum(jnp.where(slot_hit, wire2[None, :], 0.0), axis=1)
        send_all = jnp.concatenate([send_both, with_tile(send_gate)], axis=1)

        def spread(value):
            parts = value.reshape((half_axis, chunk) + value.shape[1:])
            moved = [parts[0]] + [xor_permute(parts[m], m) for m in range(1, half_axis)]
            return jnp.stack(moved).reshape(value.shape)

        recv_all = spread(send_all)
        rows = recv_all[:, :model_width]
        grads_in = recv_all[:, model_width : 2 * model_width]
        gates = recv_all[:, 2 * model_width].astype(jnp.float32)
    else:
        slot_of = holder_of(flat_ids) * slot_cap + entry_ranks(flat_ids, axis_width)
        rows, grads_in, gates = send_slots(tokens, out_grad, flat_gate, slot_of, slot_cap)
    if not two_stage:
        their_weights = from_partner(weights, "expert", swap_bit)
    first_moment, second_moment, _ = lax.optimization_barrier(
        (first_moment, second_moment, their_weights)
    )
    their_moments = from_partner((first_moment, second_moment), "expert", swap_bit)
    weights = jnp.where(swapped, their_weights, weights)
    if groups == 2:
        other = lax.ppermute(weights, "dp", [(0, 1), (1, 0)])
        first_half = lax.axis_index("dp") == 0
        whole = jnp.concatenate(
            [jnp.where(first_half, weights, other), jnp.where(first_half, other, weights)],
            axis=1,
        )[0]
    else:
        whole = lax.all_gather(weights, "dp", axis=1, tiled=True)[0]
    w_gate = whole[:, 0, :]
    w_up = whole[:, 1, :]
    w_down = whole[:, 2, :]
    w_both = jnp.concatenate([w_gate, w_up], axis=1)
    pre_gate = jnp.dot(rows, w_gate, preferred_element_type=jnp.float32)
    pre_up = jnp.dot(rows, w_up, preferred_element_type=jnp.float32)
    activated, act_slope = silu_parts(pre_gate)
    hidden = (activated * pre_up).astype(jnp.bfloat16)
    contract_hidden = (((1,), (1,)), ((), ()))
    projected = jnp.dot(grads_in, w_down, preferred_element_type=jnp.float32)
    gate_rows = jnp.sum(hidden.astype(jnp.float32) * projected, axis=1).astype(jnp.bfloat16)
    scaled_grad = (gates[:, None] * grads_in.astype(jnp.float32)).astype(jnp.bfloat16)
    hidden_grad = jnp.dot(scaled_grad, w_down, preferred_element_type=jnp.float32)
    gate_delta = (hidden_grad * pre_up * act_slope).astype(jnp.bfloat16)
    up_delta = (hidden_grad * activated).astype(jnp.bfloat16)
    both_delta = jnp.concatenate([gate_delta, up_delta], axis=1)
    row_grad = lax.dot_general(
        both_delta, w_both, contract_hidden, preferred_element_type=jnp.float32
    )
    row_grad = row_grad.astype(jnp.bfloat16)
    contract_rows = (((0,), (0,)), ((), ()))
    grad_gate = lax.dot_general(rows, gate_delta, contract_rows, preferred_element_type=jnp.float32)
    grad_up = lax.dot_general(rows, up_delta, contract_rows, preferred_element_type=jnp.float32)
    grad_down = lax.dot_general(
        scaled_grad, hidden, contract_rows, preferred_element_type=jnp.float32
    )
    part = jnp.stack([grad_gate, grad_up, grad_down], axis=1).astype(jnp.bfloat16)
    if groups == 2:
        row_half = part.shape[0] // 2
        first_half = lax.axis_index("dp") == 0
        keep = jnp.where(first_half, part[:row_half], part[row_half:])
        give = jnp.where(first_half, part[row_half:], part[:row_half])
        got = lax.ppermute(give, "dp", [(0, 1), (1, 0)])
        grad = (keep.astype(jnp.float32) + got.astype(jnp.float32)) * (1.0 / groups)
    else:
        grad = lax.psum_scatter(
            part, "dp", scatter_dimension=0, tiled=True
        ).astype(jnp.float32) * (1.0 / groups)
    grad = grad[None]
    first_moment = jnp.where(swapped, their_moments[0], first_moment)
    second_moment = jnp.where(swapped, their_moments[1], second_moment)
    new_first = (0.9 * first_moment.astype(jnp.float32) + 0.1 * grad).astype(jnp.bfloat16)
    new_second = (0.95 * second_moment.astype(jnp.float32) + 0.05 * grad * grad).astype(
        jnp.bfloat16
    )

    if two_stage:
        back_all = spread(jnp.concatenate([row_grad, with_tile(gate_rows)], axis=1))
        back_rows = back_all[:, :model_width]
        back_gate = back_all[:, model_width].astype(jnp.float32)
        weight_of = jnp.where(slot_hit, gate2[None, :], 0.0)
        weight_of = jnp.sum(weight_of.reshape(half_axis * chunk, 2 * tok_rows, route_count), axis=2)
        partial = lax.dot_general(
            weight_of,
            back_rows.astype(jnp.float32),
            (((0,), (0,)), ((), ())),
            precision=lax.Precision.HIGHEST,
            preferred_element_type=jnp.float32,
        )
        prob2 = jnp.sum(jnp.where(slot_hit, back_gate[:, None], 0.0), axis=0)
        p_partial, p_prob = from_partner(
            (partial[tok_rows:], prob2[entry_count:].astype(jnp.bfloat16)), "expert", swap_bit
        )
        token_grad = (partial[:tok_rows] + p_partial).astype(jnp.bfloat16)
        prob_grad = jnp.where(
            in_half[:entry_count], prob2[:entry_count], p_prob.astype(jnp.float32)
        )
        prob_grad = prob_grad.astype(jnp.bfloat16).reshape(tok_rows, route_count)
    else:
        back_rows, back_gate = [
            lax.all_to_all(
                part.reshape((axis_width, slot_cap) + part.shape[1:]),
                "expert",
                split_axis=0,
                concat_axis=0,
                tiled=True,
            )
            for part in (row_grad, gate_rows)
        ]
        gathered = back_rows.reshape(slot_count, model_width)[slot_of].astype(jnp.float32)
        token_grad = (
            (gathered * flat_gate[:, None])
            .reshape(tok_rows, route_count, model_width)
            .sum(axis=1)
            .astype(jnp.bfloat16)
        )
        prob_grad = back_gate.reshape(slot_count)[slot_of].reshape(tok_rows, route_count)
    return (token_grad, prob_grad, weights, grad, new_first, new_second)


def solution(mesh):
    in_specs = (
        P(("dp", "expert"), None),
        P(("dp", "expert"), None),
        P(("dp", "expert"), None),
        P(("dp", "expert"), None),
        P("expert", "dp", None, None),
        P("expert", "dp", None, None),
        P("expert", "dp", None, None),
        P(),
    )
    out_specs = (
        P(("dp", "expert"), None),
        P(("dp", "expert"), None),
        P("expert", "dp", None, None),
        P("expert", "dp", None, None),
        P("expert", "dp", None, None),
        P("expert", "dp", None, None),
    )
    return jax.shard_map(
        on_device, mesh=mesh, in_specs=in_specs, out_specs=out_specs, check_vma=False
    )
```

```python
import jax
import jax.numpy as jnp
from jax import lax
from jax.sharding import PartitionSpec as P


def from_partner(value, axis, bit):
    return lax.ppermute(value, axis, [(i, i ^ 1 << bit) for i in range(lax.axis_size(axis))])


def silu_parts(pre_gate):
    sig = jax.nn.sigmoid(pre_gate)
    return (pre_gate * sig, sig * (1.0 + pre_gate * (1.0 - sig)))


def send_slots(tokens, out_grad, flat_gate, slot_of, slot_cap):
    axis_width = lax.axis_size("expert")
    model_width = tokens.shape[1]
    entry_count = flat_gate.shape[0]
    route_count = entry_count // tokens.shape[0]
    slot_count = axis_width * slot_cap
    slot_hit = jnp.arange(slot_count, dtype=jnp.int32)[:, None] == slot_of[None, :]
    filled = jnp.any(slot_hit, axis=1)
    entry_lanes = jnp.arange(entry_count, dtype=jnp.int32)
    slot_entry = jnp.sum(jnp.where(slot_hit, entry_lanes[None, :], 0), axis=1)
    token_of = slot_entry // route_count
    zero_row = jnp.zeros((), jnp.bfloat16)
    send_rows = jnp.where(filled[:, None], tokens[token_of], zero_row)
    send_grads = jnp.where(filled[:, None], out_grad[token_of], zero_row)
    send_gate = jnp.where(filled, flat_gate[slot_entry], 0.0).astype(jnp.bfloat16)
    moved = [
        lax.all_to_all(
            part.reshape((axis_width, slot_cap) + part.shape[1:]),
            "expert",
            split_axis=0,
            concat_axis=0,
            tiled=True,
        )
        for part in (send_rows, send_grads, send_gate)
    ]
    rows = moved[0].reshape(slot_count, model_width)
    grads_in = moved[1].reshape(slot_count, model_width)
    gates = moved[2].reshape(slot_count).astype(jnp.float32)
    return rows, grads_in, gates


def xor_permute(value, mask):
    return lax.ppermute(value, "expert", [(i, i ^ mask) for i in range(lax.axis_size("expert"))])


def with_tile(column):
    lanes = jnp.arange(128, dtype=jnp.int32)[None, :] == 0
    return jnp.where(lanes, column.astype(jnp.bfloat16)[:, None], jnp.zeros((), jnp.bfloat16))


def entry_ranks(flat_ids, axis_width):
    id_onehot = (flat_ids[:, None] == jnp.arange(axis_width, dtype=jnp.int32)[None, :]).astype(
        jnp.int32
    )
    return jnp.sum((jnp.cumsum(id_onehot, axis=0) - id_onehot) * id_onehot, axis=1)


def on_device(
    tokens, out_grad, expert_ids, gate_probs, weights, first_moment, second_moment, moving_pairs
):
    axis_width = lax.axis_size("expert")
    half_axis = axis_width // 2
    swap_bit = half_axis.bit_length() - 1
    groups = lax.axis_size("dp")
    my_index = lax.axis_index("expert")
    tok_rows, route_count = expert_ids.shape
    model_width = tokens.shape[1]
    entry_count = tok_rows * route_count
    slot_cap = 5 * entry_count // (4 * axis_width)
    slot_count = axis_width * slot_cap
    pair_lanes = jnp.arange(half_axis, dtype=jnp.int32)
    my_move = jnp.sum(jnp.where(pair_lanes == my_index % half_axis, moving_pairs, 0))
    swapped = my_move == 1
    held = jnp.where(swapped, (my_index + half_axis) % axis_width, my_index)

    flat_gate = gate_probs.reshape(-1)
    flat_ids = expert_ids.reshape(-1)

    def holder_of(ids):
        lane_hit = (ids % half_axis)[:, None] == pair_lanes[None, :]
        moves = jnp.sum(jnp.where(lane_hit, moving_pairs[None, :], 0), axis=1)
        return jnp.where(moves == 1, (ids + half_axis) % axis_width, ids)

    two_stage = half_axis <= 8
    if two_stage:
        packed = jnp.concatenate([tokens, out_grad], axis=1)
        p_packed, p_ids, p_gate, their_weights = from_partner(
            (packed, expert_ids, gate_probs, weights), "expert", swap_bit
        )
        both = jnp.concatenate([packed, p_packed], axis=0)
        ids2 = jnp.concatenate([flat_ids, p_ids.reshape(-1)])
        gate2 = jnp.concatenate([flat_gate, p_gate.reshape(-1)])
        holder2 = holder_of(ids2)
        rank2 = jnp.concatenate(
            [entry_ranks(flat_ids, axis_width), entry_ranks(p_ids.reshape(-1), axis_width)]
        )
        src2 = jnp.arange(2 * entry_count, dtype=jnp.int32) // entry_count
        in_half = holder2 // half_axis == my_index // half_axis
        lane2 = holder2 % half_axis
        chunk = 2 * slot_cap
        slot2 = lane2 * chunk + src2 * slot_cap + rank2
        slot_hit = (
            jnp.arange(half_axis * chunk, dtype=jnp.int32)[:, None] == slot2[None, :]
        ) & in_half[None, :]
        tok_hit = jnp.any(slot_hit.reshape(half_axis * chunk, 2 * tok_rows, route_count), axis=2)
        tok_pick = tok_hit.astype(jnp.bfloat16)
        send_both = jnp.dot(tok_pick, both, preferred_element_type=jnp.float32).astype(
            jnp.bfloat16
        )
        wire2 = gate2.astype(jnp.bfloat16).astype(jnp.float32)
        send_gate = jnp.sum(jnp.where(slot_hit, wire2[None, :], 0.0), axis=1)
        send_all = jnp.concatenate([send_both, with_tile(send_gate)], axis=1)

        halves = [list(range(h * half_axis, (h + 1) * half_axis)) for h in range(2)]

        def spread(value):
            parts = value.reshape((half_axis, chunk) + value.shape[1:])
            moved = lax.all_to_all(
                parts, "expert", 0, 0, tiled=True, axis_index_groups=halves
            )
            return moved.reshape(value.shape)

        recv_all = spread(send_all)
        rows = recv_all[:, :model_width]
        grads_in = recv_all[:, model_width : 2 * model_width]
        gates = recv_all[:, 2 * model_width].astype(jnp.float32)
    else:
        slot_of = holder_of(flat_ids) * slot_cap + entry_ranks(flat_ids, axis_width)
        rows, grads_in, gates = send_slots(tokens, out_grad, flat_gate, slot_of, slot_cap)
    if not two_stage:
        their_weights = from_partner(weights, "expert", swap_bit)
    first_moment, second_moment, _ = lax.optimization_barrier(
        (first_moment, second_moment, their_weights)
    )
    their_moments = from_partner((first_moment, second_moment), "expert", swap_bit)
    weights = jnp.where(swapped, their_weights, weights)
    if groups == 2:
        other = lax.ppermute(weights, "dp", [(0, 1), (1, 0)])
        first_half = lax.axis_index("dp") == 0
        whole = jnp.concatenate(
            [jnp.where(first_half, weights, other), jnp.where(first_half, other, weights)],
            axis=1,
        )[0]
    else:
        whole = lax.all_gather(weights, "dp", axis=1, tiled=True)[0]
    w_gate = whole[:, 0, :]
    w_up = whole[:, 1, :]
    w_down = whole[:, 2, :]
    w_both = jnp.concatenate([w_gate, w_up], axis=1)
    pre_gate = jnp.dot(rows, w_gate, preferred_element_type=jnp.float32)
    pre_up = jnp.dot(rows, w_up, preferred_element_type=jnp.float32)
    activated, act_slope = silu_parts(pre_gate)
    hidden = (activated * pre_up).astype(jnp.bfloat16)
    contract_hidden = (((1,), (1,)), ((), ()))
    projected = jnp.dot(grads_in, w_down, preferred_element_type=jnp.float32)
    gate_rows = jnp.sum(hidden.astype(jnp.float32) * projected, axis=1).astype(jnp.bfloat16)
    scaled_grad = (gates[:, None] * grads_in.astype(jnp.float32)).astype(jnp.bfloat16)
    hidden_grad = jnp.dot(scaled_grad, w_down, preferred_element_type=jnp.float32)
    gate_delta = (hidden_grad * pre_up * act_slope).astype(jnp.bfloat16)
    up_delta = (hidden_grad * activated).astype(jnp.bfloat16)
    both_delta = jnp.concatenate([gate_delta, up_delta], axis=1)
    row_grad = lax.dot_general(
        both_delta, w_both, contract_hidden, preferred_element_type=jnp.float32
    )
    row_grad = row_grad.astype(jnp.bfloat16)
    contract_rows = (((0,), (0,)), ((), ()))
    grad_gate = lax.dot_general(rows, gate_delta, contract_rows, preferred_element_type=jnp.float32)
    grad_up = lax.dot_general(rows, up_delta, contract_rows, preferred_element_type=jnp.float32)
    grad_down = lax.dot_general(
        scaled_grad, hidden, contract_rows, preferred_element_type=jnp.float32
    )
    part = jnp.stack([grad_gate, grad_up, grad_down], axis=1).astype(jnp.bfloat16)
    if groups == 2:
        row_half = part.shape[0] // 2
        first_half = lax.axis_index("dp") == 0
        keep = jnp.where(first_half, part[:row_half], part[row_half:])
        give = jnp.where(first_half, part[row_half:], part[:row_half])
        got = lax.ppermute(give, "dp", [(0, 1), (1, 0)])
        grad = (keep.astype(jnp.float32) + got.astype(jnp.float32)) * (1.0 / groups)
    else:
        grad = lax.psum_scatter(
            part, "dp", scatter_dimension=0, tiled=True
        ).astype(jnp.float32) * (1.0 / groups)
    grad = grad[None]
    first_moment = jnp.where(swapped, their_moments[0], first_moment)
    second_moment = jnp.where(swapped, their_moments[1], second_moment)
    new_first = (0.9 * first_moment.astype(jnp.float32) + 0.1 * grad).astype(jnp.bfloat16)
    new_second = (0.95 * second_moment.astype(jnp.float32) + 0.05 * grad * grad).astype(
        jnp.bfloat16
    )

    if two_stage:
        back_all = spread(jnp.concatenate([row_grad, with_tile(gate_rows)], axis=1))
        back_rows = back_all[:, :model_width]
        back_gate = back_all[:, model_width].astype(jnp.float32)
        weight_of = jnp.where(slot_hit, gate2[None, :], 0.0)
        weight_of = jnp.sum(weight_of.reshape(half_axis * chunk, 2 * tok_rows, route_count), axis=2)
        partial = lax.dot_general(
            weight_of,
            back_rows.astype(jnp.float32),
            (((0,), (0,)), ((), ())),
            precision=lax.Precision.HIGHEST,
            preferred_element_type=jnp.float32,
        )
        prob2 = jnp.sum(jnp.where(slot_hit, back_gate[:, None], 0.0), axis=0)
        p_partial, p_prob = from_partner(
            (partial[tok_rows:], prob2[entry_count:].astype(jnp.bfloat16)), "expert", swap_bit
        )
        token_grad = (partial[:tok_rows] + p_partial).astype(jnp.bfloat16)
        prob_grad = jnp.where(
            in_half[:entry_count], prob2[:entry_count], p_prob.astype(jnp.float32)
        )
        prob_grad = prob_grad.astype(jnp.bfloat16).reshape(tok_rows, route_count)
    else:
        back_rows, back_gate = [
            lax.all_to_all(
                part.reshape((axis_width, slot_cap) + part.shape[1:]),
                "expert",
                split_axis=0,
                concat_axis=0,
                tiled=True,
            )
            for part in (row_grad, gate_rows)
        ]
        gathered = back_rows.reshape(slot_count, model_width)[slot_of].astype(jnp.float32)
        token_grad = (
            (gathered * flat_gate[:, None])
            .reshape(tok_rows, route_count, model_width)
            .sum(axis=1)
            .astype(jnp.bfloat16)
        )
        prob_grad = back_gate.reshape(slot_count)[slot_of].reshape(tok_rows, route_count)
    return (token_grad, prob_grad, weights, grad, new_first, new_second)


def solution(mesh):
    in_specs = (
        P(("dp", "expert"), None),
        P(("dp", "expert"), None),
        P(("dp", "expert"), None),
        P(("dp", "expert"), None),
        P("expert", "dp", None, None),
        P("expert", "dp", None, None),
        P("expert", "dp", None, None),
        P(),
    )
    out_specs = (
        P(("dp", "expert"), None),
        P(("dp", "expert"), None),
        P("expert", "dp", None, None),
        P("expert", "dp", None, None),
        P("expert", "dp", None, None),
        P("expert", "dp", None, None),
    )
    return jax.shard_map(
        on_device, mesh=mesh, in_specs=in_specs, out_specs=out_specs, check_vma=False
    )
```

```python
import jax
import jax.numpy as jnp
from jax import lax
from jax.sharding import PartitionSpec as P


def from_partner(value, axis, bit):
    return lax.ppermute(value, axis, [(i, i ^ 1 << bit) for i in range(lax.axis_size(axis))])


def silu_parts(pre_gate):
    sig = jax.nn.sigmoid(pre_gate)
    return (pre_gate * sig, sig * (1.0 + pre_gate * (1.0 - sig)))


def send_slots(tokens, out_grad, flat_gate, slot_of, slot_cap):
    axis_width = lax.axis_size("expert")
    model_width = tokens.shape[1]
    entry_count = flat_gate.shape[0]
    route_count = entry_count // tokens.shape[0]
    slot_count = axis_width * slot_cap
    slot_hit = jnp.arange(slot_count, dtype=jnp.int32)[:, None] == slot_of[None, :]
    filled = jnp.any(slot_hit, axis=1)
    entry_lanes = jnp.arange(entry_count, dtype=jnp.int32)
    slot_entry = jnp.sum(jnp.where(slot_hit, entry_lanes[None, :], 0), axis=1)
    token_of = slot_entry // route_count
    zero_row = jnp.zeros((), jnp.bfloat16)
    send_rows = jnp.where(filled[:, None], tokens[token_of], zero_row)
    send_grads = jnp.where(filled[:, None], out_grad[token_of], zero_row)
    send_gate = jnp.where(filled, flat_gate[slot_entry], 0.0).astype(jnp.bfloat16)
    moved = [
        lax.all_to_all(
            part.reshape((axis_width, slot_cap) + part.shape[1:]),
            "expert",
            split_axis=0,
            concat_axis=0,
            tiled=True,
        )
        for part in (send_rows, send_grads, send_gate)
    ]
    rows = moved[0].reshape(slot_count, model_width)
    grads_in = moved[1].reshape(slot_count, model_width)
    gates = moved[2].reshape(slot_count).astype(jnp.float32)
    return rows, grads_in, gates


def xor_permute(value, mask):
    return lax.ppermute(value, "expert", [(i, i ^ mask) for i in range(lax.axis_size("expert"))])


def with_tile(column):
    lanes = jnp.arange(128, dtype=jnp.int32)[None, :] == 0
    return jnp.where(lanes, column.astype(jnp.bfloat16)[:, None], jnp.zeros((), jnp.bfloat16))


def entry_ranks(flat_ids, axis_width):
    id_onehot = (flat_ids[:, None] == jnp.arange(axis_width, dtype=jnp.int32)[None, :]).astype(
        jnp.int32
    )
    return jnp.sum((jnp.cumsum(id_onehot, axis=0) - id_onehot) * id_onehot, axis=1)


def on_device(
    tokens, out_grad, expert_ids, gate_probs, weights, first_moment, second_moment, moving_pairs
):
    axis_width = lax.axis_size("expert")
    half_axis = axis_width // 2
    swap_bit = half_axis.bit_length() - 1
    groups = lax.axis_size("dp")
    my_index = lax.axis_index("expert")
    tok_rows, route_count = expert_ids.shape
    model_width = tokens.shape[1]
    entry_count = tok_rows * route_count
    slot_cap = 5 * entry_count // (4 * axis_width)
    slot_count = axis_width * slot_cap
    pair_lanes = jnp.arange(half_axis, dtype=jnp.int32)
    my_move = jnp.sum(jnp.where(pair_lanes == my_index % half_axis, moving_pairs, 0))
    swapped = my_move == 1
    held = jnp.where(swapped, (my_index + half_axis) % axis_width, my_index)

    flat_gate = gate_probs.reshape(-1)
    flat_ids = expert_ids.reshape(-1)

    def holder_of(ids):
        lane_hit = (ids % half_axis)[:, None] == pair_lanes[None, :]
        moves = jnp.sum(jnp.where(lane_hit, moving_pairs[None, :], 0), axis=1)
        return jnp.where(moves == 1, (ids + half_axis) % axis_width, ids)

    two_stage = half_axis <= 8
    if two_stage:
        packed = jnp.concatenate([tokens, out_grad], axis=1)
        p_packed, p_ids, p_gate, their_weights = from_partner(
            (packed, expert_ids, gate_probs, weights), "expert", swap_bit
        )
        both = jnp.concatenate([packed, p_packed], axis=0)
        ids2 = jnp.concatenate([flat_ids, p_ids.reshape(-1)])
        gate2 = jnp.concatenate([flat_gate, p_gate.reshape(-1)])
        holder2 = holder_of(ids2)
        rank2 = jnp.concatenate(
            [entry_ranks(flat_ids, axis_width), entry_ranks(p_ids.reshape(-1), axis_width)]
        )
        src2 = jnp.arange(2 * entry_count, dtype=jnp.int32) // entry_count
        in_half = holder2 // half_axis == my_index // half_axis
        lane2 = holder2 % half_axis
        chunk = 2 * slot_cap
        slot2 = lane2 * chunk + src2 * slot_cap + rank2
        slot_hit = (
            jnp.arange(half_axis * chunk, dtype=jnp.int32)[:, None] == slot2[None, :]
        ) & in_half[None, :]
        tok_hit = jnp.any(slot_hit.reshape(half_axis * chunk, 2 * tok_rows, route_count), axis=2)
        tok_pick = tok_hit.astype(jnp.bfloat16)
        send_both = jnp.dot(tok_pick, both, preferred_element_type=jnp.float32).astype(
            jnp.bfloat16
        )
        wire2 = gate2.astype(jnp.bfloat16).astype(jnp.float32)
        send_gate = jnp.sum(jnp.where(slot_hit, wire2[None, :], 0.0), axis=1)
        send_all = jnp.concatenate([send_both, with_tile(send_gate)], axis=1)

        halves = [list(range(h * half_axis, (h + 1) * half_axis)) for h in range(2)]

        def spread(value):
            parts = value.reshape((half_axis, chunk) + value.shape[1:])
            moved = lax.all_to_all(
                parts, "expert", 0, 0, tiled=True, axis_index_groups=halves
            )
            return moved.reshape(value.shape)

        recv_all = spread(send_all)
        rows = recv_all[:, :model_width]
        grads_in = recv_all[:, model_width : 2 * model_width]
        gates = recv_all[:, 2 * model_width].astype(jnp.float32)
    else:
        slot_of = holder_of(flat_ids) * slot_cap + entry_ranks(flat_ids, axis_width)
        rows, grads_in, gates = send_slots(tokens, out_grad, flat_gate, slot_of, slot_cap)
    if not two_stage:
        their_weights = from_partner(weights, "expert", swap_bit)
    first_moment, second_moment, _ = lax.optimization_barrier(
        (first_moment, second_moment, their_weights)
    )
    their_moments = from_partner((first_moment, second_moment), "expert", swap_bit)
    weights = jnp.where(swapped, their_weights, weights)
    if groups == 2:
        other = lax.ppermute(weights, "dp", [(0, 1), (1, 0)])
        first_half = lax.axis_index("dp") == 0
        whole = jnp.concatenate(
            [jnp.where(first_half, weights, other), jnp.where(first_half, other, weights)],
            axis=1,
        )[0]
    else:
        whole = lax.all_gather(weights, "dp", axis=1, tiled=True)[0]
    w_gate = whole[:, 0, :]
    w_up = whole[:, 1, :]
    w_down = whole[:, 2, :]
    w_both = jnp.concatenate([w_gate, w_up], axis=1)
    pre_gate = jnp.dot(rows, w_gate, preferred_element_type=jnp.float32)
    pre_up = jnp.dot(rows, w_up, preferred_element_type=jnp.float32)
    activated, act_slope = silu_parts(pre_gate)
    hidden = (activated * pre_up).astype(jnp.bfloat16)
    contract_hidden = (((1,), (1,)), ((), ()))
    projected = jnp.dot(grads_in, w_down, preferred_element_type=jnp.float32)
    gate_rows = jnp.sum(hidden.astype(jnp.float32) * projected, axis=1).astype(jnp.bfloat16)
    scaled_grad = (gates[:, None] * grads_in.astype(jnp.float32)).astype(jnp.bfloat16)
    hidden_grad = jnp.dot(scaled_grad, w_down, preferred_element_type=jnp.float32)
    gate_delta = (hidden_grad * pre_up * act_slope).astype(jnp.bfloat16)
    up_delta = (hidden_grad * activated).astype(jnp.bfloat16)
    both_delta = jnp.concatenate([gate_delta, up_delta], axis=1)
    row_grad = lax.dot_general(
        both_delta, w_both, contract_hidden, preferred_element_type=jnp.float32
    )
    row_grad = row_grad.astype(jnp.bfloat16)
    contract_rows = (((0,), (0,)), ((), ()))
    grad_gate = lax.dot_general(rows, gate_delta, contract_rows, preferred_element_type=jnp.float32)
    grad_up = lax.dot_general(rows, up_delta, contract_rows, preferred_element_type=jnp.float32)
    grad_down = lax.dot_general(
        scaled_grad, hidden, contract_rows, preferred_element_type=jnp.float32
    )
    part = jnp.stack([grad_gate, grad_up, grad_down], axis=1).astype(jnp.bfloat16)
    if groups == 2:
        row_half = part.shape[0] // 2
        first_half = lax.axis_index("dp") == 0
        keep = jnp.where(first_half, part[:row_half], part[row_half:])
        give = jnp.where(first_half, part[row_half:], part[:row_half])
        got = lax.ppermute(give, "dp", [(0, 1), (1, 0)])
        grad = (keep.astype(jnp.float32) + got.astype(jnp.float32)) * (1.0 / groups)
    else:
        grad = lax.psum_scatter(
            part, "dp", scatter_dimension=0, tiled=True
        ).astype(jnp.float32) * (1.0 / groups)
    grad = grad[None]
    first_moment = jnp.where(swapped, their_moments[0], first_moment)
    second_moment = jnp.where(swapped, their_moments[1], second_moment)
    new_first = (0.9 * first_moment.astype(jnp.float32) + 0.1 * grad).astype(jnp.bfloat16)
    new_second = (0.95 * second_moment.astype(jnp.float32) + 0.05 * grad * grad).astype(
        jnp.bfloat16
    )

    if two_stage:
        back_all = spread(jnp.concatenate([row_grad, with_tile(gate_rows)], axis=1))
        back_rows = back_all[:, :model_width]
        back_gate = back_all[:, model_width].astype(jnp.float32)
        weight_of = jnp.where(slot_hit, gate2[None, :], 0.0)
        weight_of = jnp.sum(weight_of.reshape(half_axis * chunk, 2 * tok_rows, route_count), axis=2)
        partial = lax.dot_general(
            weight_of,
            back_rows.astype(jnp.float32),
            (((0,), (0,)), ((), ())),
            precision=lax.Precision.HIGHEST,
            preferred_element_type=jnp.float32,
        )
        prob2 = jnp.sum(jnp.where(slot_hit, back_gate[:, None], 0.0), axis=0)
        p_partial, p_prob = from_partner(
            (partial[tok_rows:].astype(jnp.bfloat16), prob2[entry_count:].astype(jnp.bfloat16)),
            "expert",
            swap_bit,
        )
        token_grad = (partial[:tok_rows] + p_partial.astype(jnp.float32)).astype(jnp.bfloat16)
        prob_grad = jnp.where(
            in_half[:entry_count], prob2[:entry_count], p_prob.astype(jnp.float32)
        )
        prob_grad = prob_grad.astype(jnp.bfloat16).reshape(tok_rows, route_count)
    else:
        back_rows, back_gate = [
            lax.all_to_all(
                part.reshape((axis_width, slot_cap) + part.shape[1:]),
                "expert",
                split_axis=0,
                concat_axis=0,
                tiled=True,
            )
            for part in (row_grad, gate_rows)
        ]
        gathered = back_rows.reshape(slot_count, model_width)[slot_of].astype(jnp.float32)
        token_grad = (
            (gathered * flat_gate[:, None])
            .reshape(tok_rows, route_count, model_width)
            .sum(axis=1)
            .astype(jnp.bfloat16)
        )
        prob_grad = back_gate.reshape(slot_count)[slot_of].reshape(tok_rows, route_count)
    return (token_grad, prob_grad, weights, grad, new_first, new_second)


def solution(mesh):
    in_specs = (
        P(("dp", "expert"), None),
        P(("dp", "expert"), None),
        P(("dp", "expert"), None),
        P(("dp", "expert"), None),
        P("expert", "dp", None, None),
        P("expert", "dp", None, None),
        P("expert", "dp", None, None),
        P(),
    )
    out_specs = (
        P(("dp", "expert"), None),
        P(("dp", "expert"), None),
        P("expert", "dp", None, None),
        P("expert", "dp", None, None),
        P("expert", "dp", None, None),
        P("expert", "dp", None, None),
    )
    return jax.shard_map(
        on_device, mesh=mesh, in_specs=in_specs, out_specs=out_specs, check_vma=False
    )
```

```python
import jax
import jax.numpy as jnp
from jax import lax
from jax.sharding import PartitionSpec as P


def from_partner(value, axis, bit):
    return lax.ppermute(value, axis, [(i, i ^ 1 << bit) for i in range(lax.axis_size(axis))])


def silu_parts(pre_gate):
    sig = jax.nn.sigmoid(pre_gate)
    return (pre_gate * sig, sig * (1.0 + pre_gate * (1.0 - sig)))


def send_slots(tokens, out_grad, flat_gate, slot_of, slot_cap):
    axis_width = lax.axis_size("expert")
    model_width = tokens.shape[1]
    entry_count = flat_gate.shape[0]
    route_count = entry_count // tokens.shape[0]
    slot_count = axis_width * slot_cap
    slot_hit = jnp.arange(slot_count, dtype=jnp.int32)[:, None] == slot_of[None, :]
    filled = jnp.any(slot_hit, axis=1)
    entry_lanes = jnp.arange(entry_count, dtype=jnp.int32)
    slot_entry = jnp.sum(jnp.where(slot_hit, entry_lanes[None, :], 0), axis=1)
    token_of = slot_entry // route_count
    zero_row = jnp.zeros((), jnp.bfloat16)
    send_rows = jnp.where(filled[:, None], tokens[token_of], zero_row)
    send_grads = jnp.where(filled[:, None], out_grad[token_of], zero_row)
    send_gate = jnp.where(filled, flat_gate[slot_entry], 0.0).astype(jnp.bfloat16)
    moved = [
        lax.all_to_all(
            part.reshape((axis_width, slot_cap) + part.shape[1:]),
            "expert",
            split_axis=0,
            concat_axis=0,
            tiled=True,
        )
        for part in (send_rows, send_grads, send_gate)
    ]
    rows = moved[0].reshape(slot_count, model_width)
    grads_in = moved[1].reshape(slot_count, model_width)
    gates = moved[2].reshape(slot_count).astype(jnp.float32)
    return rows, grads_in, gates


def xor_permute(value, mask):
    return lax.ppermute(value, "expert", [(i, i ^ mask) for i in range(lax.axis_size("expert"))])


def with_tile(column):
    lanes = jnp.arange(128, dtype=jnp.int32)[None, :] == 0
    return jnp.where(lanes, column.astype(jnp.bfloat16)[:, None], jnp.zeros((), jnp.bfloat16))


def entry_ranks(flat_ids, axis_width):
    id_onehot = (flat_ids[:, None] == jnp.arange(axis_width, dtype=jnp.int32)[None, :]).astype(
        jnp.int32
    )
    return jnp.sum((jnp.cumsum(id_onehot, axis=0) - id_onehot) * id_onehot, axis=1)


def on_device(
    tokens, out_grad, expert_ids, gate_probs, weights, first_moment, second_moment, moving_pairs
):
    axis_width = lax.axis_size("expert")
    half_axis = axis_width // 2
    swap_bit = half_axis.bit_length() - 1
    groups = lax.axis_size("dp")
    my_index = lax.axis_index("expert")
    tok_rows, route_count = expert_ids.shape
    model_width = tokens.shape[1]
    entry_count = tok_rows * route_count
    slot_cap = 5 * entry_count // (4 * axis_width)
    slot_count = axis_width * slot_cap
    pair_lanes = jnp.arange(half_axis, dtype=jnp.int32)
    my_move = jnp.sum(jnp.where(pair_lanes == my_index % half_axis, moving_pairs, 0))
    swapped = my_move == 1
    held = jnp.where(swapped, (my_index + half_axis) % axis_width, my_index)

    flat_gate = gate_probs.reshape(-1)
    flat_ids = expert_ids.reshape(-1)

    def holder_of(ids):
        lane_hit = (ids % half_axis)[:, None] == pair_lanes[None, :]
        moves = jnp.sum(jnp.where(lane_hit, moving_pairs[None, :], 0), axis=1)
        return jnp.where(moves == 1, (ids + half_axis) % axis_width, ids)

    two_stage = half_axis <= 8
    if two_stage:
        packed = jnp.concatenate([tokens, out_grad], axis=1)
        p_packed, p_ids, p_gate, their_weights = from_partner(
            (packed, expert_ids, gate_probs, weights), "expert", swap_bit
        )
        both = jnp.concatenate([packed, p_packed], axis=0)
        ids2 = jnp.concatenate([flat_ids, p_ids.reshape(-1)])
        gate2 = jnp.concatenate([flat_gate, p_gate.reshape(-1)])
        holder2 = holder_of(ids2)
        rank2 = jnp.concatenate(
            [entry_ranks(flat_ids, axis_width), entry_ranks(p_ids.reshape(-1), axis_width)]
        )
        src2 = jnp.arange(2 * entry_count, dtype=jnp.int32) // entry_count
        in_half = holder2 // half_axis == my_index // half_axis
        lane2 = holder2 % half_axis
        chunk = 2 * slot_cap
        slot2 = lane2 * chunk + src2 * slot_cap + rank2
        slot_hit = (
            jnp.arange(half_axis * chunk, dtype=jnp.int32)[:, None] == slot2[None, :]
        ) & in_half[None, :]
        tok_hit = jnp.any(slot_hit.reshape(half_axis * chunk, 2 * tok_rows, route_count), axis=2)
        tok_pick = tok_hit.astype(jnp.bfloat16)
        send_both = jnp.dot(tok_pick, both, preferred_element_type=jnp.float32).astype(
            jnp.bfloat16
        )
        wire2 = gate2.astype(jnp.bfloat16).astype(jnp.float32)
        send_gate = jnp.sum(jnp.where(slot_hit, wire2[None, :], 0.0), axis=1)
        send_all = jnp.concatenate([send_both, with_tile(send_gate)], axis=1)

        halves = [list(range(h * half_axis, (h + 1) * half_axis)) for h in range(2)]

        def spread(value):
            parts = value.reshape((half_axis, chunk) + value.shape[1:])
            moved = lax.all_to_all(
                parts, "expert", 0, 0, tiled=True, axis_index_groups=halves
            )
            return moved.reshape(value.shape)

        recv_all = spread(send_all)
        rows = recv_all[:, :model_width]
        grads_in = recv_all[:, model_width : 2 * model_width]
        gates = recv_all[:, 2 * model_width].astype(jnp.float32)
    else:
        slot_of = holder_of(flat_ids) * slot_cap + entry_ranks(flat_ids, axis_width)
        rows, grads_in, gates = send_slots(tokens, out_grad, flat_gate, slot_of, slot_cap)
    if not two_stage:
        their_weights = from_partner(weights, "expert", swap_bit)
    moments, _ = lax.optimization_barrier(
        (jnp.stack([first_moment, second_moment]), their_weights)
    )
    their_moments = from_partner(moments, "expert", swap_bit)
    weights = jnp.where(swapped, their_weights, weights)
    if groups == 2:
        other = lax.ppermute(weights, "dp", [(0, 1), (1, 0)])
        first_half = lax.axis_index("dp") == 0
        whole = jnp.concatenate(
            [jnp.where(first_half, weights, other), jnp.where(first_half, other, weights)],
            axis=1,
        )[0]
    else:
        whole = lax.all_gather(weights, "dp", axis=1, tiled=True)[0]
    w_gate = whole[:, 0, :]
    w_up = whole[:, 1, :]
    w_down = whole[:, 2, :]
    w_both = jnp.concatenate([w_gate, w_up], axis=1)
    pre_gate = jnp.dot(rows, w_gate, preferred_element_type=jnp.float32)
    pre_up = jnp.dot(rows, w_up, preferred_element_type=jnp.float32)
    activated, act_slope = silu_parts(pre_gate)
    hidden = (activated * pre_up).astype(jnp.bfloat16)
    contract_hidden = (((1,), (1,)), ((), ()))
    projected = jnp.dot(grads_in, w_down, preferred_element_type=jnp.float32)
    gate_rows = jnp.sum(hidden.astype(jnp.float32) * projected, axis=1).astype(jnp.bfloat16)
    scaled_grad = (gates[:, None] * grads_in.astype(jnp.float32)).astype(jnp.bfloat16)
    hidden_grad = jnp.dot(scaled_grad, w_down, preferred_element_type=jnp.float32)
    gate_delta = (hidden_grad * pre_up * act_slope).astype(jnp.bfloat16)
    up_delta = (hidden_grad * activated).astype(jnp.bfloat16)
    both_delta = jnp.concatenate([gate_delta, up_delta], axis=1)
    row_grad = lax.dot_general(
        both_delta, w_both, contract_hidden, preferred_element_type=jnp.float32
    )
    row_grad = row_grad.astype(jnp.bfloat16)
    contract_rows = (((0,), (0,)), ((), ()))
    grad_gate = lax.dot_general(rows, gate_delta, contract_rows, preferred_element_type=jnp.float32)
    grad_up = lax.dot_general(rows, up_delta, contract_rows, preferred_element_type=jnp.float32)
    grad_down = lax.dot_general(
        scaled_grad, hidden, contract_rows, preferred_element_type=jnp.float32
    )
    part = jnp.stack([grad_gate, grad_up, grad_down], axis=1).astype(jnp.bfloat16)
    if groups == 2:
        row_half = part.shape[0] // 2
        first_half = lax.axis_index("dp") == 0
        keep = jnp.where(first_half, part[:row_half], part[row_half:])
        give = jnp.where(first_half, part[row_half:], part[:row_half])
        got = lax.ppermute(give, "dp", [(0, 1), (1, 0)])
        grad = (keep.astype(jnp.float32) + got.astype(jnp.float32)) * (1.0 / groups)
    else:
        grad = lax.psum_scatter(
            part, "dp", scatter_dimension=0, tiled=True
        ).astype(jnp.float32) * (1.0 / groups)
    grad = grad[None]
    first_moment = jnp.where(swapped, their_moments[0], first_moment)
    second_moment = jnp.where(swapped, their_moments[1], second_moment)
    new_first = (0.9 * first_moment.astype(jnp.float32) + 0.1 * grad).astype(jnp.bfloat16)
    new_second = (0.95 * second_moment.astype(jnp.float32) + 0.05 * grad * grad).astype(
        jnp.bfloat16
    )

    if two_stage:
        back_all = spread(jnp.concatenate([row_grad, with_tile(gate_rows)], axis=1))
        back_rows = back_all[:, :model_width]
        back_gate = back_all[:, model_width].astype(jnp.float32)
        weight_of = jnp.where(slot_hit, gate2[None, :], 0.0)
        weight_of = jnp.sum(weight_of.reshape(half_axis * chunk, 2 * tok_rows, route_count), axis=2)
        partial = lax.dot_general(
            weight_of,
            back_rows.astype(jnp.float32),
            (((0,), (0,)), ((), ())),
            precision=lax.Precision.HIGHEST,
            preferred_element_type=jnp.float32,
        )
        prob2 = jnp.sum(jnp.where(slot_hit, back_gate[:, None], 0.0), axis=0)
        p_partial, p_prob = from_partner(
            (partial[tok_rows:].astype(jnp.bfloat16), prob2[entry_count:].astype(jnp.bfloat16)),
            "expert",
            swap_bit,
        )
        token_grad = (partial[:tok_rows] + p_partial.astype(jnp.float32)).astype(jnp.bfloat16)
        prob_grad = jnp.where(
            in_half[:entry_count], prob2[:entry_count], p_prob.astype(jnp.float32)
        )
        prob_grad = prob_grad.astype(jnp.bfloat16).reshape(tok_rows, route_count)
    else:
        back_rows, back_gate = [
            lax.all_to_all(
                part.reshape((axis_width, slot_cap) + part.shape[1:]),
                "expert",
                split_axis=0,
                concat_axis=0,
                tiled=True,
            )
            for part in (row_grad, gate_rows)
        ]
        gathered = back_rows.reshape(slot_count, model_width)[slot_of].astype(jnp.float32)
        token_grad = (
            (gathered * flat_gate[:, None])
            .reshape(tok_rows, route_count, model_width)
            .sum(axis=1)
            .astype(jnp.bfloat16)
        )
        prob_grad = back_gate.reshape(slot_count)[slot_of].reshape(tok_rows, route_count)
    return (token_grad, prob_grad, weights, grad, new_first, new_second)


def solution(mesh):
    in_specs = (
        P(("dp", "expert"), None),
        P(("dp", "expert"), None),
        P(("dp", "expert"), None),
        P(("dp", "expert"), None),
        P("expert", "dp", None, None),
        P("expert", "dp", None, None),
        P("expert", "dp", None, None),
        P(),
    )
    out_specs = (
        P(("dp", "expert"), None),
        P(("dp", "expert"), None),
        P("expert", "dp", None, None),
        P("expert", "dp", None, None),
        P("expert", "dp", None, None),
        P("expert", "dp", None, None),
    )
    return jax.shard_map(
        on_device, mesh=mesh, in_specs=in_specs, out_specs=out_specs, check_vma=False
    )
```

```python
import jax
import jax.numpy as jnp
from jax import lax
from jax.sharding import PartitionSpec as P


def from_partner(value, axis, bit):
    return lax.ppermute(value, axis, [(i, i ^ 1 << bit) for i in range(lax.axis_size(axis))])


def silu_parts(pre_gate):
    sig = jax.nn.sigmoid(pre_gate)
    return (pre_gate * sig, sig * (1.0 + pre_gate * (1.0 - sig)))


def send_slots(tokens, out_grad, flat_gate, slot_of, slot_cap):
    axis_width = lax.axis_size("expert")
    model_width = tokens.shape[1]
    entry_count = flat_gate.shape[0]
    route_count = entry_count // tokens.shape[0]
    slot_count = axis_width * slot_cap
    slot_hit = jnp.arange(slot_count, dtype=jnp.int32)[:, None] == slot_of[None, :]
    filled = jnp.any(slot_hit, axis=1)
    entry_lanes = jnp.arange(entry_count, dtype=jnp.int32)
    slot_entry = jnp.sum(jnp.where(slot_hit, entry_lanes[None, :], 0), axis=1)
    token_of = slot_entry // route_count
    zero_row = jnp.zeros((), jnp.bfloat16)
    send_rows = jnp.where(filled[:, None], tokens[token_of], zero_row)
    send_grads = jnp.where(filled[:, None], out_grad[token_of], zero_row)
    send_gate = jnp.where(filled, flat_gate[slot_entry], 0.0).astype(jnp.bfloat16)
    moved = [
        lax.all_to_all(
            part.reshape((axis_width, slot_cap) + part.shape[1:]),
            "expert",
            split_axis=0,
            concat_axis=0,
            tiled=True,
        )
        for part in (send_rows, send_grads, send_gate)
    ]
    rows = moved[0].reshape(slot_count, model_width)
    grads_in = moved[1].reshape(slot_count, model_width)
    gates = moved[2].reshape(slot_count).astype(jnp.float32)
    return rows, grads_in, gates


def xor_permute(value, mask):
    return lax.ppermute(value, "expert", [(i, i ^ mask) for i in range(lax.axis_size("expert"))])


def with_tile(column):
    lanes = jnp.arange(128, dtype=jnp.int32)[None, :] == 0
    return jnp.where(lanes, column.astype(jnp.bfloat16)[:, None], jnp.zeros((), jnp.bfloat16))


def entry_ranks(flat_ids, axis_width):
    id_onehot = (flat_ids[:, None] == jnp.arange(axis_width, dtype=jnp.int32)[None, :]).astype(
        jnp.int32
    )
    return jnp.sum((jnp.cumsum(id_onehot, axis=0) - id_onehot) * id_onehot, axis=1)


def on_device(
    tokens, out_grad, expert_ids, gate_probs, weights, first_moment, second_moment, moving_pairs
):
    axis_width = lax.axis_size("expert")
    half_axis = axis_width // 2
    swap_bit = half_axis.bit_length() - 1
    groups = lax.axis_size("dp")
    my_index = lax.axis_index("expert")
    tok_rows, route_count = expert_ids.shape
    model_width = tokens.shape[1]
    entry_count = tok_rows * route_count
    slot_cap = 5 * entry_count // (4 * axis_width)
    slot_count = axis_width * slot_cap
    pair_lanes = jnp.arange(half_axis, dtype=jnp.int32)
    my_move = jnp.sum(jnp.where(pair_lanes == my_index % half_axis, moving_pairs, 0))
    swapped = my_move == 1
    held = jnp.where(swapped, (my_index + half_axis) % axis_width, my_index)

    flat_gate = gate_probs.reshape(-1)
    flat_ids = expert_ids.reshape(-1)

    def holder_of(ids):
        lane_hit = (ids % half_axis)[:, None] == pair_lanes[None, :]
        moves = jnp.sum(jnp.where(lane_hit, moving_pairs[None, :], 0), axis=1)
        return jnp.where(moves == 1, (ids + half_axis) % axis_width, ids)

    two_stage = half_axis <= 8
    if two_stage:
        plane = min(4, half_axis)
        column = axis_width // plane
        packed = jnp.concatenate([tokens, out_grad], axis=1)
        got = [(packed, expert_ids, gate_probs)]
        for k in range(1, column):
            if k * plane == half_axis:
                p_packed, p_ids, p_gate, their_weights = xor_permute(
                    (packed, expert_ids, gate_probs, weights), k * plane
                )
            else:
                p_packed, p_ids, p_gate = xor_permute((packed, expert_ids, gate_probs), k * plane)
            got.append((p_packed, p_ids, p_gate))
        both = jnp.concatenate([g[0] for g in got], axis=0)
        ids2 = jnp.concatenate([g[1].reshape(-1) for g in got])
        gate2 = jnp.concatenate([g[2].reshape(-1) for g in got])
        holder2 = holder_of(ids2)
        rank2 = jnp.concatenate([entry_ranks(g[1].reshape(-1), axis_width) for g in got])
        src2 = jnp.arange(column * entry_count, dtype=jnp.int32) // entry_count
        in_half = holder2 // plane == my_index // plane
        lane2 = holder2 % plane
        chunk = column * slot_cap
        slot2 = lane2 * chunk + src2 * slot_cap + rank2
        slot_hit = (
            jnp.arange(plane * chunk, dtype=jnp.int32)[:, None] == slot2[None, :]
        ) & in_half[None, :]
        tok_hit = jnp.any(
            slot_hit.reshape(plane * chunk, column * tok_rows, route_count), axis=2
        )
        tok_pick = tok_hit.astype(jnp.bfloat16)
        send_both = jnp.dot(tok_pick, both, preferred_element_type=jnp.float32).astype(
            jnp.bfloat16
        )
        wire2 = gate2.astype(jnp.bfloat16).astype(jnp.float32)
        send_gate = jnp.sum(jnp.where(slot_hit, wire2[None, :], 0.0), axis=1)
        send_all = jnp.concatenate([send_both, with_tile(send_gate)], axis=1)

        planes = [list(range(h * plane, (h + 1) * plane)) for h in range(column)]

        def spread(value):
            parts = value.reshape((plane, chunk) + value.shape[1:])
            moved = lax.all_to_all(
                parts, "expert", 0, 0, tiled=True, axis_index_groups=planes
            )
            return moved.reshape(value.shape)

        recv_all = spread(send_all)
        rows = recv_all[:, :model_width]
        grads_in = recv_all[:, model_width : 2 * model_width]
        gates = recv_all[:, 2 * model_width].astype(jnp.float32)
    else:
        slot_of = holder_of(flat_ids) * slot_cap + entry_ranks(flat_ids, axis_width)
        rows, grads_in, gates = send_slots(tokens, out_grad, flat_gate, slot_of, slot_cap)
    if not two_stage:
        their_weights = from_partner(weights, "expert", swap_bit)
    first_moment, second_moment, _ = lax.optimization_barrier(
        (first_moment, second_moment, their_weights)
    )
    their_moments = from_partner((first_moment, second_moment), "expert", swap_bit)
    weights = jnp.where(swapped, their_weights, weights)
    if groups == 2:
        other = lax.ppermute(weights, "dp", [(0, 1), (1, 0)])
        first_half = lax.axis_index("dp") == 0
        whole = jnp.concatenate(
            [jnp.where(first_half, weights, other), jnp.where(first_half, other, weights)],
            axis=1,
        )[0]
    else:
        whole = lax.all_gather(weights, "dp", axis=1, tiled=True)[0]
    w_gate = whole[:, 0, :]
    w_up = whole[:, 1, :]
    w_down = whole[:, 2, :]
    w_both = jnp.concatenate([w_gate, w_up], axis=1)
    pre_gate = jnp.dot(rows, w_gate, preferred_element_type=jnp.float32)
    pre_up = jnp.dot(rows, w_up, preferred_element_type=jnp.float32)
    activated, act_slope = silu_parts(pre_gate)
    hidden = (activated * pre_up).astype(jnp.bfloat16)
    contract_hidden = (((1,), (1,)), ((), ()))
    projected = jnp.dot(grads_in, w_down, preferred_element_type=jnp.float32)
    gate_rows = jnp.sum(hidden.astype(jnp.float32) * projected, axis=1).astype(jnp.bfloat16)
    scaled_grad = (gates[:, None] * grads_in.astype(jnp.float32)).astype(jnp.bfloat16)
    hidden_grad = jnp.dot(scaled_grad, w_down, preferred_element_type=jnp.float32)
    gate_delta = (hidden_grad * pre_up * act_slope).astype(jnp.bfloat16)
    up_delta = (hidden_grad * activated).astype(jnp.bfloat16)
    both_delta = jnp.concatenate([gate_delta, up_delta], axis=1)
    row_grad = lax.dot_general(
        both_delta, w_both, contract_hidden, preferred_element_type=jnp.float32
    )
    row_grad = row_grad.astype(jnp.bfloat16)
    contract_rows = (((0,), (0,)), ((), ()))
    grad_gate = lax.dot_general(rows, gate_delta, contract_rows, preferred_element_type=jnp.float32)
    grad_up = lax.dot_general(rows, up_delta, contract_rows, preferred_element_type=jnp.float32)
    grad_down = lax.dot_general(
        scaled_grad, hidden, contract_rows, preferred_element_type=jnp.float32
    )
    part = jnp.stack([grad_gate, grad_up, grad_down], axis=1).astype(jnp.bfloat16)
    if groups == 2:
        row_half = part.shape[0] // 2
        first_half = lax.axis_index("dp") == 0
        keep = jnp.where(first_half, part[:row_half], part[row_half:])
        give = jnp.where(first_half, part[row_half:], part[:row_half])
        got = lax.ppermute(give, "dp", [(0, 1), (1, 0)])
        grad = (keep.astype(jnp.float32) + got.astype(jnp.float32)) * (1.0 / groups)
    else:
        grad = lax.psum_scatter(
            part, "dp", scatter_dimension=0, tiled=True
        ).astype(jnp.float32) * (1.0 / groups)
    grad = grad[None]
    first_moment = jnp.where(swapped, their_moments[0], first_moment)
    second_moment = jnp.where(swapped, their_moments[1], second_moment)
    new_first = (0.9 * first_moment.astype(jnp.float32) + 0.1 * grad).astype(jnp.bfloat16)
    new_second = (0.95 * second_moment.astype(jnp.float32) + 0.05 * grad * grad).astype(
        jnp.bfloat16
    )

    if two_stage:
        back_all = spread(jnp.concatenate([row_grad, with_tile(gate_rows)], axis=1))
        back_rows = back_all[:, :model_width]
        back_gate = back_all[:, model_width].astype(jnp.float32)
        weight_of = jnp.where(slot_hit, gate2[None, :], 0.0)
        weight_of = jnp.sum(
            weight_of.reshape(plane * chunk, column * tok_rows, route_count), axis=2
        )
        partial = lax.dot_general(
            weight_of,
            back_rows.astype(jnp.float32),
            (((0,), (0,)), ((), ())),
            precision=lax.Precision.HIGHEST,
            preferred_element_type=jnp.float32,
        )
        prob2 = jnp.sum(jnp.where(slot_hit, back_gate[:, None], 0.0), axis=0)
        token_acc = partial[:tok_rows]
        prob_parts = [prob2[:entry_count]]
        for k in range(1, column):
            k_partial, k_prob = xor_permute(
                (
                    partial[k * tok_rows : (k + 1) * tok_rows].astype(jnp.bfloat16),
                    prob2[k * entry_count : (k + 1) * entry_count].astype(jnp.bfloat16),
                ),
                k * plane,
            )
            token_acc = token_acc + k_partial.astype(jnp.float32)
            prob_parts.append(k_prob.astype(jnp.float32))
        token_grad = token_acc.astype(jnp.bfloat16)
        served_by = (holder2[:entry_count] // plane) ^ (my_index // plane)
        prob_grad = jnp.zeros((entry_count,), jnp.float32)
        for k in range(column):
            prob_grad = jnp.where(served_by == k, prob_parts[k], prob_grad)
        prob_grad = prob_grad.astype(jnp.bfloat16).reshape(tok_rows, route_count)
    else:
        back_rows, back_gate = [
            lax.all_to_all(
                part.reshape((axis_width, slot_cap) + part.shape[1:]),
                "expert",
                split_axis=0,
                concat_axis=0,
                tiled=True,
            )
            for part in (row_grad, gate_rows)
        ]
        gathered = back_rows.reshape(slot_count, model_width)[slot_of].astype(jnp.float32)
        token_grad = (
            (gathered * flat_gate[:, None])
            .reshape(tok_rows, route_count, model_width)
            .sum(axis=1)
            .astype(jnp.bfloat16)
        )
        prob_grad = back_gate.reshape(slot_count)[slot_of].reshape(tok_rows, route_count)
    return (token_grad, prob_grad, weights, grad, new_first, new_second)


def solution(mesh):
    in_specs = (
        P(("dp", "expert"), None),
        P(("dp", "expert"), None),
        P(("dp", "expert"), None),
        P(("dp", "expert"), None),
        P("expert", "dp", None, None),
        P("expert", "dp", None, None),
        P("expert", "dp", None, None),
        P(),
    )
    out_specs = (
        P(("dp", "expert"), None),
        P(("dp", "expert"), None),
        P("expert", "dp", None, None),
        P("expert", "dp", None, None),
        P("expert", "dp", None, None),
        P("expert", "dp", None, None),
    )
    return jax.shard_map(
        on_device, mesh=mesh, in_specs=in_specs, out_specs=out_specs, check_vma=False
    )
```

```python
import jax
import jax.numpy as jnp
from jax import lax
from jax.sharding import PartitionSpec as P


def from_partner(value, axis, bit):
    return lax.ppermute(value, axis, [(i, i ^ 1 << bit) for i in range(lax.axis_size(axis))])


def silu_parts(pre_gate):
    sig = jax.nn.sigmoid(pre_gate)
    return (pre_gate * sig, sig * (1.0 + pre_gate * (1.0 - sig)))


def send_slots(tokens, out_grad, flat_gate, slot_of, slot_cap):
    axis_width = lax.axis_size("expert")
    model_width = tokens.shape[1]
    entry_count = flat_gate.shape[0]
    route_count = entry_count // tokens.shape[0]
    slot_count = axis_width * slot_cap
    slot_hit = jnp.arange(slot_count, dtype=jnp.int32)[:, None] == slot_of[None, :]
    filled = jnp.any(slot_hit, axis=1)
    entry_lanes = jnp.arange(entry_count, dtype=jnp.int32)
    slot_entry = jnp.sum(jnp.where(slot_hit, entry_lanes[None, :], 0), axis=1)
    token_of = slot_entry // route_count
    zero_row = jnp.zeros((), jnp.bfloat16)
    send_rows = jnp.where(filled[:, None], tokens[token_of], zero_row)
    send_grads = jnp.where(filled[:, None], out_grad[token_of], zero_row)
    send_gate = jnp.where(filled, flat_gate[slot_entry], 0.0).astype(jnp.bfloat16)
    moved = [
        lax.all_to_all(
            part.reshape((axis_width, slot_cap) + part.shape[1:]),
            "expert",
            split_axis=0,
            concat_axis=0,
            tiled=True,
        )
        for part in (send_rows, send_grads, send_gate)
    ]
    rows = moved[0].reshape(slot_count, model_width)
    grads_in = moved[1].reshape(slot_count, model_width)
    gates = moved[2].reshape(slot_count).astype(jnp.float32)
    return rows, grads_in, gates


def xor_permute(value, mask):
    return lax.ppermute(value, "expert", [(i, i ^ mask) for i in range(lax.axis_size("expert"))])


def with_tile(column):
    lanes = jnp.arange(128, dtype=jnp.int32)[None, :] == 0
    return jnp.where(lanes, column.astype(jnp.bfloat16)[:, None], jnp.zeros((), jnp.bfloat16))


def entry_ranks(flat_ids, axis_width):
    id_onehot = (flat_ids[:, None] == jnp.arange(axis_width, dtype=jnp.int32)[None, :]).astype(
        jnp.int32
    )
    return jnp.sum((jnp.cumsum(id_onehot, axis=0) - id_onehot) * id_onehot, axis=1)


def on_device(
    tokens, out_grad, expert_ids, gate_probs, weights, first_moment, second_moment, moving_pairs
):
    axis_width = lax.axis_size("expert")
    half_axis = axis_width // 2
    swap_bit = half_axis.bit_length() - 1
    groups = lax.axis_size("dp")
    my_index = lax.axis_index("expert")
    tok_rows, route_count = expert_ids.shape
    model_width = tokens.shape[1]
    entry_count = tok_rows * route_count
    slot_cap = 5 * entry_count // (4 * axis_width)
    slot_count = axis_width * slot_cap
    pair_lanes = jnp.arange(half_axis, dtype=jnp.int32)
    my_move = jnp.sum(jnp.where(pair_lanes == my_index % half_axis, moving_pairs, 0))
    swapped = my_move == 1
    held = jnp.where(swapped, (my_index + half_axis) % axis_width, my_index)

    flat_gate = gate_probs.reshape(-1)
    flat_ids = expert_ids.reshape(-1)

    def holder_of(ids):
        lane_hit = (ids % half_axis)[:, None] == pair_lanes[None, :]
        moves = jnp.sum(jnp.where(lane_hit, moving_pairs[None, :], 0), axis=1)
        return jnp.where(moves == 1, (ids + half_axis) % axis_width, ids)

    two_stage = half_axis <= 8
    if two_stage:
        plane = min(4, half_axis)
        column = axis_width // plane
        packed = jnp.concatenate([tokens, out_grad], axis=1)
        got = [(packed, expert_ids, gate_probs)]
        for k in range(1, column):
            if k * plane == half_axis:
                p_packed, p_ids, p_gate, their_weights = xor_permute(
                    (packed, expert_ids, gate_probs, weights), k * plane
                )
            else:
                p_packed, p_ids, p_gate = xor_permute((packed, expert_ids, gate_probs), k * plane)
            got.append((p_packed, p_ids, p_gate))
        both = jnp.concatenate([g[0] for g in got], axis=0)
        ids2 = jnp.concatenate([g[1].reshape(-1) for g in got])
        gate2 = jnp.concatenate([g[2].reshape(-1) for g in got])
        holder2 = holder_of(ids2)
        rank2 = jnp.concatenate([entry_ranks(g[1].reshape(-1), axis_width) for g in got])
        src2 = jnp.arange(column * entry_count, dtype=jnp.int32) // entry_count
        in_half = holder2 // plane == my_index // plane
        lane2 = holder2 % plane
        chunk = column * slot_cap
        slot2 = lane2 * chunk + src2 * slot_cap + rank2
        slot_hit = (
            jnp.arange(plane * chunk, dtype=jnp.int32)[:, None] == slot2[None, :]
        ) & in_half[None, :]
        tok_hit = jnp.any(
            slot_hit.reshape(plane * chunk, column * tok_rows, route_count), axis=2
        )
        tok_pick = tok_hit.astype(jnp.bfloat16)
        send_both = jnp.dot(tok_pick, both, preferred_element_type=jnp.float32).astype(
            jnp.bfloat16
        )
        wire2 = gate2.astype(jnp.bfloat16).astype(jnp.float32)
        send_gate = jnp.sum(jnp.where(slot_hit, wire2[None, :], 0.0), axis=1)
        send_all = jnp.concatenate([send_both, with_tile(send_gate)], axis=1)

        planes = [list(range(h * plane, (h + 1) * plane)) for h in range(column)]

        def spread(value):
            parts = value.reshape((plane, chunk) + value.shape[1:])
            moved = lax.all_to_all(
                parts, "expert", 0, 0, tiled=True, axis_index_groups=planes
            )
            return moved.reshape(value.shape)

        recv_all = spread(send_all)
        rows = recv_all[:, :model_width]
        grads_in = recv_all[:, model_width : 2 * model_width]
        gates = recv_all[:, 2 * model_width].astype(jnp.float32)
    else:
        slot_of = holder_of(flat_ids) * slot_cap + entry_ranks(flat_ids, axis_width)
        rows, grads_in, gates = send_slots(tokens, out_grad, flat_gate, slot_of, slot_cap)
    if not two_stage:
        their_weights = from_partner(weights, "expert", swap_bit)
    first_moment, second_moment, _ = lax.optimization_barrier(
        (first_moment, second_moment, their_weights)
    )
    if two_stage:
        pairs = [[p, p + half_axis] for p in range(half_axis)]
        pair_both = lax.all_gather(
            jnp.stack([first_moment, second_moment]), "expert", axis_index_groups=pairs
        )
        mine_first = my_index < half_axis
        their_moments = jnp.where(mine_first, pair_both[1], pair_both[0])
    else:
        their_moments = from_partner((first_moment, second_moment), "expert", swap_bit)
    weights = jnp.where(swapped, their_weights, weights)
    if groups == 2:
        other = lax.ppermute(weights, "dp", [(0, 1), (1, 0)])
        first_half = lax.axis_index("dp") == 0
        whole = jnp.concatenate(
            [jnp.where(first_half, weights, other), jnp.where(first_half, other, weights)],
            axis=1,
        )[0]
    else:
        whole = lax.all_gather(weights, "dp", axis=1, tiled=True)[0]
    w_gate = whole[:, 0, :]
    w_up = whole[:, 1, :]
    w_down = whole[:, 2, :]
    w_both = jnp.concatenate([w_gate, w_up], axis=1)
    pre_gate = jnp.dot(rows, w_gate, preferred_element_type=jnp.float32)
    pre_up = jnp.dot(rows, w_up, preferred_element_type=jnp.float32)
    activated, act_slope = silu_parts(pre_gate)
    hidden = (activated * pre_up).astype(jnp.bfloat16)
    contract_hidden = (((1,), (1,)), ((), ()))
    projected = jnp.dot(grads_in, w_down, preferred_element_type=jnp.float32)
    gate_rows = jnp.sum(hidden.astype(jnp.float32) * projected, axis=1).astype(jnp.bfloat16)
    scaled_grad = (gates[:, None] * grads_in.astype(jnp.float32)).astype(jnp.bfloat16)
    hidden_grad = jnp.dot(scaled_grad, w_down, preferred_element_type=jnp.float32)
    gate_delta = (hidden_grad * pre_up * act_slope).astype(jnp.bfloat16)
    up_delta = (hidden_grad * activated).astype(jnp.bfloat16)
    both_delta = jnp.concatenate([gate_delta, up_delta], axis=1)
    row_grad = lax.dot_general(
        both_delta, w_both, contract_hidden, preferred_element_type=jnp.float32
    )
    row_grad = row_grad.astype(jnp.bfloat16)
    contract_rows = (((0,), (0,)), ((), ()))
    grad_gate = lax.dot_general(rows, gate_delta, contract_rows, preferred_element_type=jnp.float32)
    grad_up = lax.dot_general(rows, up_delta, contract_rows, preferred_element_type=jnp.float32)
    grad_down = lax.dot_general(
        scaled_grad, hidden, contract_rows, preferred_element_type=jnp.float32
    )
    part = jnp.stack([grad_gate, grad_up, grad_down], axis=1).astype(jnp.bfloat16)
    if groups == 2:
        row_half = part.shape[0] // 2
        first_half = lax.axis_index("dp") == 0
        keep = jnp.where(first_half, part[:row_half], part[row_half:])
        give = jnp.where(first_half, part[row_half:], part[:row_half])
        got = lax.ppermute(give, "dp", [(0, 1), (1, 0)])
        grad = (keep.astype(jnp.float32) + got.astype(jnp.float32)) * (1.0 / groups)
    else:
        grad = lax.psum_scatter(
            part, "dp", scatter_dimension=0, tiled=True
        ).astype(jnp.float32) * (1.0 / groups)
    grad = grad[None]
    first_moment = jnp.where(swapped, their_moments[0], first_moment)
    second_moment = jnp.where(swapped, their_moments[1], second_moment)
    new_first = (0.9 * first_moment.astype(jnp.float32) + 0.1 * grad).astype(jnp.bfloat16)
    new_second = (0.95 * second_moment.astype(jnp.float32) + 0.05 * grad * grad).astype(
        jnp.bfloat16
    )

    if two_stage:
        back_all = spread(jnp.concatenate([row_grad, with_tile(gate_rows)], axis=1))
        back_rows = back_all[:, :model_width]
        back_gate = back_all[:, model_width].astype(jnp.float32)
        weight_of = jnp.where(slot_hit, gate2[None, :], 0.0)
        weight_of = jnp.sum(
            weight_of.reshape(plane * chunk, column * tok_rows, route_count), axis=2
        )
        partial = lax.dot_general(
            weight_of,
            back_rows.astype(jnp.float32),
            (((0,), (0,)), ((), ())),
            precision=lax.Precision.HIGHEST,
            preferred_element_type=jnp.float32,
        )
        prob2 = jnp.sum(jnp.where(slot_hit, back_gate[:, None], 0.0), axis=0)
        token_acc = partial[:tok_rows]
        prob_parts = [prob2[:entry_count]]
        for k in range(1, column):
            k_partial, k_prob = xor_permute(
                (
                    partial[k * tok_rows : (k + 1) * tok_rows].astype(jnp.bfloat16),
                    prob2[k * entry_count : (k + 1) * entry_count].astype(jnp.bfloat16),
                ),
                k * plane,
            )
            token_acc = token_acc + k_partial.astype(jnp.float32)
            prob_parts.append(k_prob.astype(jnp.float32))
        token_grad = token_acc.astype(jnp.bfloat16)
        served_by = (holder2[:entry_count] // plane) ^ (my_index // plane)
        prob_grad = jnp.zeros((entry_count,), jnp.float32)
        for k in range(column):
            prob_grad = jnp.where(served_by == k, prob_parts[k], prob_grad)
        prob_grad = prob_grad.astype(jnp.bfloat16).reshape(tok_rows, route_count)
    else:
        back_rows, back_gate = [
            lax.all_to_all(
                part.reshape((axis_width, slot_cap) + part.shape[1:]),
                "expert",
                split_axis=0,
                concat_axis=0,
                tiled=True,
            )
            for part in (row_grad, gate_rows)
        ]
        gathered = back_rows.reshape(slot_count, model_width)[slot_of].astype(jnp.float32)
        token_grad = (
            (gathered * flat_gate[:, None])
            .reshape(tok_rows, route_count, model_width)
            .sum(axis=1)
            .astype(jnp.bfloat16)
        )
        prob_grad = back_gate.reshape(slot_count)[slot_of].reshape(tok_rows, route_count)
    return (token_grad, prob_grad, weights, grad, new_first, new_second)


def solution(mesh):
    in_specs = (
        P(("dp", "expert"), None),
        P(("dp", "expert"), None),
        P(("dp", "expert"), None),
        P(("dp", "expert"), None),
        P("expert", "dp", None, None),
        P("expert", "dp", None, None),
        P("expert", "dp", None, None),
        P(),
    )
    out_specs = (
        P(("dp", "expert"), None),
        P(("dp", "expert"), None),
        P("expert", "dp", None, None),
        P("expert", "dp", None, None),
        P("expert", "dp", None, None),
        P("expert", "dp", None, None),
    )
    return jax.shard_map(
        on_device, mesh=mesh, in_specs=in_specs, out_specs=out_specs, check_vma=False
    )
```

```python
import jax
import jax.numpy as jnp
from jax import lax
from jax.sharding import PartitionSpec as P


def from_partner(value, axis, bit):
    return lax.ppermute(value, axis, [(i, i ^ 1 << bit) for i in range(lax.axis_size(axis))])


def silu_parts(pre_gate):
    sig = jax.nn.sigmoid(pre_gate)
    return (pre_gate * sig, sig * (1.0 + pre_gate * (1.0 - sig)))


def send_slots(tokens, out_grad, flat_gate, slot_of, slot_cap):
    axis_width = lax.axis_size("expert")
    model_width = tokens.shape[1]
    entry_count = flat_gate.shape[0]
    route_count = entry_count // tokens.shape[0]
    slot_count = axis_width * slot_cap
    slot_hit = jnp.arange(slot_count, dtype=jnp.int32)[:, None] == slot_of[None, :]
    filled = jnp.any(slot_hit, axis=1)
    entry_lanes = jnp.arange(entry_count, dtype=jnp.int32)
    slot_entry = jnp.sum(jnp.where(slot_hit, entry_lanes[None, :], 0), axis=1)
    token_of = slot_entry // route_count
    zero_row = jnp.zeros((), jnp.bfloat16)
    send_rows = jnp.where(filled[:, None], tokens[token_of], zero_row)
    send_grads = jnp.where(filled[:, None], out_grad[token_of], zero_row)
    send_gate = jnp.where(filled, flat_gate[slot_entry], 0.0).astype(jnp.bfloat16)
    moved = [
        lax.all_to_all(
            part.reshape((axis_width, slot_cap) + part.shape[1:]),
            "expert",
            split_axis=0,
            concat_axis=0,
            tiled=True,
        )
        for part in (send_rows, send_grads, send_gate)
    ]
    rows = moved[0].reshape(slot_count, model_width)
    grads_in = moved[1].reshape(slot_count, model_width)
    gates = moved[2].reshape(slot_count).astype(jnp.float32)
    return rows, grads_in, gates


def xor_permute(value, mask):
    return lax.ppermute(value, "expert", [(i, i ^ mask) for i in range(lax.axis_size("expert"))])


def with_tile(column):
    lanes = jnp.arange(128, dtype=jnp.int32)[None, :] == 0
    return jnp.where(lanes, column.astype(jnp.bfloat16)[:, None], jnp.zeros((), jnp.bfloat16))


def entry_ranks(flat_ids, axis_width):
    id_onehot = (flat_ids[:, None] == jnp.arange(axis_width, dtype=jnp.int32)[None, :]).astype(
        jnp.int32
    )
    return jnp.sum((jnp.cumsum(id_onehot, axis=0) - id_onehot) * id_onehot, axis=1)


def on_device(
    tokens, out_grad, expert_ids, gate_probs, weights, first_moment, second_moment, moving_pairs
):
    axis_width = lax.axis_size("expert")
    half_axis = axis_width // 2
    swap_bit = half_axis.bit_length() - 1
    groups = lax.axis_size("dp")
    my_index = lax.axis_index("expert")
    tok_rows, route_count = expert_ids.shape
    model_width = tokens.shape[1]
    entry_count = tok_rows * route_count
    slot_cap = 5 * entry_count // (4 * axis_width)
    slot_count = axis_width * slot_cap
    pair_lanes = jnp.arange(half_axis, dtype=jnp.int32)
    my_move = jnp.sum(jnp.where(pair_lanes == my_index % half_axis, moving_pairs, 0))
    swapped = my_move == 1
    held = jnp.where(swapped, (my_index + half_axis) % axis_width, my_index)

    flat_gate = gate_probs.reshape(-1)
    flat_ids = expert_ids.reshape(-1)

    def holder_of(ids):
        lane_hit = (ids % half_axis)[:, None] == pair_lanes[None, :]
        moves = jnp.sum(jnp.where(lane_hit, moving_pairs[None, :], 0), axis=1)
        return jnp.where(moves == 1, (ids + half_axis) % axis_width, ids)

    two_stage = half_axis <= 8
    if two_stage:
        plane = min(4, half_axis)
        column = axis_width // plane
        packed = jnp.concatenate([tokens, out_grad], axis=1)
        got = [(packed, expert_ids, gate_probs)]
        for k in range(1, column):
            if k * plane == half_axis:
                p_packed, p_ids, p_gate, their_weights = xor_permute(
                    (packed, expert_ids, gate_probs, weights), k * plane
                )
            else:
                p_packed, p_ids, p_gate = xor_permute((packed, expert_ids, gate_probs), k * plane)
            got.append((p_packed, p_ids, p_gate))
        both = jnp.concatenate([g[0] for g in got], axis=0)
        ids2 = jnp.concatenate([g[1].reshape(-1) for g in got])
        gate2 = jnp.concatenate([g[2].reshape(-1) for g in got])
        holder2 = holder_of(ids2)
        rank2 = jnp.concatenate([entry_ranks(g[1].reshape(-1), axis_width) for g in got])
        src2 = jnp.arange(column * entry_count, dtype=jnp.int32) // entry_count
        in_half = holder2 // plane == my_index // plane
        lane2 = holder2 % plane
        chunk = column * slot_cap
        slot2 = lane2 * chunk + src2 * slot_cap + rank2
        slot_hit = (
            jnp.arange(plane * chunk, dtype=jnp.int32)[:, None] == slot2[None, :]
        ) & in_half[None, :]
        tok_hit = jnp.any(
            slot_hit.reshape(plane * chunk, column * tok_rows, route_count), axis=2
        )
        tok_pick = tok_hit.astype(jnp.bfloat16)
        send_both = jnp.dot(tok_pick, both, preferred_element_type=jnp.float32).astype(
            jnp.bfloat16
        )
        wire2 = gate2.astype(jnp.bfloat16).astype(jnp.float32)
        send_gate = jnp.sum(jnp.where(slot_hit, wire2[None, :], 0.0), axis=1)
        send_all = jnp.concatenate([send_both, with_tile(send_gate)], axis=1)

        planes = [list(range(h * plane, (h + 1) * plane)) for h in range(column)]

        def spread(value):
            parts = value.reshape((plane, chunk) + value.shape[1:])
            moved = lax.all_to_all(
                parts, "expert", 0, 0, tiled=True, axis_index_groups=planes
            )
            return moved.reshape(value.shape)

        recv_all = spread(send_all)
        rows = recv_all[:, :model_width]
        grads_in = recv_all[:, model_width : 2 * model_width]
        gates = recv_all[:, 2 * model_width].astype(jnp.float32)
    else:
        slot_of = holder_of(flat_ids) * slot_cap + entry_ranks(flat_ids, axis_width)
        rows, grads_in, gates = send_slots(tokens, out_grad, flat_gate, slot_of, slot_cap)
    if not two_stage:
        their_weights = from_partner(weights, "expert", swap_bit)
    if two_stage:
        pairs = [[p, p + half_axis] for p in range(half_axis)]
        pair_both = lax.all_gather(
            jnp.stack([first_moment, second_moment]), "expert", axis_index_groups=pairs
        )
        mine_first = my_index < half_axis
        their_moments = jnp.where(mine_first, pair_both[1], pair_both[0])
    else:
        first_moment, second_moment, _ = lax.optimization_barrier(
            (first_moment, second_moment, their_weights)
        )
        their_moments = from_partner((first_moment, second_moment), "expert", swap_bit)
    weights = jnp.where(swapped, their_weights, weights)
    if groups == 2:
        other = lax.ppermute(weights, "dp", [(0, 1), (1, 0)])
        first_half = lax.axis_index("dp") == 0
        whole = jnp.concatenate(
            [jnp.where(first_half, weights, other), jnp.where(first_half, other, weights)],
            axis=1,
        )[0]
    else:
        whole = lax.all_gather(weights, "dp", axis=1, tiled=True)[0]
    w_gate = whole[:, 0, :]
    w_up = whole[:, 1, :]
    w_down = whole[:, 2, :]
    w_both = jnp.concatenate([w_gate, w_up], axis=1)
    pre_gate = jnp.dot(rows, w_gate, preferred_element_type=jnp.float32)
    pre_up = jnp.dot(rows, w_up, preferred_element_type=jnp.float32)
    activated, act_slope = silu_parts(pre_gate)
    hidden = (activated * pre_up).astype(jnp.bfloat16)
    contract_hidden = (((1,), (1,)), ((), ()))
    projected = jnp.dot(grads_in, w_down, preferred_element_type=jnp.float32)
    gate_rows = jnp.sum(hidden.astype(jnp.float32) * projected, axis=1).astype(jnp.bfloat16)
    scaled_grad = (gates[:, None] * grads_in.astype(jnp.float32)).astype(jnp.bfloat16)
    hidden_grad = jnp.dot(scaled_grad, w_down, preferred_element_type=jnp.float32)
    gate_delta = (hidden_grad * pre_up * act_slope).astype(jnp.bfloat16)
    up_delta = (hidden_grad * activated).astype(jnp.bfloat16)
    both_delta = jnp.concatenate([gate_delta, up_delta], axis=1)
    row_grad = lax.dot_general(
        both_delta, w_both, contract_hidden, preferred_element_type=jnp.float32
    )
    row_grad = row_grad.astype(jnp.bfloat16)
    contract_rows = (((0,), (0,)), ((), ()))
    grad_gate = lax.dot_general(rows, gate_delta, contract_rows, preferred_element_type=jnp.float32)
    grad_up = lax.dot_general(rows, up_delta, contract_rows, preferred_element_type=jnp.float32)
    grad_down = lax.dot_general(
        scaled_grad, hidden, contract_rows, preferred_element_type=jnp.float32
    )
    part = jnp.stack([grad_gate, grad_up, grad_down], axis=1).astype(jnp.bfloat16)
    if groups == 2:
        row_half = part.shape[0] // 2
        first_half = lax.axis_index("dp") == 0
        keep = jnp.where(first_half, part[:row_half], part[row_half:])
        give = jnp.where(first_half, part[row_half:], part[:row_half])
        got = lax.ppermute(give, "dp", [(0, 1), (1, 0)])
        grad = (keep.astype(jnp.float32) + got.astype(jnp.float32)) * (1.0 / groups)
    else:
        grad = lax.psum_scatter(
            part, "dp", scatter_dimension=0, tiled=True
        ).astype(jnp.float32) * (1.0 / groups)
    grad = grad[None]
    first_moment = jnp.where(swapped, their_moments[0], first_moment)
    second_moment = jnp.where(swapped, their_moments[1], second_moment)
    new_first = (0.9 * first_moment.astype(jnp.float32) + 0.1 * grad).astype(jnp.bfloat16)
    new_second = (0.95 * second_moment.astype(jnp.float32) + 0.05 * grad * grad).astype(
        jnp.bfloat16
    )

    if two_stage:
        back_all = spread(jnp.concatenate([row_grad, with_tile(gate_rows)], axis=1))
        back_rows = back_all[:, :model_width]
        back_gate = back_all[:, model_width].astype(jnp.float32)
        weight_of = jnp.where(slot_hit, gate2[None, :], 0.0)
        weight_of = jnp.sum(
            weight_of.reshape(plane * chunk, column * tok_rows, route_count), axis=2
        )
        partial = lax.dot_general(
            weight_of,
            back_rows.astype(jnp.float32),
            (((0,), (0,)), ((), ())),
            precision=lax.Precision.HIGHEST,
            preferred_element_type=jnp.float32,
        )
        prob2 = jnp.sum(jnp.where(slot_hit, back_gate[:, None], 0.0), axis=0)
        token_acc = partial[:tok_rows]
        prob_parts = [prob2[:entry_count]]
        for k in range(1, column):
            k_partial, k_prob = xor_permute(
                (
                    partial[k * tok_rows : (k + 1) * tok_rows].astype(jnp.bfloat16),
                    prob2[k * entry_count : (k + 1) * entry_count].astype(jnp.bfloat16),
                ),
                k * plane,
            )
            token_acc = token_acc + k_partial.astype(jnp.float32)
            prob_parts.append(k_prob.astype(jnp.float32))
        token_grad = token_acc.astype(jnp.bfloat16)
        served_by = (holder2[:entry_count] // plane) ^ (my_index // plane)
        prob_grad = jnp.zeros((entry_count,), jnp.float32)
        for k in range(column):
            prob_grad = jnp.where(served_by == k, prob_parts[k], prob_grad)
        prob_grad = prob_grad.astype(jnp.bfloat16).reshape(tok_rows, route_count)
    else:
        back_rows, back_gate = [
            lax.all_to_all(
                part.reshape((axis_width, slot_cap) + part.shape[1:]),
                "expert",
                split_axis=0,
                concat_axis=0,
                tiled=True,
            )
            for part in (row_grad, gate_rows)
        ]
        gathered = back_rows.reshape(slot_count, model_width)[slot_of].astype(jnp.float32)
        token_grad = (
            (gathered * flat_gate[:, None])
            .reshape(tok_rows, route_count, model_width)
            .sum(axis=1)
            .astype(jnp.bfloat16)
        )
        prob_grad = back_gate.reshape(slot_count)[slot_of].reshape(tok_rows, route_count)
    return (token_grad, prob_grad, weights, grad, new_first, new_second)


def solution(mesh):
    in_specs = (
        P(("dp", "expert"), None),
        P(("dp", "expert"), None),
        P(("dp", "expert"), None),
        P(("dp", "expert"), None),
        P("expert", "dp", None, None),
        P("expert", "dp", None, None),
        P("expert", "dp", None, None),
        P(),
    )
    out_specs = (
        P(("dp", "expert"), None),
        P(("dp", "expert"), None),
        P("expert", "dp", None, None),
        P("expert", "dp", None, None),
        P("expert", "dp", None, None),
        P("expert", "dp", None, None),
    )
    return jax.shard_map(
        on_device, mesh=mesh, in_specs=in_specs, out_specs=out_specs, check_vma=False
    )
```

```python
import jax
import jax.numpy as jnp
from jax import lax
from jax.sharding import PartitionSpec as P


def from_partner(value, axis, bit):
    return lax.ppermute(value, axis, [(i, i ^ 1 << bit) for i in range(lax.axis_size(axis))])


def silu_parts(pre_gate):
    sig = jax.nn.sigmoid(pre_gate)
    return (pre_gate * sig, sig * (1.0 + pre_gate * (1.0 - sig)))


def send_slots(tokens, out_grad, flat_gate, slot_of, slot_cap):
    axis_width = lax.axis_size("expert")
    model_width = tokens.shape[1]
    entry_count = flat_gate.shape[0]
    route_count = entry_count // tokens.shape[0]
    slot_count = axis_width * slot_cap
    slot_hit = jnp.arange(slot_count, dtype=jnp.int32)[:, None] == slot_of[None, :]
    filled = jnp.any(slot_hit, axis=1)
    entry_lanes = jnp.arange(entry_count, dtype=jnp.int32)
    slot_entry = jnp.sum(jnp.where(slot_hit, entry_lanes[None, :], 0), axis=1)
    token_of = slot_entry // route_count
    zero_row = jnp.zeros((), jnp.bfloat16)
    send_rows = jnp.where(filled[:, None], tokens[token_of], zero_row)
    send_grads = jnp.where(filled[:, None], out_grad[token_of], zero_row)
    send_gate = jnp.where(filled, flat_gate[slot_entry], 0.0).astype(jnp.bfloat16)
    moved = [
        lax.all_to_all(
            part.reshape((axis_width, slot_cap) + part.shape[1:]),
            "expert",
            split_axis=0,
            concat_axis=0,
            tiled=True,
        )
        for part in (send_rows, send_grads, send_gate)
    ]
    rows = moved[0].reshape(slot_count, model_width)
    grads_in = moved[1].reshape(slot_count, model_width)
    gates = moved[2].reshape(slot_count).astype(jnp.float32)
    return rows, grads_in, gates


def xor_permute(value, mask):
    return lax.ppermute(value, "expert", [(i, i ^ mask) for i in range(lax.axis_size("expert"))])


def with_tile(column):
    lanes = jnp.arange(128, dtype=jnp.int32)[None, :] == 0
    return jnp.where(lanes, column.astype(jnp.bfloat16)[:, None], jnp.zeros((), jnp.bfloat16))


def entry_ranks(flat_ids, axis_width):
    id_onehot = (flat_ids[:, None] == jnp.arange(axis_width, dtype=jnp.int32)[None, :]).astype(
        jnp.int32
    )
    return jnp.sum((jnp.cumsum(id_onehot, axis=0) - id_onehot) * id_onehot, axis=1)


def on_device(
    tokens, out_grad, expert_ids, gate_probs, weights, first_moment, second_moment, moving_pairs
):
    axis_width = lax.axis_size("expert")
    half_axis = axis_width // 2
    swap_bit = half_axis.bit_length() - 1
    groups = lax.axis_size("dp")
    my_index = lax.axis_index("expert")
    tok_rows, route_count = expert_ids.shape
    model_width = tokens.shape[1]
    entry_count = tok_rows * route_count
    slot_cap = 5 * entry_count // (4 * axis_width)
    slot_count = axis_width * slot_cap
    pair_lanes = jnp.arange(half_axis, dtype=jnp.int32)
    my_move = jnp.sum(jnp.where(pair_lanes == my_index % half_axis, moving_pairs, 0))
    swapped = my_move == 1
    held = jnp.where(swapped, (my_index + half_axis) % axis_width, my_index)

    flat_gate = gate_probs.reshape(-1)
    flat_ids = expert_ids.reshape(-1)

    def holder_of(ids):
        lane_hit = (ids % half_axis)[:, None] == pair_lanes[None, :]
        moves = jnp.sum(jnp.where(lane_hit, moving_pairs[None, :], 0), axis=1)
        return jnp.where(moves == 1, (ids + half_axis) % axis_width, ids)

    two_stage = half_axis <= 8
    if two_stage:
        packed = jnp.concatenate([tokens, out_grad], axis=1)
        p_packed, p_ids, p_gate, their_weights = from_partner(
            (packed, expert_ids, gate_probs, weights), "expert", swap_bit
        )
        both = jnp.concatenate([packed, p_packed], axis=0)
        ids2 = jnp.concatenate([flat_ids, p_ids.reshape(-1)])
        gate2 = jnp.concatenate([flat_gate, p_gate.reshape(-1)])
        holder2 = holder_of(ids2)
        rank2 = jnp.concatenate(
            [entry_ranks(flat_ids, axis_width), entry_ranks(p_ids.reshape(-1), axis_width)]
        )
        src2 = jnp.arange(2 * entry_count, dtype=jnp.int32) // entry_count
        in_half = holder2 // half_axis == my_index // half_axis
        lane2 = holder2 % half_axis
        chunk = 2 * slot_cap
        slot2 = lane2 * chunk + src2 * slot_cap + rank2
        slot_hit = (
            jnp.arange(half_axis * chunk, dtype=jnp.int32)[:, None] == slot2[None, :]
        ) & in_half[None, :]
        tok_hit = jnp.any(slot_hit.reshape(half_axis * chunk, 2 * tok_rows, route_count), axis=2)
        tok_pick = tok_hit.astype(jnp.bfloat16)
        send_both = jnp.dot(tok_pick, both, preferred_element_type=jnp.float32).astype(
            jnp.bfloat16
        )
        wire2 = gate2.astype(jnp.bfloat16).astype(jnp.float32)
        send_gate = jnp.sum(jnp.where(slot_hit, wire2[None, :], 0.0), axis=1)
        send_all = jnp.concatenate([send_both, with_tile(send_gate)], axis=1)

        halves = [list(range(h * half_axis, (h + 1) * half_axis)) for h in range(2)]

        def spread(value):
            parts = value.reshape((half_axis, chunk) + value.shape[1:])
            moved = lax.all_to_all(
                parts, "expert", 0, 0, tiled=True, axis_index_groups=halves
            )
            return moved.reshape(value.shape)

        recv_all = spread(send_all)
        rows = recv_all[:, :model_width]
        grads_in = recv_all[:, model_width : 2 * model_width]
        gates = recv_all[:, 2 * model_width].astype(jnp.float32)
    else:
        slot_of = holder_of(flat_ids) * slot_cap + entry_ranks(flat_ids, axis_width)
        rows, grads_in, gates = send_slots(tokens, out_grad, flat_gate, slot_of, slot_cap)
    if not two_stage:
        their_weights = from_partner(weights, "expert", swap_bit)
    moments = (first_moment, second_moment)
    if not two_stage:
        moments, _ = lax.optimization_barrier((moments, their_weights))
        their_moments = from_partner(moments, "expert", swap_bit)
    weights = jnp.where(swapped, their_weights, weights)
    if groups == 2:
        other = lax.ppermute(weights, "dp", [(0, 1), (1, 0)])
        first_half = lax.axis_index("dp") == 0
        whole = jnp.concatenate(
            [jnp.where(first_half, weights, other), jnp.where(first_half, other, weights)],
            axis=1,
        )[0]
    else:
        whole = lax.all_gather(weights, "dp", axis=1, tiled=True)[0]
    w_gate = whole[:, 0, :]
    w_up = whole[:, 1, :]
    w_down = whole[:, 2, :]
    w_both = jnp.concatenate([w_gate, w_up], axis=1)
    pre_gate = jnp.dot(rows, w_gate, preferred_element_type=jnp.float32)
    pre_up = jnp.dot(rows, w_up, preferred_element_type=jnp.float32)
    activated, act_slope = silu_parts(pre_gate)
    hidden = (activated * pre_up).astype(jnp.bfloat16)
    contract_hidden = (((1,), (1,)), ((), ()))
    projected = jnp.dot(grads_in, w_down, preferred_element_type=jnp.float32)
    gate_rows = jnp.sum(hidden.astype(jnp.float32) * projected, axis=1).astype(jnp.bfloat16)
    scaled_grad = (gates[:, None] * grads_in.astype(jnp.float32)).astype(jnp.bfloat16)
    hidden_grad = jnp.dot(scaled_grad, w_down, preferred_element_type=jnp.float32)
    gate_delta = (hidden_grad * pre_up * act_slope).astype(jnp.bfloat16)
    up_delta = (hidden_grad * activated).astype(jnp.bfloat16)
    both_delta = jnp.concatenate([gate_delta, up_delta], axis=1)
    row_grad = lax.dot_general(
        both_delta, w_both, contract_hidden, preferred_element_type=jnp.float32
    )
    row_grad = row_grad.astype(jnp.bfloat16)
    contract_rows = (((0,), (0,)), ((), ()))
    grad_gate = lax.dot_general(rows, gate_delta, contract_rows, preferred_element_type=jnp.float32)
    grad_up = lax.dot_general(rows, up_delta, contract_rows, preferred_element_type=jnp.float32)
    grad_down = lax.dot_general(
        scaled_grad, hidden, contract_rows, preferred_element_type=jnp.float32
    )
    part = jnp.stack([grad_gate, grad_up, grad_down], axis=1).astype(jnp.bfloat16)
    if groups == 2:
        row_half = part.shape[0] // 2
        first_half = lax.axis_index("dp") == 0
        keep = jnp.where(first_half, part[:row_half], part[row_half:])
        give = jnp.where(first_half, part[row_half:], part[:row_half])
        got = lax.ppermute(give, "dp", [(0, 1), (1, 0)])
        grad = (keep.astype(jnp.float32) + got.astype(jnp.float32)) * (1.0 / groups)
    else:
        grad = lax.psum_scatter(
            part, "dp", scatter_dimension=0, tiled=True
        ).astype(jnp.float32) * (1.0 / groups)
    grad = grad[None]

    if two_stage:
        back_in = jnp.concatenate([row_grad, with_tile(gate_rows)], axis=1)
        back_in, moments = lax.optimization_barrier((back_in, moments))
        back_all = spread(back_in)
        their_moments = from_partner(moments, "expert", swap_bit)
        back_rows = back_all[:, :model_width]
        back_gate = back_all[:, model_width].astype(jnp.float32)
        weight_of = jnp.where(slot_hit, gate2[None, :], 0.0)
        weight_of = jnp.sum(weight_of.reshape(half_axis * chunk, 2 * tok_rows, route_count), axis=2)
        partial = lax.dot_general(
            weight_of,
            back_rows.astype(jnp.float32),
            (((0,), (0,)), ((), ())),
            precision=lax.Precision.HIGHEST,
            preferred_element_type=jnp.float32,
        )
        prob2 = jnp.sum(jnp.where(slot_hit, back_gate[:, None], 0.0), axis=0)
        p_partial, p_prob = from_partner(
            (partial[tok_rows:].astype(jnp.bfloat16), prob2[entry_count:].astype(jnp.bfloat16)),
            "expert",
            swap_bit,
        )
        token_grad = (partial[:tok_rows] + p_partial.astype(jnp.float32)).astype(jnp.bfloat16)
        prob_grad = jnp.where(
            in_half[:entry_count], prob2[:entry_count], p_prob.astype(jnp.float32)
        )
        prob_grad = prob_grad.astype(jnp.bfloat16).reshape(tok_rows, route_count)
    else:
        back_rows, back_gate = [
            lax.all_to_all(
                part.reshape((axis_width, slot_cap) + part.shape[1:]),
                "expert",
                split_axis=0,
                concat_axis=0,
                tiled=True,
            )
            for part in (row_grad, gate_rows)
        ]
        gathered = back_rows.reshape(slot_count, model_width)[slot_of].astype(jnp.float32)
        token_grad = (
            (gathered * flat_gate[:, None])
            .reshape(tok_rows, route_count, model_width)
            .sum(axis=1)
            .astype(jnp.bfloat16)
        )
        prob_grad = back_gate.reshape(slot_count)[slot_of].reshape(tok_rows, route_count)
    first_moment = jnp.where(swapped, their_moments[0], first_moment)
    second_moment = jnp.where(swapped, their_moments[1], second_moment)
    new_first = (0.9 * first_moment.astype(jnp.float32) + 0.1 * grad).astype(jnp.bfloat16)
    new_second = (0.95 * second_moment.astype(jnp.float32) + 0.05 * grad * grad).astype(
        jnp.bfloat16
    )
    return (token_grad, prob_grad, weights, grad, new_first, new_second)


def solution(mesh):
    in_specs = (
        P(("dp", "expert"), None),
        P(("dp", "expert"), None),
        P(("dp", "expert"), None),
        P(("dp", "expert"), None),
        P("expert", "dp", None, None),
        P("expert", "dp", None, None),
        P("expert", "dp", None, None),
        P(),
    )
    out_specs = (
        P(("dp", "expert"), None),
        P(("dp", "expert"), None),
        P("expert", "dp", None, None),
        P("expert", "dp", None, None),
        P("expert", "dp", None, None),
        P("expert", "dp", None, None),
    )
    return jax.shard_map(
        on_device, mesh=mesh, in_specs=in_specs, out_specs=out_specs, check_vma=False
    )
```

```python
import jax
import jax.numpy as jnp
from jax import lax
from jax.sharding import PartitionSpec as P


def from_partner(value, axis, bit):
    return lax.ppermute(value, axis, [(i, i ^ 1 << bit) for i in range(lax.axis_size(axis))])


def silu_parts(pre_gate):
    sig = jax.nn.sigmoid(pre_gate)
    return (pre_gate * sig, sig * (1.0 + pre_gate * (1.0 - sig)))


def send_slots(tokens, out_grad, flat_gate, slot_of, slot_cap):
    axis_width = lax.axis_size("expert")
    model_width = tokens.shape[1]
    entry_count = flat_gate.shape[0]
    route_count = entry_count // tokens.shape[0]
    slot_count = axis_width * slot_cap
    slot_hit = jnp.arange(slot_count, dtype=jnp.int32)[:, None] == slot_of[None, :]
    filled = jnp.any(slot_hit, axis=1)
    entry_lanes = jnp.arange(entry_count, dtype=jnp.int32)
    slot_entry = jnp.sum(jnp.where(slot_hit, entry_lanes[None, :], 0), axis=1)
    token_of = slot_entry // route_count
    zero_row = jnp.zeros((), jnp.bfloat16)
    send_rows = jnp.where(filled[:, None], tokens[token_of], zero_row)
    send_grads = jnp.where(filled[:, None], out_grad[token_of], zero_row)
    send_gate = jnp.where(filled, flat_gate[slot_entry], 0.0).astype(jnp.bfloat16)
    moved = [
        lax.all_to_all(
            part.reshape((axis_width, slot_cap) + part.shape[1:]),
            "expert",
            split_axis=0,
            concat_axis=0,
            tiled=True,
        )
        for part in (send_rows, send_grads, send_gate)
    ]
    rows = moved[0].reshape(slot_count, model_width)
    grads_in = moved[1].reshape(slot_count, model_width)
    gates = moved[2].reshape(slot_count).astype(jnp.float32)
    return rows, grads_in, gates


def xor_permute(value, mask):
    return lax.ppermute(value, "expert", [(i, i ^ mask) for i in range(lax.axis_size("expert"))])


def with_tile(column):
    lanes = jnp.arange(128, dtype=jnp.int32)[None, :] == 0
    return jnp.where(lanes, column.astype(jnp.bfloat16)[:, None], jnp.zeros((), jnp.bfloat16))


def entry_ranks(flat_ids, axis_width):
    id_onehot = (flat_ids[:, None] == jnp.arange(axis_width, dtype=jnp.int32)[None, :]).astype(
        jnp.int32
    )
    return jnp.sum((jnp.cumsum(id_onehot, axis=0) - id_onehot) * id_onehot, axis=1)


def on_device(
    tokens, out_grad, expert_ids, gate_probs, weights, first_moment, second_moment, moving_pairs
):
    axis_width = lax.axis_size("expert")
    half_axis = axis_width // 2
    swap_bit = half_axis.bit_length() - 1
    groups = lax.axis_size("dp")
    my_index = lax.axis_index("expert")
    tok_rows, route_count = expert_ids.shape
    model_width = tokens.shape[1]
    entry_count = tok_rows * route_count
    slot_cap = 5 * entry_count // (4 * axis_width)
    slot_count = axis_width * slot_cap
    pair_lanes = jnp.arange(half_axis, dtype=jnp.int32)
    my_move = jnp.sum(jnp.where(pair_lanes == my_index % half_axis, moving_pairs, 0))
    swapped = my_move == 1
    held = jnp.where(swapped, (my_index + half_axis) % axis_width, my_index)

    flat_gate = gate_probs.reshape(-1)
    flat_ids = expert_ids.reshape(-1)

    def holder_of(ids):
        lane_hit = (ids % half_axis)[:, None] == pair_lanes[None, :]
        moves = jnp.sum(jnp.where(lane_hit, moving_pairs[None, :], 0), axis=1)
        return jnp.where(moves == 1, (ids + half_axis) % axis_width, ids)

    two_stage = half_axis <= 8
    if two_stage:
        packed = jnp.concatenate([tokens, out_grad], axis=1)
        slabs = jnp.stack([weights, first_moment, second_moment])
        p_packed, p_ids, p_gate, p_slabs = from_partner(
            (packed, expert_ids, gate_probs, slabs), "expert", swap_bit
        )
        their_weights = p_slabs[0]
        both = jnp.concatenate([packed, p_packed], axis=0)
        ids2 = jnp.concatenate([flat_ids, p_ids.reshape(-1)])
        gate2 = jnp.concatenate([flat_gate, p_gate.reshape(-1)])
        holder2 = holder_of(ids2)
        rank2 = jnp.concatenate(
            [entry_ranks(flat_ids, axis_width), entry_ranks(p_ids.reshape(-1), axis_width)]
        )
        src2 = jnp.arange(2 * entry_count, dtype=jnp.int32) // entry_count
        in_half = holder2 // half_axis == my_index // half_axis
        lane2 = holder2 % half_axis
        chunk = 2 * slot_cap
        slot2 = lane2 * chunk + src2 * slot_cap + rank2
        slot_hit = (
            jnp.arange(half_axis * chunk, dtype=jnp.int32)[:, None] == slot2[None, :]
        ) & in_half[None, :]
        tok_hit = jnp.any(slot_hit.reshape(half_axis * chunk, 2 * tok_rows, route_count), axis=2)
        tok_pick = tok_hit.astype(jnp.bfloat16)
        send_both = jnp.dot(tok_pick, both, preferred_element_type=jnp.float32).astype(
            jnp.bfloat16
        )
        wire2 = gate2.astype(jnp.bfloat16).astype(jnp.float32)
        send_gate = jnp.sum(jnp.where(slot_hit, wire2[None, :], 0.0), axis=1)
        send_all = jnp.concatenate([send_both, with_tile(send_gate)], axis=1)

        halves = [list(range(h * half_axis, (h + 1) * half_axis)) for h in range(2)]

        def spread(value):
            parts = value.reshape((half_axis, chunk) + value.shape[1:])
            moved = lax.all_to_all(
                parts, "expert", 0, 0, tiled=True, axis_index_groups=halves
            )
            return moved.reshape(value.shape)

        recv_all = spread(send_all)
        rows = recv_all[:, :model_width]
        grads_in = recv_all[:, model_width : 2 * model_width]
        gates = recv_all[:, 2 * model_width].astype(jnp.float32)
    else:
        slot_of = holder_of(flat_ids) * slot_cap + entry_ranks(flat_ids, axis_width)
        rows, grads_in, gates = send_slots(tokens, out_grad, flat_gate, slot_of, slot_cap)
    if not two_stage:
        their_weights = from_partner(weights, "expert", swap_bit)
    if two_stage:
        their_moments = (p_slabs[1], p_slabs[2])
    else:
        first_moment, second_moment, _ = lax.optimization_barrier(
            (first_moment, second_moment, their_weights)
        )
        their_moments = from_partner((first_moment, second_moment), "expert", swap_bit)
    weights = jnp.where(swapped, their_weights, weights)
    if groups == 2:
        other = lax.ppermute(weights, "dp", [(0, 1), (1, 0)])
        first_half = lax.axis_index("dp") == 0
        whole = jnp.concatenate(
            [jnp.where(first_half, weights, other), jnp.where(first_half, other, weights)],
            axis=1,
        )[0]
    else:
        whole = lax.all_gather(weights, "dp", axis=1, tiled=True)[0]
    w_gate = whole[:, 0, :]
    w_up = whole[:, 1, :]
    w_down = whole[:, 2, :]
    w_both = jnp.concatenate([w_gate, w_up], axis=1)
    pre_gate = jnp.dot(rows, w_gate, preferred_element_type=jnp.float32)
    pre_up = jnp.dot(rows, w_up, preferred_element_type=jnp.float32)
    activated, act_slope = silu_parts(pre_gate)
    hidden = (activated * pre_up).astype(jnp.bfloat16)
    contract_hidden = (((1,), (1,)), ((), ()))
    projected = jnp.dot(grads_in, w_down, preferred_element_type=jnp.float32)
    gate_rows = jnp.sum(hidden.astype(jnp.float32) * projected, axis=1).astype(jnp.bfloat16)
    scaled_grad = (gates[:, None] * grads_in.astype(jnp.float32)).astype(jnp.bfloat16)
    hidden_grad = jnp.dot(scaled_grad, w_down, preferred_element_type=jnp.float32)
    gate_delta = (hidden_grad * pre_up * act_slope).astype(jnp.bfloat16)
    up_delta = (hidden_grad * activated).astype(jnp.bfloat16)
    both_delta = jnp.concatenate([gate_delta, up_delta], axis=1)
    row_grad = lax.dot_general(
        both_delta, w_both, contract_hidden, preferred_element_type=jnp.float32
    )
    row_grad = row_grad.astype(jnp.bfloat16)
    contract_rows = (((0,), (0,)), ((), ()))
    grad_gate = lax.dot_general(rows, gate_delta, contract_rows, preferred_element_type=jnp.float32)
    grad_up = lax.dot_general(rows, up_delta, contract_rows, preferred_element_type=jnp.float32)
    grad_down = lax.dot_general(
        scaled_grad, hidden, contract_rows, preferred_element_type=jnp.float32
    )
    part = jnp.stack([grad_gate, grad_up, grad_down], axis=1).astype(jnp.bfloat16)
    if groups == 2:
        row_half = part.shape[0] // 2
        first_half = lax.axis_index("dp") == 0
        keep = jnp.where(first_half, part[:row_half], part[row_half:])
        give = jnp.where(first_half, part[row_half:], part[:row_half])
        got = lax.ppermute(give, "dp", [(0, 1), (1, 0)])
        grad = (keep.astype(jnp.float32) + got.astype(jnp.float32)) * (1.0 / groups)
    else:
        grad = lax.psum_scatter(
            part, "dp", scatter_dimension=0, tiled=True
        ).astype(jnp.float32) * (1.0 / groups)
    grad = grad[None]
    first_moment = jnp.where(swapped, their_moments[0], first_moment)
    second_moment = jnp.where(swapped, their_moments[1], second_moment)
    new_first = (0.9 * first_moment.astype(jnp.float32) + 0.1 * grad).astype(jnp.bfloat16)
    new_second = (0.95 * second_moment.astype(jnp.float32) + 0.05 * grad * grad).astype(
        jnp.bfloat16
    )

    if two_stage:
        back_all = spread(jnp.concatenate([row_grad, with_tile(gate_rows)], axis=1))
        back_rows = back_all[:, :model_width]
        back_gate = back_all[:, model_width].astype(jnp.float32)
        weight_of = jnp.where(slot_hit, gate2[None, :], 0.0)
        weight_of = jnp.sum(weight_of.reshape(half_axis * chunk, 2 * tok_rows, route_count), axis=2)
        partial = lax.dot_general(
            weight_of,
            back_rows.astype(jnp.float32),
            (((0,), (0,)), ((), ())),
            precision=lax.Precision.HIGHEST,
            preferred_element_type=jnp.float32,
        )
        prob2 = jnp.sum(jnp.where(slot_hit, back_gate[:, None], 0.0), axis=0)
        p_partial, p_prob = from_partner(
            (partial[tok_rows:].astype(jnp.bfloat16), prob2[entry_count:].astype(jnp.bfloat16)),
            "expert",
            swap_bit,
        )
        token_grad = (partial[:tok_rows] + p_partial.astype(jnp.float32)).astype(jnp.bfloat16)
        prob_grad = jnp.where(
            in_half[:entry_count], prob2[:entry_count], p_prob.astype(jnp.float32)
        )
        prob_grad = prob_grad.astype(jnp.bfloat16).reshape(tok_rows, route_count)
    else:
        back_rows, back_gate = [
            lax.all_to_all(
                part.reshape((axis_width, slot_cap) + part.shape[1:]),
                "expert",
                split_axis=0,
                concat_axis=0,
                tiled=True,
            )
            for part in (row_grad, gate_rows)
        ]
        gathered = back_rows.reshape(slot_count, model_width)[slot_of].astype(jnp.float32)
        token_grad = (
            (gathered * flat_gate[:, None])
            .reshape(tok_rows, route_count, model_width)
            .sum(axis=1)
            .astype(jnp.bfloat16)
        )
        prob_grad = back_gate.reshape(slot_count)[slot_of].reshape(tok_rows, route_count)
    return (token_grad, prob_grad, weights, grad, new_first, new_second)


def solution(mesh):
    in_specs = (
        P(("dp", "expert"), None),
        P(("dp", "expert"), None),
        P(("dp", "expert"), None),
        P(("dp", "expert"), None),
        P("expert", "dp", None, None),
        P("expert", "dp", None, None),
        P("expert", "dp", None, None),
        P(),
    )
    out_specs = (
        P(("dp", "expert"), None),
        P(("dp", "expert"), None),
        P("expert", "dp", None, None),
        P("expert", "dp", None, None),
        P("expert", "dp", None, None),
        P("expert", "dp", None, None),
    )
    return jax.shard_map(
        on_device, mesh=mesh, in_specs=in_specs, out_specs=out_specs, check_vma=False
    )
```

```python
import jax
import jax.numpy as jnp
from jax import lax
from jax.sharding import PartitionSpec as P


def from_partner(value, axis, bit):
    return lax.ppermute(value, axis, [(i, i ^ 1 << bit) for i in range(lax.axis_size(axis))])


def silu_parts(pre_gate):
    sig = jax.nn.sigmoid(pre_gate)
    return (pre_gate * sig, sig * (1.0 + pre_gate * (1.0 - sig)))


def send_slots(tokens, out_grad, flat_gate, slot_of, slot_cap):
    axis_width = lax.axis_size("expert")
    model_width = tokens.shape[1]
    entry_count = flat_gate.shape[0]
    route_count = entry_count // tokens.shape[0]
    slot_count = axis_width * slot_cap
    slot_hit = jnp.arange(slot_count, dtype=jnp.int32)[:, None] == slot_of[None, :]
    filled = jnp.any(slot_hit, axis=1)
    entry_lanes = jnp.arange(entry_count, dtype=jnp.int32)
    slot_entry = jnp.sum(jnp.where(slot_hit, entry_lanes[None, :], 0), axis=1)
    token_of = slot_entry // route_count
    zero_row = jnp.zeros((), jnp.bfloat16)
    send_rows = jnp.where(filled[:, None], tokens[token_of], zero_row)
    send_grads = jnp.where(filled[:, None], out_grad[token_of], zero_row)
    send_gate = jnp.where(filled, flat_gate[slot_entry], 0.0).astype(jnp.bfloat16)
    moved = [
        lax.all_to_all(
            part.reshape((axis_width, slot_cap) + part.shape[1:]),
            "expert",
            split_axis=0,
            concat_axis=0,
            tiled=True,
        )
        for part in (send_rows, send_grads, send_gate)
    ]
    rows = moved[0].reshape(slot_count, model_width)
    grads_in = moved[1].reshape(slot_count, model_width)
    gates = moved[2].reshape(slot_count).astype(jnp.float32)
    return rows, grads_in, gates


def xor_permute(value, mask):
    return lax.ppermute(value, "expert", [(i, i ^ mask) for i in range(lax.axis_size("expert"))])


def with_tile(column):
    lanes = jnp.arange(128, dtype=jnp.int32)[None, :] == 0
    return jnp.where(lanes, column.astype(jnp.bfloat16)[:, None], jnp.zeros((), jnp.bfloat16))


def entry_ranks(flat_ids, axis_width):
    id_onehot = (flat_ids[:, None] == jnp.arange(axis_width, dtype=jnp.int32)[None, :]).astype(
        jnp.int32
    )
    return jnp.sum((jnp.cumsum(id_onehot, axis=0) - id_onehot) * id_onehot, axis=1)


def on_device(
    tokens, out_grad, expert_ids, gate_probs, weights, first_moment, second_moment, moving_pairs
):
    axis_width = lax.axis_size("expert")
    half_axis = axis_width // 2
    swap_bit = half_axis.bit_length() - 1
    groups = lax.axis_size("dp")
    my_index = lax.axis_index("expert")
    tok_rows, route_count = expert_ids.shape
    model_width = tokens.shape[1]
    entry_count = tok_rows * route_count
    slot_cap = 5 * entry_count // (4 * axis_width)
    slot_count = axis_width * slot_cap
    pair_lanes = jnp.arange(half_axis, dtype=jnp.int32)
    my_move = jnp.sum(jnp.where(pair_lanes == my_index % half_axis, moving_pairs, 0))
    swapped = my_move == 1
    held = jnp.where(swapped, (my_index + half_axis) % axis_width, my_index)

    flat_gate = gate_probs.reshape(-1)
    flat_ids = expert_ids.reshape(-1)

    def holder_of(ids):
        lane_hit = (ids % half_axis)[:, None] == pair_lanes[None, :]
        moves = jnp.sum(jnp.where(lane_hit, moving_pairs[None, :], 0), axis=1)
        return jnp.where(moves == 1, (ids + half_axis) % axis_width, ids)

    two_stage = half_axis <= 8
    if two_stage:
        gate_hi = gate_probs.astype(jnp.bfloat16)
        gate_rest = gate_probs - gate_hi.astype(jnp.float32)
        gate_mid = gate_rest.astype(jnp.bfloat16)
        gate_lo = (gate_rest - gate_mid.astype(jnp.float32)).astype(jnp.bfloat16)
        side = jnp.concatenate(
            [
                expert_ids.astype(jnp.bfloat16),
                gate_hi,
                gate_mid,
                gate_lo,
                jnp.zeros((tok_rows, 128 - 4 * route_count), jnp.bfloat16),
            ],
            axis=1,
        )
        packed = jnp.concatenate([tokens, out_grad, side], axis=1)
        p_packed, their_weights = from_partner((packed, weights), "expert", swap_bit)
        p_side = p_packed[:, 2 * model_width :].astype(jnp.float32)
        p_ids = p_side[:, :route_count].astype(jnp.int32)
        p_gate = (
            p_side[:, route_count : 2 * route_count]
            + p_side[:, 2 * route_count : 3 * route_count]
        ) + p_side[:, 3 * route_count : 4 * route_count]
        both = jnp.concatenate([packed, p_packed], axis=0)[:, : 2 * model_width]
        ids2 = jnp.concatenate([flat_ids, p_ids.reshape(-1)])
        gate2 = jnp.concatenate([flat_gate, p_gate.reshape(-1)])
        holder2 = holder_of(ids2)
        rank2 = jnp.concatenate(
            [entry_ranks(flat_ids, axis_width), entry_ranks(p_ids.reshape(-1), axis_width)]
        )
        src2 = jnp.arange(2 * entry_count, dtype=jnp.int32) // entry_count
        in_half = holder2 // half_axis == my_index // half_axis
        lane2 = holder2 % half_axis
        chunk = 2 * slot_cap
        slot2 = lane2 * chunk + src2 * slot_cap + rank2
        slot_hit = (
            jnp.arange(half_axis * chunk, dtype=jnp.int32)[:, None] == slot2[None, :]
        ) & in_half[None, :]
        tok_hit = jnp.any(slot_hit.reshape(half_axis * chunk, 2 * tok_rows, route_count), axis=2)
        tok_pick = tok_hit.astype(jnp.bfloat16)
        send_both = jnp.dot(tok_pick, both, preferred_element_type=jnp.float32).astype(
            jnp.bfloat16
        )
        wire2 = gate2.astype(jnp.bfloat16).astype(jnp.float32)
        send_gate = jnp.sum(jnp.where(slot_hit, wire2[None, :], 0.0), axis=1)
        send_all = jnp.concatenate([send_both, with_tile(send_gate)], axis=1)

        halves = [list(range(h * half_axis, (h + 1) * half_axis)) for h in range(2)]

        def spread(value):
            parts = value.reshape((half_axis, chunk) + value.shape[1:])
            moved = lax.all_to_all(
                parts, "expert", 0, 0, tiled=True, axis_index_groups=halves
            )
            return moved.reshape(value.shape)

        recv_all = spread(send_all)
        rows = recv_all[:, :model_width]
        grads_in = recv_all[:, model_width : 2 * model_width]
        gates = recv_all[:, 2 * model_width].astype(jnp.float32)
    else:
        slot_of = holder_of(flat_ids) * slot_cap + entry_ranks(flat_ids, axis_width)
        rows, grads_in, gates = send_slots(tokens, out_grad, flat_gate, slot_of, slot_cap)
    if not two_stage:
        their_weights = from_partner(weights, "expert", swap_bit)
    first_moment, second_moment, _ = lax.optimization_barrier(
        (first_moment, second_moment, their_weights)
    )
    their_moments = from_partner((first_moment, second_moment), "expert", swap_bit)
    weights = jnp.where(swapped, their_weights, weights)
    if groups == 2:
        other = lax.ppermute(weights, "dp", [(0, 1), (1, 0)])
        first_half = lax.axis_index("dp") == 0
        whole = jnp.concatenate(
            [jnp.where(first_half, weights, other), jnp.where(first_half, other, weights)],
            axis=1,
        )[0]
    else:
        whole = lax.all_gather(weights, "dp", axis=1, tiled=True)[0]
    w_gate = whole[:, 0, :]
    w_up = whole[:, 1, :]
    w_down = whole[:, 2, :]
    w_both = jnp.concatenate([w_gate, w_up], axis=1)
    pre_gate = jnp.dot(rows, w_gate, preferred_element_type=jnp.float32)
    pre_up = jnp.dot(rows, w_up, preferred_element_type=jnp.float32)
    activated, act_slope = silu_parts(pre_gate)
    hidden = (activated * pre_up).astype(jnp.bfloat16)
    contract_hidden = (((1,), (1,)), ((), ()))
    projected = jnp.dot(grads_in, w_down, preferred_element_type=jnp.float32)
    gate_rows = jnp.sum(hidden.astype(jnp.float32) * projected, axis=1).astype(jnp.bfloat16)
    scaled_grad = (gates[:, None] * grads_in.astype(jnp.float32)).astype(jnp.bfloat16)
    hidden_grad = jnp.dot(scaled_grad, w_down, preferred_element_type=jnp.float32)
    gate_delta = (hidden_grad * pre_up * act_slope).astype(jnp.bfloat16)
    up_delta = (hidden_grad * activated).astype(jnp.bfloat16)
    both_delta = jnp.concatenate([gate_delta, up_delta], axis=1)
    row_grad = lax.dot_general(
        both_delta, w_both, contract_hidden, preferred_element_type=jnp.float32
    )
    row_grad = row_grad.astype(jnp.bfloat16)
    contract_rows = (((0,), (0,)), ((), ()))
    grad_gate = lax.dot_general(rows, gate_delta, contract_rows, preferred_element_type=jnp.float32)
    grad_up = lax.dot_general(rows, up_delta, contract_rows, preferred_element_type=jnp.float32)
    grad_down = lax.dot_general(
        scaled_grad, hidden, contract_rows, preferred_element_type=jnp.float32
    )
    part = jnp.stack([grad_gate, grad_up, grad_down], axis=1).astype(jnp.bfloat16)
    if groups == 2:
        row_half = part.shape[0] // 2
        first_half = lax.axis_index("dp") == 0
        keep = jnp.where(first_half, part[:row_half], part[row_half:])
        give = jnp.where(first_half, part[row_half:], part[:row_half])
        got = lax.ppermute(give, "dp", [(0, 1), (1, 0)])
        grad = (keep.astype(jnp.float32) + got.astype(jnp.float32)) * (1.0 / groups)
    else:
        grad = lax.psum_scatter(
            part, "dp", scatter_dimension=0, tiled=True
        ).astype(jnp.float32) * (1.0 / groups)
    grad = grad[None]
    first_moment = jnp.where(swapped, their_moments[0], first_moment)
    second_moment = jnp.where(swapped, their_moments[1], second_moment)
    new_first = (0.9 * first_moment.astype(jnp.float32) + 0.1 * grad).astype(jnp.bfloat16)
    new_second = (0.95 * second_moment.astype(jnp.float32) + 0.05 * grad * grad).astype(
        jnp.bfloat16
    )

    if two_stage:
        back_all = spread(jnp.concatenate([row_grad, with_tile(gate_rows)], axis=1))
        back_rows = back_all[:, :model_width]
        back_gate = back_all[:, model_width].astype(jnp.float32)
        weight_of = jnp.where(slot_hit, gate2[None, :], 0.0)
        weight_of = jnp.sum(weight_of.reshape(half_axis * chunk, 2 * tok_rows, route_count), axis=2)
        partial = lax.dot_general(
            weight_of,
            back_rows.astype(jnp.float32),
            (((0,), (0,)), ((), ())),
            precision=lax.Precision.HIGHEST,
            preferred_element_type=jnp.float32,
        )
        prob2 = jnp.sum(jnp.where(slot_hit, back_gate[:, None], 0.0), axis=0)
        p_partial, p_prob = from_partner(
            (partial[tok_rows:].astype(jnp.bfloat16), prob2[entry_count:].astype(jnp.bfloat16)),
            "expert",
            swap_bit,
        )
        token_grad = (partial[:tok_rows] + p_partial.astype(jnp.float32)).astype(jnp.bfloat16)
        prob_grad = jnp.where(
            in_half[:entry_count], prob2[:entry_count], p_prob.astype(jnp.float32)
        )
        prob_grad = prob_grad.astype(jnp.bfloat16).reshape(tok_rows, route_count)
    else:
        back_rows, back_gate = [
            lax.all_to_all(
                part.reshape((axis_width, slot_cap) + part.shape[1:]),
                "expert",
                split_axis=0,
                concat_axis=0,
                tiled=True,
            )
            for part in (row_grad, gate_rows)
        ]
        gathered = back_rows.reshape(slot_count, model_width)[slot_of].astype(jnp.float32)
        token_grad = (
            (gathered * flat_gate[:, None])
            .reshape(tok_rows, route_count, model_width)
            .sum(axis=1)
            .astype(jnp.bfloat16)
        )
        prob_grad = back_gate.reshape(slot_count)[slot_of].reshape(tok_rows, route_count)
    return (token_grad, prob_grad, weights, grad, new_first, new_second)


def solution(mesh):
    in_specs = (
        P(("dp", "expert"), None),
        P(("dp", "expert"), None),
        P(("dp", "expert"), None),
        P(("dp", "expert"), None),
        P("expert", "dp", None, None),
        P("expert", "dp", None, None),
        P("expert", "dp", None, None),
        P(),
    )
    out_specs = (
        P(("dp", "expert"), None),
        P(("dp", "expert"), None),
        P("expert", "dp", None, None),
        P("expert", "dp", None, None),
        P("expert", "dp", None, None),
        P("expert", "dp", None, None),
    )
    return jax.shard_map(
        on_device, mesh=mesh, in_specs=in_specs, out_specs=out_specs, check_vma=False
    )
```

```python
import jax
import jax.numpy as jnp
from jax import lax
from jax.sharding import PartitionSpec as P


def from_partner(value, axis, bit):
    return lax.ppermute(value, axis, [(i, i ^ 1 << bit) for i in range(lax.axis_size(axis))])


def silu_parts(pre_gate):
    sig = jax.nn.sigmoid(pre_gate)
    return (pre_gate * sig, sig * (1.0 + pre_gate * (1.0 - sig)))


def send_slots(tokens, out_grad, flat_gate, slot_of, slot_cap):
    axis_width = lax.axis_size("expert")
    model_width = tokens.shape[1]
    entry_count = flat_gate.shape[0]
    route_count = entry_count // tokens.shape[0]
    slot_count = axis_width * slot_cap
    slot_hit = jnp.arange(slot_count, dtype=jnp.int32)[:, None] == slot_of[None, :]
    filled = jnp.any(slot_hit, axis=1)
    entry_lanes = jnp.arange(entry_count, dtype=jnp.int32)
    slot_entry = jnp.sum(jnp.where(slot_hit, entry_lanes[None, :], 0), axis=1)
    token_of = slot_entry // route_count
    zero_row = jnp.zeros((), jnp.bfloat16)
    send_rows = jnp.where(filled[:, None], tokens[token_of], zero_row)
    send_grads = jnp.where(filled[:, None], out_grad[token_of], zero_row)
    send_gate = jnp.where(filled, flat_gate[slot_entry], 0.0).astype(jnp.bfloat16)
    moved = [
        lax.all_to_all(
            part.reshape((axis_width, slot_cap) + part.shape[1:]),
            "expert",
            split_axis=0,
            concat_axis=0,
            tiled=True,
        )
        for part in (send_rows, send_grads, send_gate)
    ]
    rows = moved[0].reshape(slot_count, model_width)
    grads_in = moved[1].reshape(slot_count, model_width)
    gates = moved[2].reshape(slot_count).astype(jnp.float32)
    return rows, grads_in, gates


def xor_permute(value, mask):
    return lax.ppermute(value, "expert", [(i, i ^ mask) for i in range(lax.axis_size("expert"))])


def with_tile(column):
    lanes = jnp.arange(128, dtype=jnp.int32)[None, :] == 0
    return jnp.where(lanes, column.astype(jnp.bfloat16)[:, None], jnp.zeros((), jnp.bfloat16))


def entry_ranks(flat_ids, axis_width):
    id_onehot = (flat_ids[:, None] == jnp.arange(axis_width, dtype=jnp.int32)[None, :]).astype(
        jnp.int32
    )
    return jnp.sum((jnp.cumsum(id_onehot, axis=0) - id_onehot) * id_onehot, axis=1)


def on_device(
    tokens, out_grad, expert_ids, gate_probs, weights, first_moment, second_moment, moving_pairs
):
    axis_width = lax.axis_size("expert")
    half_axis = axis_width // 2
    swap_bit = half_axis.bit_length() - 1
    groups = lax.axis_size("dp")
    my_index = lax.axis_index("expert")
    tok_rows, route_count = expert_ids.shape
    model_width = tokens.shape[1]
    entry_count = tok_rows * route_count
    slot_cap = 5 * entry_count // (4 * axis_width)
    slot_count = axis_width * slot_cap
    pair_lanes = jnp.arange(half_axis, dtype=jnp.int32)
    my_move = jnp.sum(jnp.where(pair_lanes == my_index % half_axis, moving_pairs, 0))
    swapped = my_move == 1
    held = jnp.where(swapped, (my_index + half_axis) % axis_width, my_index)

    flat_gate = gate_probs.reshape(-1)
    flat_ids = expert_ids.reshape(-1)

    def holder_of(ids):
        lane_hit = (ids % half_axis)[:, None] == pair_lanes[None, :]
        moves = jnp.sum(jnp.where(lane_hit, moving_pairs[None, :], 0), axis=1)
        return jnp.where(moves == 1, (ids + half_axis) % axis_width, ids)

    two_stage = half_axis <= 8
    if two_stage:
        plane = min(4, half_axis)
        column = axis_width // plane
        packed = jnp.concatenate([tokens, out_grad], axis=1)
        got = [(packed, expert_ids, gate_probs)]
        for k in range(1, column):
            got.append(xor_permute((packed, expert_ids, gate_probs), k * plane))
        weights, got = lax.optimization_barrier((weights, got))
        their_weights = from_partner(weights, "expert", swap_bit)
        both = jnp.concatenate([g[0] for g in got], axis=0)
        ids2 = jnp.concatenate([g[1].reshape(-1) for g in got])
        gate2 = jnp.concatenate([g[2].reshape(-1) for g in got])
        holder2 = holder_of(ids2)
        rank2 = jnp.concatenate([entry_ranks(g[1].reshape(-1), axis_width) for g in got])
        src2 = jnp.arange(column * entry_count, dtype=jnp.int32) // entry_count
        in_half = holder2 // plane == my_index // plane
        lane2 = holder2 % plane
        chunk = column * slot_cap
        slot2 = lane2 * chunk + src2 * slot_cap + rank2
        slot_hit = (
            jnp.arange(plane * chunk, dtype=jnp.int32)[:, None] == slot2[None, :]
        ) & in_half[None, :]
        tok_hit = jnp.any(
            slot_hit.reshape(plane * chunk, column * tok_rows, route_count), axis=2
        )
        tok_pick = tok_hit.astype(jnp.bfloat16)
        send_both = jnp.dot(tok_pick, both, preferred_element_type=jnp.float32).astype(
            jnp.bfloat16
        )
        wire2 = gate2.astype(jnp.bfloat16).astype(jnp.float32)
        send_gate = jnp.sum(jnp.where(slot_hit, wire2[None, :], 0.0), axis=1)
        send_all = jnp.concatenate([send_both, with_tile(send_gate)], axis=1)

        planes = [list(range(h * plane, (h + 1) * plane)) for h in range(column)]

        def spread(value):
            parts = value.reshape((plane, chunk) + value.shape[1:])
            moved = lax.all_to_all(
                parts, "expert", 0, 0, tiled=True, axis_index_groups=planes
            )
            return moved.reshape(value.shape)

        recv_all = spread(send_all)
        rows = recv_all[:, :model_width]
        grads_in = recv_all[:, model_width : 2 * model_width]
        gates = recv_all[:, 2 * model_width].astype(jnp.float32)
    else:
        slot_of = holder_of(flat_ids) * slot_cap + entry_ranks(flat_ids, axis_width)
        rows, grads_in, gates = send_slots(tokens, out_grad, flat_gate, slot_of, slot_cap)
    if not two_stage:
        their_weights = from_partner(weights, "expert", swap_bit)
    first_moment, second_moment, _ = lax.optimization_barrier(
        (first_moment, second_moment, their_weights)
    )
    their_moments = from_partner((first_moment, second_moment), "expert", swap_bit)
    weights = jnp.where(swapped, their_weights, weights)
    if groups == 2:
        other = lax.ppermute(weights, "dp", [(0, 1), (1, 0)])
        first_half = lax.axis_index("dp") == 0
        whole = jnp.concatenate(
            [jnp.where(first_half, weights, other), jnp.where(first_half, other, weights)],
            axis=1,
        )[0]
    else:
        whole = lax.all_gather(weights, "dp", axis=1, tiled=True)[0]
    w_gate = whole[:, 0, :]
    w_up = whole[:, 1, :]
    w_down = whole[:, 2, :]
    w_both = jnp.concatenate([w_gate, w_up], axis=1)
    pre_gate = jnp.dot(rows, w_gate, preferred_element_type=jnp.float32)
    pre_up = jnp.dot(rows, w_up, preferred_element_type=jnp.float32)
    activated, act_slope = silu_parts(pre_gate)
    hidden = (activated * pre_up).astype(jnp.bfloat16)
    contract_hidden = (((1,), (1,)), ((), ()))
    projected = jnp.dot(grads_in, w_down, preferred_element_type=jnp.float32)
    gate_rows = jnp.sum(hidden.astype(jnp.float32) * projected, axis=1).astype(jnp.bfloat16)
    scaled_grad = (gates[:, None] * grads_in.astype(jnp.float32)).astype(jnp.bfloat16)
    hidden_grad = jnp.dot(scaled_grad, w_down, preferred_element_type=jnp.float32)
    gate_delta = (hidden_grad * pre_up * act_slope).astype(jnp.bfloat16)
    up_delta = (hidden_grad * activated).astype(jnp.bfloat16)
    both_delta = jnp.concatenate([gate_delta, up_delta], axis=1)
    row_grad = lax.dot_general(
        both_delta, w_both, contract_hidden, preferred_element_type=jnp.float32
    )
    row_grad = row_grad.astype(jnp.bfloat16)
    contract_rows = (((0,), (0,)), ((), ()))
    grad_gate = lax.dot_general(rows, gate_delta, contract_rows, preferred_element_type=jnp.float32)
    grad_up = lax.dot_general(rows, up_delta, contract_rows, preferred_element_type=jnp.float32)
    grad_down = lax.dot_general(
        scaled_grad, hidden, contract_rows, preferred_element_type=jnp.float32
    )
    part = jnp.stack([grad_gate, grad_up, grad_down], axis=1).astype(jnp.bfloat16)
    if groups == 2:
        row_half = part.shape[0] // 2
        first_half = lax.axis_index("dp") == 0
        keep = jnp.where(first_half, part[:row_half], part[row_half:])
        give = jnp.where(first_half, part[row_half:], part[:row_half])
        got = lax.ppermute(give, "dp", [(0, 1), (1, 0)])
        grad = (keep.astype(jnp.float32) + got.astype(jnp.float32)) * (1.0 / groups)
    else:
        grad = lax.psum_scatter(
            part, "dp", scatter_dimension=0, tiled=True
        ).astype(jnp.float32) * (1.0 / groups)
    grad = grad[None]
    first_moment = jnp.where(swapped, their_moments[0], first_moment)
    second_moment = jnp.where(swapped, their_moments[1], second_moment)
    new_first = (0.9 * first_moment.astype(jnp.float32) + 0.1 * grad).astype(jnp.bfloat16)
    new_second = (0.95 * second_moment.astype(jnp.float32) + 0.05 * grad * grad).astype(
        jnp.bfloat16
    )

    if two_stage:
        back_all = spread(jnp.concatenate([row_grad, with_tile(gate_rows)], axis=1))
        back_rows = back_all[:, :model_width]
        back_gate = back_all[:, model_width].astype(jnp.float32)
        weight_of = jnp.where(slot_hit, gate2[None, :], 0.0)
        weight_of = jnp.sum(
            weight_of.reshape(plane * chunk, column * tok_rows, route_count), axis=2
        )
        partial = lax.dot_general(
            weight_of,
            back_rows.astype(jnp.float32),
            (((0,), (0,)), ((), ())),
            precision=lax.Precision.HIGHEST,
            preferred_element_type=jnp.float32,
        )
        prob2 = jnp.sum(jnp.where(slot_hit, back_gate[:, None], 0.0), axis=0)
        token_acc = partial[:tok_rows]
        prob_parts = [prob2[:entry_count]]
        for k in range(1, column):
            k_partial, k_prob = xor_permute(
                (
                    partial[k * tok_rows : (k + 1) * tok_rows].astype(jnp.bfloat16),
                    prob2[k * entry_count : (k + 1) * entry_count].astype(jnp.bfloat16),
                ),
                k * plane,
            )
            token_acc = token_acc + k_partial.astype(jnp.float32)
            prob_parts.append(k_prob.astype(jnp.float32))
        token_grad = token_acc.astype(jnp.bfloat16)
        served_by = (holder2[:entry_count] // plane) ^ (my_index // plane)
        prob_grad = jnp.zeros((entry_count,), jnp.float32)
        for k in range(column):
            prob_grad = jnp.where(served_by == k, prob_parts[k], prob_grad)
        prob_grad = prob_grad.astype(jnp.bfloat16).reshape(tok_rows, route_count)
    else:
        back_rows, back_gate = [
            lax.all_to_all(
                part.reshape((axis_width, slot_cap) + part.shape[1:]),
                "expert",
                split_axis=0,
                concat_axis=0,
                tiled=True,
            )
            for part in (row_grad, gate_rows)
        ]
        gathered = back_rows.reshape(slot_count, model_width)[slot_of].astype(jnp.float32)
        token_grad = (
            (gathered * flat_gate[:, None])
            .reshape(tok_rows, route_count, model_width)
            .sum(axis=1)
            .astype(jnp.bfloat16)
        )
        prob_grad = back_gate.reshape(slot_count)[slot_of].reshape(tok_rows, route_count)
    return (token_grad, prob_grad, weights, grad, new_first, new_second)


def solution(mesh):
    in_specs = (
        P(("dp", "expert"), None),
        P(("dp", "expert"), None),
        P(("dp", "expert"), None),
        P(("dp", "expert"), None),
        P("expert", "dp", None, None),
        P("expert", "dp", None, None),
        P("expert", "dp", None, None),
        P(),
    )
    out_specs = (
        P(("dp", "expert"), None),
        P(("dp", "expert"), None),
        P("expert", "dp", None, None),
        P("expert", "dp", None, None),
        P("expert", "dp", None, None),
        P("expert", "dp", None, None),
    )
    return jax.shard_map(
        on_device, mesh=mesh, in_specs=in_specs, out_specs=out_specs, check_vma=False
    )
```

```python
import jax
import jax.numpy as jnp
from jax import lax
from jax.sharding import PartitionSpec as P


def from_partner(value, axis, bit):
    return lax.ppermute(value, axis, [(i, i ^ 1 << bit) for i in range(lax.axis_size(axis))])


def silu_parts(pre_gate):
    sig = jax.nn.sigmoid(pre_gate)
    return (pre_gate * sig, sig * (1.0 + pre_gate * (1.0 - sig)))


def send_slots(tokens, out_grad, flat_gate, slot_of, slot_cap):
    axis_width = lax.axis_size("expert")
    model_width = tokens.shape[1]
    entry_count = flat_gate.shape[0]
    route_count = entry_count // tokens.shape[0]
    slot_count = axis_width * slot_cap
    slot_hit = jnp.arange(slot_count, dtype=jnp.int32)[:, None] == slot_of[None, :]
    filled = jnp.any(slot_hit, axis=1)
    entry_lanes = jnp.arange(entry_count, dtype=jnp.int32)
    slot_entry = jnp.sum(jnp.where(slot_hit, entry_lanes[None, :], 0), axis=1)
    token_of = slot_entry // route_count
    zero_row = jnp.zeros((), jnp.bfloat16)
    send_rows = jnp.where(filled[:, None], tokens[token_of], zero_row)
    send_grads = jnp.where(filled[:, None], out_grad[token_of], zero_row)
    send_gate = jnp.where(filled, flat_gate[slot_entry], 0.0).astype(jnp.bfloat16)
    moved = [
        lax.all_to_all(
            part.reshape((axis_width, slot_cap) + part.shape[1:]),
            "expert",
            split_axis=0,
            concat_axis=0,
            tiled=True,
        )
        for part in (send_rows, send_grads, send_gate)
    ]
    rows = moved[0].reshape(slot_count, model_width)
    grads_in = moved[1].reshape(slot_count, model_width)
    gates = moved[2].reshape(slot_count).astype(jnp.float32)
    return rows, grads_in, gates


def xor_permute(value, mask):
    return lax.ppermute(value, "expert", [(i, i ^ mask) for i in range(lax.axis_size("expert"))])


def with_tile(column):
    lanes = jnp.arange(128, dtype=jnp.int32)[None, :] == 0
    return jnp.where(lanes, column.astype(jnp.bfloat16)[:, None], jnp.zeros((), jnp.bfloat16))


def entry_ranks(flat_ids, axis_width):
    id_onehot = (flat_ids[:, None] == jnp.arange(axis_width, dtype=jnp.int32)[None, :]).astype(
        jnp.int32
    )
    return jnp.sum((jnp.cumsum(id_onehot, axis=0) - id_onehot) * id_onehot, axis=1)


def on_device(
    tokens, out_grad, expert_ids, gate_probs, weights, first_moment, second_moment, moving_pairs
):
    axis_width = lax.axis_size("expert")
    half_axis = axis_width // 2
    swap_bit = half_axis.bit_length() - 1
    groups = lax.axis_size("dp")
    my_index = lax.axis_index("expert")
    tok_rows, route_count = expert_ids.shape
    model_width = tokens.shape[1]
    entry_count = tok_rows * route_count
    slot_cap = 5 * entry_count // (4 * axis_width)
    slot_count = axis_width * slot_cap
    pair_lanes = jnp.arange(half_axis, dtype=jnp.int32)
    my_move = jnp.sum(jnp.where(pair_lanes == my_index % half_axis, moving_pairs, 0))
    swapped = my_move == 1
    held = jnp.where(swapped, (my_index + half_axis) % axis_width, my_index)

    flat_gate = gate_probs.reshape(-1)
    flat_ids = expert_ids.reshape(-1)

    def holder_of(ids):
        lane_hit = (ids % half_axis)[:, None] == pair_lanes[None, :]
        moves = jnp.sum(jnp.where(lane_hit, moving_pairs[None, :], 0), axis=1)
        return jnp.where(moves == 1, (ids + half_axis) % axis_width, ids)

    two_stage = half_axis <= 8
    if two_stage:
        packed = jnp.concatenate([tokens, out_grad], axis=1)
        p_packed, p_ids, p_gate, their_weights = from_partner(
            (packed, expert_ids, gate_probs, weights), "expert", swap_bit
        )
        both = jnp.concatenate([packed, p_packed], axis=0)
        ids2 = jnp.concatenate([flat_ids, p_ids.reshape(-1)])
        gate2 = jnp.concatenate([flat_gate, p_gate.reshape(-1)])
        holder2 = holder_of(ids2)
        rank2 = jnp.concatenate(
            [entry_ranks(flat_ids, axis_width), entry_ranks(p_ids.reshape(-1), axis_width)]
        )
        src2 = jnp.arange(2 * entry_count, dtype=jnp.int32) // entry_count
        in_half = holder2 // half_axis == my_index // half_axis
        lane2 = holder2 % half_axis
        chunk = 2 * slot_cap
        slot2 = lane2 * chunk + src2 * slot_cap + rank2
        slot_hit = (
            jnp.arange(half_axis * chunk, dtype=jnp.int32)[:, None] == slot2[None, :]
        ) & in_half[None, :]
        tok_hit = jnp.any(slot_hit.reshape(half_axis * chunk, 2 * tok_rows, route_count), axis=2)
        tok_pick = tok_hit.astype(jnp.bfloat16)
        send_both = jnp.dot(tok_pick, both, preferred_element_type=jnp.float32).astype(
            jnp.bfloat16
        )
        wire2 = gate2.astype(jnp.bfloat16).astype(jnp.float32)
        send_gate = jnp.sum(jnp.where(slot_hit, wire2[None, :], 0.0), axis=1)
        send_all = jnp.concatenate([send_both, with_tile(send_gate)], axis=1)

        halves = [list(range(h * half_axis, (h + 1) * half_axis)) for h in range(2)]

        def spread(value):
            parts = value.reshape((half_axis, chunk) + value.shape[1:])
            moved = lax.all_to_all(
                parts, "expert", 0, 0, tiled=True, axis_index_groups=halves
            )
            return moved.reshape(value.shape)

        recv_all = spread(send_all)
        rows = recv_all[:, :model_width]
        grads_in = recv_all[:, model_width : 2 * model_width]
        gates = recv_all[:, 2 * model_width].astype(jnp.float32)
    else:
        slot_of = holder_of(flat_ids) * slot_cap + entry_ranks(flat_ids, axis_width)
        rows, grads_in, gates = send_slots(tokens, out_grad, flat_gate, slot_of, slot_cap)
    if not two_stage:
        their_weights = from_partner(weights, "expert", swap_bit)
    first_moment, second_moment, _ = lax.optimization_barrier(
        (first_moment, second_moment, their_weights)
    )
    if two_stage:
        pairs = [[p, p + half_axis] for p in range(half_axis)]
        pair_second = lax.all_gather(second_moment, "expert", axis_index_groups=pairs)
        their_second = jnp.where(my_index < half_axis, pair_second[1], pair_second[0])
        their_moments = (from_partner(first_moment, "expert", swap_bit), their_second)
    else:
        their_moments = from_partner((first_moment, second_moment), "expert", swap_bit)
    weights = jnp.where(swapped, their_weights, weights)
    if groups == 2:
        other = lax.ppermute(weights, "dp", [(0, 1), (1, 0)])
        first_half = lax.axis_index("dp") == 0
        whole = jnp.concatenate(
            [jnp.where(first_half, weights, other), jnp.where(first_half, other, weights)],
            axis=1,
        )[0]
    else:
        whole = lax.all_gather(weights, "dp", axis=1, tiled=True)[0]
    w_gate = whole[:, 0, :]
    w_up = whole[:, 1, :]
    w_down = whole[:, 2, :]
    w_both = jnp.concatenate([w_gate, w_up], axis=1)
    pre_gate = jnp.dot(rows, w_gate, preferred_element_type=jnp.float32)
    pre_up = jnp.dot(rows, w_up, preferred_element_type=jnp.float32)
    activated, act_slope = silu_parts(pre_gate)
    hidden = (activated * pre_up).astype(jnp.bfloat16)
    contract_hidden = (((1,), (1,)), ((), ()))
    projected = jnp.dot(grads_in, w_down, preferred_element_type=jnp.float32)
    gate_rows = jnp.sum(hidden.astype(jnp.float32) * projected, axis=1).astype(jnp.bfloat16)
    scaled_grad = (gates[:, None] * grads_in.astype(jnp.float32)).astype(jnp.bfloat16)
    hidden_grad = jnp.dot(scaled_grad, w_down, preferred_element_type=jnp.float32)
    gate_delta = (hidden_grad * pre_up * act_slope).astype(jnp.bfloat16)
    up_delta = (hidden_grad * activated).astype(jnp.bfloat16)
    both_delta = jnp.concatenate([gate_delta, up_delta], axis=1)
    row_grad = lax.dot_general(
        both_delta, w_both, contract_hidden, preferred_element_type=jnp.float32
    )
    row_grad = row_grad.astype(jnp.bfloat16)
    contract_rows = (((0,), (0,)), ((), ()))
    grad_gate = lax.dot_general(rows, gate_delta, contract_rows, preferred_element_type=jnp.float32)
    grad_up = lax.dot_general(rows, up_delta, contract_rows, preferred_element_type=jnp.float32)
    grad_down = lax.dot_general(
        scaled_grad, hidden, contract_rows, preferred_element_type=jnp.float32
    )
    part = jnp.stack([grad_gate, grad_up, grad_down], axis=1).astype(jnp.bfloat16)
    if groups == 2:
        row_half = part.shape[0] // 2
        first_half = lax.axis_index("dp") == 0
        keep = jnp.where(first_half, part[:row_half], part[row_half:])
        give = jnp.where(first_half, part[row_half:], part[:row_half])
        got = lax.ppermute(give, "dp", [(0, 1), (1, 0)])
        grad = (keep.astype(jnp.float32) + got.astype(jnp.float32)) * (1.0 / groups)
    else:
        grad = lax.psum_scatter(
            part, "dp", scatter_dimension=0, tiled=True
        ).astype(jnp.float32) * (1.0 / groups)
    grad = grad[None]
    first_moment = jnp.where(swapped, their_moments[0], first_moment)
    second_moment = jnp.where(swapped, their_moments[1], second_moment)
    new_first = (0.9 * first_moment.astype(jnp.float32) + 0.1 * grad).astype(jnp.bfloat16)
    new_second = (0.95 * second_moment.astype(jnp.float32) + 0.05 * grad * grad).astype(
        jnp.bfloat16
    )

    if two_stage:
        back_all = spread(jnp.concatenate([row_grad, with_tile(gate_rows)], axis=1))
        back_rows = back_all[:, :model_width]
        back_gate = back_all[:, model_width].astype(jnp.float32)
        weight_of = jnp.where(slot_hit, gate2[None, :], 0.0)
        weight_of = jnp.sum(weight_of.reshape(half_axis * chunk, 2 * tok_rows, route_count), axis=2)
        partial = lax.dot_general(
            weight_of,
            back_rows.astype(jnp.float32),
            (((0,), (0,)), ((), ())),
            precision=lax.Precision.HIGHEST,
            preferred_element_type=jnp.float32,
        )
        prob2 = jnp.sum(jnp.where(slot_hit, back_gate[:, None], 0.0), axis=0)
        p_partial, p_prob = from_partner(
            (partial[tok_rows:].astype(jnp.bfloat16), prob2[entry_count:].astype(jnp.bfloat16)),
            "expert",
            swap_bit,
        )
        token_grad = (partial[:tok_rows] + p_partial.astype(jnp.float32)).astype(jnp.bfloat16)
        prob_grad = jnp.where(
            in_half[:entry_count], prob2[:entry_count], p_prob.astype(jnp.float32)
        )
        prob_grad = prob_grad.astype(jnp.bfloat16).reshape(tok_rows, route_count)
    else:
        back_rows, back_gate = [
            lax.all_to_all(
                part.reshape((axis_width, slot_cap) + part.shape[1:]),
                "expert",
                split_axis=0,
                concat_axis=0,
                tiled=True,
            )
            for part in (row_grad, gate_rows)
        ]
        gathered = back_rows.reshape(slot_count, model_width)[slot_of].astype(jnp.float32)
        token_grad = (
            (gathered * flat_gate[:, None])
            .reshape(tok_rows, route_count, model_width)
            .sum(axis=1)
            .astype(jnp.bfloat16)
        )
        prob_grad = back_gate.reshape(slot_count)[slot_of].reshape(tok_rows, route_count)
    return (token_grad, prob_grad, weights, grad, new_first, new_second)


def solution(mesh):
    in_specs = (
        P(("dp", "expert"), None),
        P(("dp", "expert"), None),
        P(("dp", "expert"), None),
        P(("dp", "expert"), None),
        P("expert", "dp", None, None),
        P("expert", "dp", None, None),
        P("expert", "dp", None, None),
        P(),
    )
    out_specs = (
        P(("dp", "expert"), None),
        P(("dp", "expert"), None),
        P("expert", "dp", None, None),
        P("expert", "dp", None, None),
        P("expert", "dp", None, None),
        P("expert", "dp", None, None),
    )
    return jax.shard_map(
        on_device, mesh=mesh, in_specs=in_specs, out_specs=out_specs, check_vma=False
    )
```

```python
import jax
import jax.numpy as jnp
from jax import lax
from jax.sharding import PartitionSpec as P


def from_partner(value, axis, bit):
    return lax.ppermute(value, axis, [(i, i ^ 1 << bit) for i in range(lax.axis_size(axis))])


def silu_parts(pre_gate):
    sig = jax.nn.sigmoid(pre_gate)
    return (pre_gate * sig, sig * (1.0 + pre_gate * (1.0 - sig)))


def send_slots(tokens, out_grad, flat_gate, slot_of, slot_cap):
    axis_width = lax.axis_size("expert")
    model_width = tokens.shape[1]
    entry_count = flat_gate.shape[0]
    route_count = entry_count // tokens.shape[0]
    slot_count = axis_width * slot_cap
    slot_hit = jnp.arange(slot_count, dtype=jnp.int32)[:, None] == slot_of[None, :]
    filled = jnp.any(slot_hit, axis=1)
    entry_lanes = jnp.arange(entry_count, dtype=jnp.int32)
    slot_entry = jnp.sum(jnp.where(slot_hit, entry_lanes[None, :], 0), axis=1)
    token_of = slot_entry // route_count
    zero_row = jnp.zeros((), jnp.bfloat16)
    send_rows = jnp.where(filled[:, None], tokens[token_of], zero_row)
    send_grads = jnp.where(filled[:, None], out_grad[token_of], zero_row)
    send_gate = jnp.where(filled, flat_gate[slot_entry], 0.0).astype(jnp.bfloat16)
    moved = [
        lax.all_to_all(
            part.reshape((axis_width, slot_cap) + part.shape[1:]),
            "expert",
            split_axis=0,
            concat_axis=0,
            tiled=True,
        )
        for part in (send_rows, send_grads, send_gate)
    ]
    rows = moved[0].reshape(slot_count, model_width)
    grads_in = moved[1].reshape(slot_count, model_width)
    gates = moved[2].reshape(slot_count).astype(jnp.float32)
    return rows, grads_in, gates


def xor_permute(value, mask):
    return lax.ppermute(value, "expert", [(i, i ^ mask) for i in range(lax.axis_size("expert"))])


def with_tile(column):
    lanes = jnp.arange(128, dtype=jnp.int32)[None, :] == 0
    return jnp.where(lanes, column.astype(jnp.bfloat16)[:, None], jnp.zeros((), jnp.bfloat16))


def entry_ranks(flat_ids, axis_width):
    id_onehot = (flat_ids[:, None] == jnp.arange(axis_width, dtype=jnp.int32)[None, :]).astype(
        jnp.int32
    )
    return jnp.sum((jnp.cumsum(id_onehot, axis=0) - id_onehot) * id_onehot, axis=1)


def on_device(
    tokens, out_grad, expert_ids, gate_probs, weights, first_moment, second_moment, moving_pairs
):
    axis_width = lax.axis_size("expert")
    half_axis = axis_width // 2
    swap_bit = half_axis.bit_length() - 1
    groups = lax.axis_size("dp")
    my_index = lax.axis_index("expert")
    tok_rows, route_count = expert_ids.shape
    model_width = tokens.shape[1]
    entry_count = tok_rows * route_count
    slot_cap = 5 * entry_count // (4 * axis_width)
    slot_count = axis_width * slot_cap
    pair_lanes = jnp.arange(half_axis, dtype=jnp.int32)
    my_move = jnp.sum(jnp.where(pair_lanes == my_index % half_axis, moving_pairs, 0))
    swapped = my_move == 1
    held = jnp.where(swapped, (my_index + half_axis) % axis_width, my_index)

    flat_gate = gate_probs.reshape(-1)
    flat_ids = expert_ids.reshape(-1)

    def holder_of(ids):
        lane_hit = (ids % half_axis)[:, None] == pair_lanes[None, :]
        moves = jnp.sum(jnp.where(lane_hit, moving_pairs[None, :], 0), axis=1)
        return jnp.where(moves == 1, (ids + half_axis) % axis_width, ids)

    two_stage = half_axis <= 8
    if two_stage:
        packed = jnp.concatenate([tokens, out_grad], axis=1)
        p_packed, p_ids, p_gate, their_weights = from_partner(
            (packed, expert_ids, gate_probs, weights), "expert", swap_bit
        )
        both = jnp.concatenate([packed, p_packed], axis=0)
        ids2 = jnp.concatenate([flat_ids, p_ids.reshape(-1)])
        gate2 = jnp.concatenate([flat_gate, p_gate.reshape(-1)])
        holder2 = holder_of(ids2)
        rank2 = jnp.concatenate(
            [entry_ranks(flat_ids, axis_width), entry_ranks(p_ids.reshape(-1), axis_width)]
        )
        src2 = jnp.arange(2 * entry_count, dtype=jnp.int32) // entry_count
        in_half = holder2 // half_axis == my_index // half_axis
        lane2 = holder2 % half_axis
        chunk = 2 * slot_cap
        slot2 = lane2 * chunk + src2 * slot_cap + rank2
        slot_hit = (
            jnp.arange(half_axis * chunk, dtype=jnp.int32)[:, None] == slot2[None, :]
        ) & in_half[None, :]
        tok_hit = jnp.any(slot_hit.reshape(half_axis * chunk, 2 * tok_rows, route_count), axis=2)
        tok_pick = tok_hit.astype(jnp.bfloat16)
        send_both = jnp.dot(tok_pick, both, preferred_element_type=jnp.float32).astype(
            jnp.bfloat16
        )
        wire2 = gate2.astype(jnp.bfloat16).astype(jnp.float32)
        send_gate = jnp.sum(jnp.where(slot_hit, wire2[None, :], 0.0), axis=1)
        send_all = jnp.concatenate([send_both, with_tile(send_gate)], axis=1)

        halves = [list(range(h * half_axis, (h + 1) * half_axis)) for h in range(2)]

        def spread(value):
            parts = value.reshape((half_axis, chunk) + value.shape[1:])
            moved = lax.all_to_all(
                parts, "expert", 0, 0, tiled=True, axis_index_groups=halves
            )
            return moved.reshape(value.shape)

        recv_all = spread(send_all)
        rows = recv_all[:, :model_width]
        grads_in = recv_all[:, model_width : 2 * model_width]
        gates = recv_all[:, 2 * model_width].astype(jnp.float32)
    else:
        slot_of = holder_of(flat_ids) * slot_cap + entry_ranks(flat_ids, axis_width)
        rows, grads_in, gates = send_slots(tokens, out_grad, flat_gate, slot_of, slot_cap)
    if not two_stage:
        their_weights = from_partner(weights, "expert", swap_bit)
    first_moment, second_moment, _ = lax.optimization_barrier(
        (first_moment, second_moment, their_weights)
    )
    their_moments = from_partner((first_moment, second_moment), "expert", swap_bit)
    weights = jnp.where(swapped, their_weights, weights)
    if groups == 2:
        other = lax.ppermute(weights, "dp", [(0, 1), (1, 0)])
        first_half = lax.axis_index("dp") == 0
        whole = jnp.concatenate(
            [jnp.where(first_half, weights, other), jnp.where(first_half, other, weights)],
            axis=1,
        )[0]
    else:
        whole = lax.all_gather(weights, "dp", axis=1, tiled=True)[0]
    w_gate = whole[:, 0, :]
    w_up = whole[:, 1, :]
    w_down = whole[:, 2, :]
    w_both = jnp.concatenate([w_gate, w_up], axis=1)
    pre_gate = jnp.dot(rows, w_gate, preferred_element_type=jnp.float32)
    pre_up = jnp.dot(rows, w_up, preferred_element_type=jnp.float32)
    activated, act_slope = silu_parts(pre_gate)
    hidden = (activated * pre_up).astype(jnp.bfloat16)
    contract_hidden = (((1,), (1,)), ((), ()))
    projected = jnp.dot(grads_in, w_down, preferred_element_type=jnp.float32)
    gate_rows = jnp.sum(hidden.astype(jnp.float32) * projected, axis=1).astype(jnp.bfloat16)
    scaled_grad = (gates[:, None] * grads_in.astype(jnp.float32)).astype(jnp.bfloat16)
    hidden_grad = jnp.dot(scaled_grad, w_down, preferred_element_type=jnp.float32)
    gate_delta = (hidden_grad * pre_up * act_slope).astype(jnp.bfloat16)
    up_delta = (hidden_grad * activated).astype(jnp.bfloat16)
    both_delta = jnp.concatenate([gate_delta, up_delta], axis=1)
    row_grad = lax.dot_general(
        both_delta, w_both, contract_hidden, preferred_element_type=jnp.float32
    )
    row_grad = row_grad.astype(jnp.bfloat16)
    contract_rows = (((0,), (0,)), ((), ()))
    grad_gate = lax.dot_general(rows, gate_delta, contract_rows, preferred_element_type=jnp.float32)
    grad_up = lax.dot_general(rows, up_delta, contract_rows, preferred_element_type=jnp.float32)
    grad_down = lax.dot_general(
        scaled_grad, hidden, contract_rows, preferred_element_type=jnp.float32
    )
    part = jnp.stack([grad_gate, grad_up, grad_down], axis=1).astype(jnp.bfloat16)
    if groups == 2:
        row_half = part.shape[0] // 2
        first_half = lax.axis_index("dp") == 0
        keep = jnp.where(first_half, part[:row_half], part[row_half:])
        give = jnp.where(first_half, part[row_half:], part[:row_half])
        got = lax.ppermute(give, "dp", [(0, 1), (1, 0)])
        grad = (keep.astype(jnp.float32) + got.astype(jnp.float32)) * (1.0 / groups)
    else:
        grad = lax.psum_scatter(
            part, "dp", scatter_dimension=0, tiled=True
        ).astype(jnp.float32) * (1.0 / groups)
    grad = grad[None]

    if two_stage:
        back_in = jnp.concatenate([row_grad, with_tile(gate_rows)], axis=1)
        back_in, their_moments = lax.optimization_barrier((back_in, their_moments))
        back_all = spread(back_in)
        back_rows = back_all[:, :model_width]
        back_gate = back_all[:, model_width].astype(jnp.float32)
        weight_of = jnp.where(slot_hit, gate2[None, :], 0.0)
        weight_of = jnp.sum(weight_of.reshape(half_axis * chunk, 2 * tok_rows, route_count), axis=2)
        partial = lax.dot_general(
            weight_of,
            back_rows.astype(jnp.float32),
            (((0,), (0,)), ((), ())),
            precision=lax.Precision.HIGHEST,
            preferred_element_type=jnp.float32,
        )
        prob2 = jnp.sum(jnp.where(slot_hit, back_gate[:, None], 0.0), axis=0)
        p_partial, p_prob = from_partner(
            (partial[tok_rows:].astype(jnp.bfloat16), prob2[entry_count:].astype(jnp.bfloat16)),
            "expert",
            swap_bit,
        )
        token_grad = (partial[:tok_rows] + p_partial.astype(jnp.float32)).astype(jnp.bfloat16)
        prob_grad = jnp.where(
            in_half[:entry_count], prob2[:entry_count], p_prob.astype(jnp.float32)
        )
        prob_grad = prob_grad.astype(jnp.bfloat16).reshape(tok_rows, route_count)
    else:
        back_rows, back_gate = [
            lax.all_to_all(
                part.reshape((axis_width, slot_cap) + part.shape[1:]),
                "expert",
                split_axis=0,
                concat_axis=0,
                tiled=True,
            )
            for part in (row_grad, gate_rows)
        ]
        gathered = back_rows.reshape(slot_count, model_width)[slot_of].astype(jnp.float32)
        token_grad = (
            (gathered * flat_gate[:, None])
            .reshape(tok_rows, route_count, model_width)
            .sum(axis=1)
            .astype(jnp.bfloat16)
        )
        prob_grad = back_gate.reshape(slot_count)[slot_of].reshape(tok_rows, route_count)
    first_moment = jnp.where(swapped, their_moments[0], first_moment)
    second_moment = jnp.where(swapped, their_moments[1], second_moment)
    new_first = (0.9 * first_moment.astype(jnp.float32) + 0.1 * grad).astype(jnp.bfloat16)
    new_second = (0.95 * second_moment.astype(jnp.float32) + 0.05 * grad * grad).astype(
        jnp.bfloat16
    )
    return (token_grad, prob_grad, weights, grad, new_first, new_second)


def solution(mesh):
    in_specs = (
        P(("dp", "expert"), None),
        P(("dp", "expert"), None),
        P(("dp", "expert"), None),
        P(("dp", "expert"), None),
        P("expert", "dp", None, None),
        P("expert", "dp", None, None),
        P("expert", "dp", None, None),
        P(),
    )
    out_specs = (
        P(("dp", "expert"), None),
        P(("dp", "expert"), None),
        P("expert", "dp", None, None),
        P("expert", "dp", None, None),
        P("expert", "dp", None, None),
        P("expert", "dp", None, None),
    )
    return jax.shard_map(
        on_device, mesh=mesh, in_specs=in_specs, out_specs=out_specs, check_vma=False
    )
```

```python
import jax
import jax.numpy as jnp
from jax import lax
from jax.sharding import PartitionSpec as P


def from_partner(value, axis, bit):
    return lax.ppermute(value, axis, [(i, i ^ 1 << bit) for i in range(lax.axis_size(axis))])


def silu_parts(pre_gate):
    sig = jax.nn.sigmoid(pre_gate)
    return (pre_gate * sig, sig * (1.0 + pre_gate * (1.0 - sig)))


def send_slots(tokens, out_grad, flat_gate, slot_of, slot_cap):
    axis_width = lax.axis_size("expert")
    model_width = tokens.shape[1]
    entry_count = flat_gate.shape[0]
    route_count = entry_count // tokens.shape[0]
    slot_count = axis_width * slot_cap
    slot_hit = jnp.arange(slot_count, dtype=jnp.int32)[:, None] == slot_of[None, :]
    filled = jnp.any(slot_hit, axis=1)
    entry_lanes = jnp.arange(entry_count, dtype=jnp.int32)
    slot_entry = jnp.sum(jnp.where(slot_hit, entry_lanes[None, :], 0), axis=1)
    token_of = slot_entry // route_count
    zero_row = jnp.zeros((), jnp.bfloat16)
    send_rows = jnp.where(filled[:, None], tokens[token_of], zero_row)
    send_grads = jnp.where(filled[:, None], out_grad[token_of], zero_row)
    send_gate = jnp.where(filled, flat_gate[slot_entry], 0.0).astype(jnp.bfloat16)
    moved = [
        lax.all_to_all(
            part.reshape((axis_width, slot_cap) + part.shape[1:]),
            "expert",
            split_axis=0,
            concat_axis=0,
            tiled=True,
        )
        for part in (send_rows, send_grads, send_gate)
    ]
    rows = moved[0].reshape(slot_count, model_width)
    grads_in = moved[1].reshape(slot_count, model_width)
    gates = moved[2].reshape(slot_count).astype(jnp.float32)
    return rows, grads_in, gates


def xor_permute(value, mask):
    return lax.ppermute(value, "expert", [(i, i ^ mask) for i in range(lax.axis_size("expert"))])


def with_tile(column):
    lanes = jnp.arange(128, dtype=jnp.int32)[None, :] == 0
    return jnp.where(lanes, column.astype(jnp.bfloat16)[:, None], jnp.zeros((), jnp.bfloat16))


def entry_ranks(flat_ids, axis_width):
    id_onehot = (flat_ids[:, None] == jnp.arange(axis_width, dtype=jnp.int32)[None, :]).astype(
        jnp.int32
    )
    return jnp.sum((jnp.cumsum(id_onehot, axis=0) - id_onehot) * id_onehot, axis=1)


def on_device(
    tokens, out_grad, expert_ids, gate_probs, weights, first_moment, second_moment, moving_pairs
):
    axis_width = lax.axis_size("expert")
    half_axis = axis_width // 2
    swap_bit = half_axis.bit_length() - 1
    groups = lax.axis_size("dp")
    my_index = lax.axis_index("expert")
    tok_rows, route_count = expert_ids.shape
    model_width = tokens.shape[1]
    entry_count = tok_rows * route_count
    slot_cap = 5 * entry_count // (4 * axis_width)
    slot_count = axis_width * slot_cap
    pair_lanes = jnp.arange(half_axis, dtype=jnp.int32)
    my_move = jnp.sum(jnp.where(pair_lanes == my_index % half_axis, moving_pairs, 0))
    swapped = my_move == 1
    held = jnp.where(swapped, (my_index + half_axis) % axis_width, my_index)

    flat_gate = gate_probs.reshape(-1)
    flat_ids = expert_ids.reshape(-1)

    def holder_of(ids):
        lane_hit = (ids % half_axis)[:, None] == pair_lanes[None, :]
        moves = jnp.sum(jnp.where(lane_hit, moving_pairs[None, :], 0), axis=1)
        return jnp.where(moves == 1, (ids + half_axis) % axis_width, ids)

    two_stage = half_axis <= 8
    if two_stage:
        packed = jnp.concatenate([tokens, out_grad], axis=1)
        p_packed, p_ids, p_gate, their_weights = from_partner(
            (packed, expert_ids, gate_probs, weights), "expert", swap_bit
        )
        both = jnp.concatenate([packed, p_packed], axis=0)
        ids2 = jnp.concatenate([flat_ids, p_ids.reshape(-1)])
        gate2 = jnp.concatenate([flat_gate, p_gate.reshape(-1)])
        holder2 = holder_of(ids2)
        rank2 = jnp.concatenate(
            [entry_ranks(flat_ids, axis_width), entry_ranks(p_ids.reshape(-1), axis_width)]
        )
        src2 = jnp.arange(2 * entry_count, dtype=jnp.int32) // entry_count
        in_half = holder2 // half_axis == my_index // half_axis
        lane2 = holder2 % half_axis
        chunk = 2 * slot_cap
        slot2 = lane2 * chunk + src2 * slot_cap + rank2
        slot_hit = (
            jnp.arange(half_axis * chunk, dtype=jnp.int32)[:, None] == slot2[None, :]
        ) & in_half[None, :]
        tok_hit = jnp.any(slot_hit.reshape(half_axis * chunk, 2 * tok_rows, route_count), axis=2)
        tok_pick = tok_hit.astype(jnp.bfloat16)
        send_both = jnp.dot(tok_pick, both, preferred_element_type=jnp.float32).astype(
            jnp.bfloat16
        )
        wire2 = gate2.astype(jnp.bfloat16).astype(jnp.float32)
        send_gate = jnp.sum(jnp.where(slot_hit, wire2[None, :], 0.0), axis=1)
        send_all = jnp.concatenate([send_both, with_tile(send_gate)], axis=1)

        halves = [list(range(h * half_axis, (h + 1) * half_axis)) for h in range(2)]

        def spread(value):
            parts = value.reshape((half_axis, chunk) + value.shape[1:])
            moved = lax.all_to_all(
                parts, "expert", 0, 0, tiled=True, axis_index_groups=halves
            )
            return moved.reshape(value.shape)

        recv_all = spread(send_all)
        rows = recv_all[:, :model_width]
        grads_in = recv_all[:, model_width : 2 * model_width]
        gates = recv_all[:, 2 * model_width].astype(jnp.float32)
    else:
        slot_of = holder_of(flat_ids) * slot_cap + entry_ranks(flat_ids, axis_width)
        rows, grads_in, gates = send_slots(tokens, out_grad, flat_gate, slot_of, slot_cap)
    if not two_stage:
        their_weights = from_partner(weights, "expert", swap_bit)
    first_moment, second_moment, _ = lax.optimization_barrier(
        (first_moment, second_moment, their_weights)
    )
    their_moments = from_partner((first_moment, second_moment), "expert", swap_bit)
    weights = jnp.where(swapped, their_weights, weights)
    if groups == 2:
        other = lax.ppermute(weights, "dp", [(0, 1), (1, 0)])
        first_half = lax.axis_index("dp") == 0
        whole = jnp.concatenate(
            [jnp.where(first_half, weights, other), jnp.where(first_half, other, weights)],
            axis=1,
        )[0]
    else:
        whole = lax.all_gather(weights, "dp", axis=1, tiled=True)[0]
    w_gate = whole[:, 0, :]
    w_up = whole[:, 1, :]
    w_down = whole[:, 2, :]
    w_both = jnp.concatenate([w_gate, w_up], axis=1)
    pre_gate = jnp.dot(rows, w_gate, preferred_element_type=jnp.float32)
    pre_up = jnp.dot(rows, w_up, preferred_element_type=jnp.float32)
    activated, act_slope = silu_parts(pre_gate)
    hidden = (activated * pre_up).astype(jnp.bfloat16)
    contract_hidden = (((1,), (1,)), ((), ()))
    projected = jnp.dot(grads_in, w_down, preferred_element_type=jnp.float32)
    gate_rows = jnp.sum(hidden.astype(jnp.float32) * projected, axis=1).astype(jnp.bfloat16)
    scaled_grad = (gates[:, None] * grads_in.astype(jnp.float32)).astype(jnp.bfloat16)
    hidden_grad = jnp.dot(scaled_grad, w_down, preferred_element_type=jnp.float32)
    gate_delta = (hidden_grad * pre_up * act_slope).astype(jnp.bfloat16)
    up_delta = (hidden_grad * activated).astype(jnp.bfloat16)
    both_delta = jnp.concatenate([gate_delta, up_delta], axis=1)
    row_grad = lax.dot_general(
        both_delta, w_both, contract_hidden, preferred_element_type=jnp.float32
    )
    row_grad = row_grad.astype(jnp.bfloat16)
    contract_rows = (((0,), (0,)), ((), ()))
    grad_gate = lax.dot_general(rows, gate_delta, contract_rows, preferred_element_type=jnp.float32)
    grad_up = lax.dot_general(rows, up_delta, contract_rows, preferred_element_type=jnp.float32)
    grad_down = lax.dot_general(
        scaled_grad, hidden, contract_rows, preferred_element_type=jnp.float32
    )
    part = jnp.stack([grad_gate, grad_up, grad_down], axis=1).astype(jnp.bfloat16)
    if groups == 2:
        row_half = part.shape[0] // 2
        first_half = lax.axis_index("dp") == 0
        keep = jnp.where(first_half, part[:row_half], part[row_half:])
        give = jnp.where(first_half, part[row_half:], part[:row_half])
        got = lax.ppermute(give, "dp", [(0, 1), (1, 0)])
        grad = (keep.astype(jnp.float32) + got.astype(jnp.float32)) * (1.0 / groups)
    else:
        grad = lax.psum_scatter(
            part, "dp", scatter_dimension=0, tiled=True
        ).astype(jnp.float32) * (1.0 / groups)
    grad = grad[None]
    first_moment = jnp.where(swapped, their_moments[0], first_moment)
    second_moment = jnp.where(swapped, their_moments[1], second_moment)
    new_first = (0.9 * first_moment.astype(jnp.float32) + 0.1 * grad).astype(jnp.bfloat16)
    new_second = (0.95 * second_moment.astype(jnp.float32) + 0.05 * grad * grad).astype(
        jnp.bfloat16
    )

    if two_stage:
        back_all = spread(jnp.concatenate([row_grad, with_tile(gate_rows)], axis=1))
        back_rows = back_all[:, :model_width]
        back_gate = back_all[:, model_width].astype(jnp.float32)
        weight_of = jnp.where(slot_hit, gate2[None, :], 0.0)
        weight_of = jnp.sum(weight_of.reshape(half_axis * chunk, 2 * tok_rows, route_count), axis=2)
        partial = lax.dot_general(
            weight_of,
            back_rows.astype(jnp.float32),
            (((0,), (0,)), ((), ())),
            precision=lax.Precision.HIGHEST,
            preferred_element_type=jnp.float32,
        )
        prob2 = jnp.sum(jnp.where(slot_hit, back_gate[:, None], 0.0), axis=0)
        prob_tile = jnp.concatenate(
            [
                prob2[entry_count:].reshape(tok_rows, route_count),
                jnp.zeros((tok_rows, 128 - route_count), jnp.float32),
            ],
            axis=1,
        )
        p_back = from_partner(
            jnp.concatenate([partial[tok_rows:], prob_tile], axis=1).astype(jnp.bfloat16),
            "expert",
            swap_bit,
        )
        p_partial = p_back[:, :model_width]
        p_prob = p_back[:, model_width : model_width + route_count].reshape(-1)
        token_grad = (partial[:tok_rows] + p_partial.astype(jnp.float32)).astype(jnp.bfloat16)
        prob_grad = jnp.where(
            in_half[:entry_count], prob2[:entry_count], p_prob.astype(jnp.float32)
        )
        prob_grad = prob_grad.astype(jnp.bfloat16).reshape(tok_rows, route_count)
    else:
        back_rows, back_gate = [
            lax.all_to_all(
                part.reshape((axis_width, slot_cap) + part.shape[1:]),
                "expert",
                split_axis=0,
                concat_axis=0,
                tiled=True,
            )
            for part in (row_grad, gate_rows)
        ]
        gathered = back_rows.reshape(slot_count, model_width)[slot_of].astype(jnp.float32)
        token_grad = (
            (gathered * flat_gate[:, None])
            .reshape(tok_rows, route_count, model_width)
            .sum(axis=1)
            .astype(jnp.bfloat16)
        )
        prob_grad = back_gate.reshape(slot_count)[slot_of].reshape(tok_rows, route_count)
    return (token_grad, prob_grad, weights, grad, new_first, new_second)


def solution(mesh):
    in_specs = (
        P(("dp", "expert"), None),
        P(("dp", "expert"), None),
        P(("dp", "expert"), None),
        P(("dp", "expert"), None),
        P("expert", "dp", None, None),
        P("expert", "dp", None, None),
        P("expert", "dp", None, None),
        P(),
    )
    out_specs = (
        P(("dp", "expert"), None),
        P(("dp", "expert"), None),
        P("expert", "dp", None, None),
        P("expert", "dp", None, None),
        P("expert", "dp", None, None),
        P("expert", "dp", None, None),
    )
    return jax.shard_map(
        on_device, mesh=mesh, in_specs=in_specs, out_specs=out_specs, check_vma=False
    )
```

```python
import jax
import jax.numpy as jnp
from jax import lax
from jax.sharding import PartitionSpec as P


def from_partner(value, axis, bit):
    return lax.ppermute(value, axis, [(i, i ^ 1 << bit) for i in range(lax.axis_size(axis))])


def silu_parts(pre_gate):
    sig = jax.nn.sigmoid(pre_gate)
    return (pre_gate * sig, sig * (1.0 + pre_gate * (1.0 - sig)))


def send_slots(tokens, out_grad, flat_gate, slot_of, slot_cap):
    axis_width = lax.axis_size("expert")
    model_width = tokens.shape[1]
    entry_count = flat_gate.shape[0]
    route_count = entry_count // tokens.shape[0]
    slot_count = axis_width * slot_cap
    slot_hit = jnp.arange(slot_count, dtype=jnp.int32)[:, None] == slot_of[None, :]
    filled = jnp.any(slot_hit, axis=1)
    entry_lanes = jnp.arange(entry_count, dtype=jnp.int32)
    slot_entry = jnp.sum(jnp.where(slot_hit, entry_lanes[None, :], 0), axis=1)
    token_of = slot_entry // route_count
    zero_row = jnp.zeros((), jnp.bfloat16)
    send_rows = jnp.where(filled[:, None], tokens[token_of], zero_row)
    send_grads = jnp.where(filled[:, None], out_grad[token_of], zero_row)
    send_gate = jnp.where(filled, flat_gate[slot_entry], 0.0).astype(jnp.bfloat16)
    moved = [
        lax.all_to_all(
            part.reshape((axis_width, slot_cap) + part.shape[1:]),
            "expert",
            split_axis=0,
            concat_axis=0,
            tiled=True,
        )
        for part in (send_rows, send_grads, send_gate)
    ]
    rows = moved[0].reshape(slot_count, model_width)
    grads_in = moved[1].reshape(slot_count, model_width)
    gates = moved[2].reshape(slot_count).astype(jnp.float32)
    return rows, grads_in, gates


def xor_permute(value, mask):
    return lax.ppermute(value, "expert", [(i, i ^ mask) for i in range(lax.axis_size("expert"))])


def with_tile(column):
    lanes = jnp.arange(128, dtype=jnp.int32)[None, :] == 0
    return jnp.where(lanes, column.astype(jnp.bfloat16)[:, None], jnp.zeros((), jnp.bfloat16))


def entry_ranks(flat_ids, axis_width):
    id_onehot = (flat_ids[:, None] == jnp.arange(axis_width, dtype=jnp.int32)[None, :]).astype(
        jnp.int32
    )
    return jnp.sum((jnp.cumsum(id_onehot, axis=0) - id_onehot) * id_onehot, axis=1)


def on_device(
    tokens, out_grad, expert_ids, gate_probs, weights, first_moment, second_moment, moving_pairs
):
    axis_width = lax.axis_size("expert")
    half_axis = axis_width // 2
    swap_bit = half_axis.bit_length() - 1
    groups = lax.axis_size("dp")
    my_index = lax.axis_index("expert")
    tok_rows, route_count = expert_ids.shape
    model_width = tokens.shape[1]
    entry_count = tok_rows * route_count
    slot_cap = 5 * entry_count // (4 * axis_width)
    slot_count = axis_width * slot_cap
    pair_lanes = jnp.arange(half_axis, dtype=jnp.int32)
    my_move = jnp.sum(jnp.where(pair_lanes == my_index % half_axis, moving_pairs, 0))
    swapped = my_move == 1
    held = jnp.where(swapped, (my_index + half_axis) % axis_width, my_index)

    flat_gate = gate_probs.reshape(-1)
    flat_ids = expert_ids.reshape(-1)

    def holder_of(ids):
        lane_hit = (ids % half_axis)[:, None] == pair_lanes[None, :]
        moves = jnp.sum(jnp.where(lane_hit, moving_pairs[None, :], 0), axis=1)
        return jnp.where(moves == 1, (ids + half_axis) % axis_width, ids)

    two_stage = half_axis <= 8
    if two_stage:
        packed = jnp.concatenate([tokens, out_grad], axis=1)
        small = jnp.concatenate([expert_ids.astype(jnp.float32), gate_probs], axis=1)
        p_packed, p_small, their_weights = from_partner(
            (packed, small, weights), "expert", swap_bit
        )
        p_ids = p_small[:, :route_count].astype(jnp.int32)
        p_gate = p_small[:, route_count:]
        both = jnp.concatenate([packed, p_packed], axis=0)
        ids2 = jnp.concatenate([flat_ids, p_ids.reshape(-1)])
        gate2 = jnp.concatenate([flat_gate, p_gate.reshape(-1)])
        holder2 = holder_of(ids2)
        rank2 = jnp.concatenate(
            [entry_ranks(flat_ids, axis_width), entry_ranks(p_ids.reshape(-1), axis_width)]
        )
        src2 = jnp.arange(2 * entry_count, dtype=jnp.int32) // entry_count
        in_half = holder2 // half_axis == my_index // half_axis
        lane2 = holder2 % half_axis
        chunk = 2 * slot_cap
        slot2 = lane2 * chunk + src2 * slot_cap + rank2
        slot_hit = (
            jnp.arange(half_axis * chunk, dtype=jnp.int32)[:, None] == slot2[None, :]
        ) & in_half[None, :]
        tok_hit = jnp.any(slot_hit.reshape(half_axis * chunk, 2 * tok_rows, route_count), axis=2)
        tok_pick = tok_hit.astype(jnp.bfloat16)
        send_both = jnp.dot(tok_pick, both, preferred_element_type=jnp.float32).astype(
            jnp.bfloat16
        )
        wire2 = gate2.astype(jnp.bfloat16).astype(jnp.float32)
        send_gate = jnp.sum(jnp.where(slot_hit, wire2[None, :], 0.0), axis=1)
        send_all = jnp.concatenate([send_both, with_tile(send_gate)], axis=1)

        halves = [list(range(h * half_axis, (h + 1) * half_axis)) for h in range(2)]

        def spread(value):
            parts = value.reshape((half_axis, chunk) + value.shape[1:])
            moved = lax.all_to_all(
                parts, "expert", 0, 0, tiled=True, axis_index_groups=halves
            )
            return moved.reshape(value.shape)

        recv_all = spread(send_all)
        rows = recv_all[:, :model_width]
        grads_in = recv_all[:, model_width : 2 * model_width]
        gates = recv_all[:, 2 * model_width].astype(jnp.float32)
    else:
        slot_of = holder_of(flat_ids) * slot_cap + entry_ranks(flat_ids, axis_width)
        rows, grads_in, gates = send_slots(tokens, out_grad, flat_gate, slot_of, slot_cap)
    if not two_stage:
        their_weights = from_partner(weights, "expert", swap_bit)
    first_moment, second_moment, _ = lax.optimization_barrier(
        (first_moment, second_moment, their_weights)
    )
    their_moments = from_partner((first_moment, second_moment), "expert", swap_bit)
    weights = jnp.where(swapped, their_weights, weights)
    if groups == 2:
        other = lax.ppermute(weights, "dp", [(0, 1), (1, 0)])
        first_half = lax.axis_index("dp") == 0
        whole = jnp.concatenate(
            [jnp.where(first_half, weights, other), jnp.where(first_half, other, weights)],
            axis=1,
        )[0]
    else:
        whole = lax.all_gather(weights, "dp", axis=1, tiled=True)[0]
    w_gate = whole[:, 0, :]
    w_up = whole[:, 1, :]
    w_down = whole[:, 2, :]
    w_both = jnp.concatenate([w_gate, w_up], axis=1)
    pre_gate = jnp.dot(rows, w_gate, preferred_element_type=jnp.float32)
    pre_up = jnp.dot(rows, w_up, preferred_element_type=jnp.float32)
    activated, act_slope = silu_parts(pre_gate)
    hidden = (activated * pre_up).astype(jnp.bfloat16)
    contract_hidden = (((1,), (1,)), ((), ()))
    projected = jnp.dot(grads_in, w_down, preferred_element_type=jnp.float32)
    gate_rows = jnp.sum(hidden.astype(jnp.float32) * projected, axis=1).astype(jnp.bfloat16)
    scaled_grad = (gates[:, None] * grads_in.astype(jnp.float32)).astype(jnp.bfloat16)
    hidden_grad = jnp.dot(scaled_grad, w_down, preferred_element_type=jnp.float32)
    gate_delta = (hidden_grad * pre_up * act_slope).astype(jnp.bfloat16)
    up_delta = (hidden_grad * activated).astype(jnp.bfloat16)
    both_delta = jnp.concatenate([gate_delta, up_delta], axis=1)
    row_grad = lax.dot_general(
        both_delta, w_both, contract_hidden, preferred_element_type=jnp.float32
    )
    row_grad = row_grad.astype(jnp.bfloat16)
    contract_rows = (((0,), (0,)), ((), ()))
    grad_gate = lax.dot_general(rows, gate_delta, contract_rows, preferred_element_type=jnp.float32)
    grad_up = lax.dot_general(rows, up_delta, contract_rows, preferred_element_type=jnp.float32)
    grad_down = lax.dot_general(
        scaled_grad, hidden, contract_rows, preferred_element_type=jnp.float32
    )
    part = jnp.stack([grad_gate, grad_up, grad_down], axis=1).astype(jnp.bfloat16)
    if groups == 2:
        row_half = part.shape[0] // 2
        first_half = lax.axis_index("dp") == 0
        keep = jnp.where(first_half, part[:row_half], part[row_half:])
        give = jnp.where(first_half, part[row_half:], part[:row_half])
        got = lax.ppermute(give, "dp", [(0, 1), (1, 0)])
        grad = (keep.astype(jnp.float32) + got.astype(jnp.float32)) * (1.0 / groups)
    else:
        grad = lax.psum_scatter(
            part, "dp", scatter_dimension=0, tiled=True
        ).astype(jnp.float32) * (1.0 / groups)
    grad = grad[None]
    first_moment = jnp.where(swapped, their_moments[0], first_moment)
    second_moment = jnp.where(swapped, their_moments[1], second_moment)
    new_first = (0.9 * first_moment.astype(jnp.float32) + 0.1 * grad).astype(jnp.bfloat16)
    new_second = (0.95 * second_moment.astype(jnp.float32) + 0.05 * grad * grad).astype(
        jnp.bfloat16
    )

    if two_stage:
        back_all = spread(jnp.concatenate([row_grad, with_tile(gate_rows)], axis=1))
        back_rows = back_all[:, :model_width]
        back_gate = back_all[:, model_width].astype(jnp.float32)
        weight_of = jnp.where(slot_hit, gate2[None, :], 0.0)
        weight_of = jnp.sum(weight_of.reshape(half_axis * chunk, 2 * tok_rows, route_count), axis=2)
        partial = lax.dot_general(
            weight_of,
            back_rows.astype(jnp.float32),
            (((0,), (0,)), ((), ())),
            precision=lax.Precision.HIGHEST,
            preferred_element_type=jnp.float32,
        )
        prob2 = jnp.sum(jnp.where(slot_hit, back_gate[:, None], 0.0), axis=0)
        p_partial, p_prob = from_partner(
            (partial[tok_rows:].astype(jnp.bfloat16), prob2[entry_count:].astype(jnp.bfloat16)),
            "expert",
            swap_bit,
        )
        token_grad = (partial[:tok_rows] + p_partial.astype(jnp.float32)).astype(jnp.bfloat16)
        prob_grad = jnp.where(
            in_half[:entry_count], prob2[:entry_count], p_prob.astype(jnp.float32)
        )
        prob_grad = prob_grad.astype(jnp.bfloat16).reshape(tok_rows, route_count)
    else:
        back_rows, back_gate = [
            lax.all_to_all(
                part.reshape((axis_width, slot_cap) + part.shape[1:]),
                "expert",
                split_axis=0,
                concat_axis=0,
                tiled=True,
            )
            for part in (row_grad, gate_rows)
        ]
        gathered = back_rows.reshape(slot_count, model_width)[slot_of].astype(jnp.float32)
        token_grad = (
            (gathered * flat_gate[:, None])
            .reshape(tok_rows, route_count, model_width)
            .sum(axis=1)
            .astype(jnp.bfloat16)
        )
        prob_grad = back_gate.reshape(slot_count)[slot_of].reshape(tok_rows, route_count)
    return (token_grad, prob_grad, weights, grad, new_first, new_second)


def solution(mesh):
    in_specs = (
        P(("dp", "expert"), None),
        P(("dp", "expert"), None),
        P(("dp", "expert"), None),
        P(("dp", "expert"), None),
        P("expert", "dp", None, None),
        P("expert", "dp", None, None),
        P("expert", "dp", None, None),
        P(),
    )
    out_specs = (
        P(("dp", "expert"), None),
        P(("dp", "expert"), None),
        P("expert", "dp", None, None),
        P("expert", "dp", None, None),
        P("expert", "dp", None, None),
        P("expert", "dp", None, None),
    )
    return jax.shard_map(
        on_device, mesh=mesh, in_specs=in_specs, out_specs=out_specs, check_vma=False
    )
```

```python
import jax
import jax.numpy as jnp
from jax import lax
from jax.sharding import PartitionSpec as P


def from_partner(value, axis, bit):
    return lax.ppermute(value, axis, [(i, i ^ 1 << bit) for i in range(lax.axis_size(axis))])


def silu_parts(pre_gate):
    sig = jax.nn.sigmoid(pre_gate)
    return (pre_gate * sig, sig * (1.0 + pre_gate * (1.0 - sig)))


def send_slots(tokens, out_grad, flat_gate, slot_of, slot_cap):
    axis_width = lax.axis_size("expert")
    model_width = tokens.shape[1]
    entry_count = flat_gate.shape[0]
    route_count = entry_count // tokens.shape[0]
    slot_count = axis_width * slot_cap
    slot_hit = jnp.arange(slot_count, dtype=jnp.int32)[:, None] == slot_of[None, :]
    filled = jnp.any(slot_hit, axis=1)
    entry_lanes = jnp.arange(entry_count, dtype=jnp.int32)
    slot_entry = jnp.sum(jnp.where(slot_hit, entry_lanes[None, :], 0), axis=1)
    token_of = slot_entry // route_count
    zero_row = jnp.zeros((), jnp.bfloat16)
    send_rows = jnp.where(filled[:, None], tokens[token_of], zero_row)
    send_grads = jnp.where(filled[:, None], out_grad[token_of], zero_row)
    send_gate = jnp.where(filled, flat_gate[slot_entry], 0.0).astype(jnp.bfloat16)
    moved = [
        lax.all_to_all(
            part.reshape((axis_width, slot_cap) + part.shape[1:]),
            "expert",
            split_axis=0,
            concat_axis=0,
            tiled=True,
        )
        for part in (send_rows, send_grads, send_gate)
    ]
    rows = moved[0].reshape(slot_count, model_width)
    grads_in = moved[1].reshape(slot_count, model_width)
    gates = moved[2].reshape(slot_count).astype(jnp.float32)
    return rows, grads_in, gates


def xor_permute(value, mask):
    return lax.ppermute(value, "expert", [(i, i ^ mask) for i in range(lax.axis_size("expert"))])


def with_tile(column):
    lanes = jnp.arange(128, dtype=jnp.int32)[None, :] == 0
    return jnp.where(lanes, column.astype(jnp.bfloat16)[:, None], jnp.zeros((), jnp.bfloat16))


def entry_ranks(flat_ids, axis_width):
    id_onehot = (flat_ids[:, None] == jnp.arange(axis_width, dtype=jnp.int32)[None, :]).astype(
        jnp.int32
    )
    return jnp.sum((jnp.cumsum(id_onehot, axis=0) - id_onehot) * id_onehot, axis=1)


def on_device(
    tokens, out_grad, expert_ids, gate_probs, weights, first_moment, second_moment, moving_pairs
):
    axis_width = lax.axis_size("expert")
    half_axis = axis_width // 2
    swap_bit = half_axis.bit_length() - 1
    groups = lax.axis_size("dp")
    my_index = lax.axis_index("expert")
    tok_rows, route_count = expert_ids.shape
    model_width = tokens.shape[1]
    entry_count = tok_rows * route_count
    slot_cap = 5 * entry_count // (4 * axis_width)
    slot_count = axis_width * slot_cap
    pair_lanes = jnp.arange(half_axis, dtype=jnp.int32)
    my_move = jnp.sum(jnp.where(pair_lanes == my_index % half_axis, moving_pairs, 0))
    swapped = my_move == 1
    held = jnp.where(swapped, (my_index + half_axis) % axis_width, my_index)

    flat_gate = gate_probs.reshape(-1)
    flat_ids = expert_ids.reshape(-1)

    def holder_of(ids):
        lane_hit = (ids % half_axis)[:, None] == pair_lanes[None, :]
        moves = jnp.sum(jnp.where(lane_hit, moving_pairs[None, :], 0), axis=1)
        return jnp.where(moves == 1, (ids + half_axis) % axis_width, ids)

    two_stage = half_axis <= 8
    if two_stage:
        packed = jnp.concatenate([tokens, out_grad], axis=1)
        small = jnp.concatenate([expert_ids.astype(jnp.float32), gate_probs], axis=1)
        p_packed, p_small, their_weights = from_partner(
            (packed, small, weights), "expert", swap_bit
        )
        p_ids = p_small[:, :route_count].astype(jnp.int32)
        p_gate = p_small[:, route_count:]
        both = jnp.concatenate([packed, p_packed], axis=0)
        ids2 = jnp.concatenate([flat_ids, p_ids.reshape(-1)])
        gate2 = jnp.concatenate([flat_gate, p_gate.reshape(-1)])
        holder2 = holder_of(ids2)
        rank2 = jnp.concatenate(
            [entry_ranks(flat_ids, axis_width), entry_ranks(p_ids.reshape(-1), axis_width)]
        )
        src2 = jnp.arange(2 * entry_count, dtype=jnp.int32) // entry_count
        in_half = holder2 // half_axis == my_index // half_axis
        lane2 = holder2 % half_axis
        chunk = 2 * slot_cap
        slot2 = lane2 * chunk + src2 * slot_cap + rank2
        slot_hit = (
            jnp.arange(half_axis * chunk, dtype=jnp.int32)[:, None] == slot2[None, :]
        ) & in_half[None, :]
        tok_hit = jnp.any(slot_hit.reshape(half_axis * chunk, 2 * tok_rows, route_count), axis=2)
        tok_pick = tok_hit.astype(jnp.bfloat16)
        send_both = jnp.dot(tok_pick, both, preferred_element_type=jnp.float32).astype(
            jnp.bfloat16
        )
        wire2 = gate2.astype(jnp.bfloat16).astype(jnp.float32)
        send_gate = jnp.sum(jnp.where(slot_hit, wire2[None, :], 0.0), axis=1)
        send_all = jnp.concatenate([send_both, with_tile(send_gate)], axis=1)

        halves = [list(range(h * half_axis, (h + 1) * half_axis)) for h in range(2)]

        def spread(value):
            parts = value.reshape((half_axis, chunk) + value.shape[1:])
            moved = lax.all_to_all(
                parts, "expert", 0, 0, tiled=True, axis_index_groups=halves
            )
            return moved.reshape(value.shape)

        recv_all = spread(send_all)
        rows = recv_all[:, :model_width]
        grads_in = recv_all[:, model_width : 2 * model_width]
        gates = recv_all[:, 2 * model_width].astype(jnp.float32)
    else:
        slot_of = holder_of(flat_ids) * slot_cap + entry_ranks(flat_ids, axis_width)
        rows, grads_in, gates = send_slots(tokens, out_grad, flat_gate, slot_of, slot_cap)
    if not two_stage:
        their_weights = from_partner(weights, "expert", swap_bit)
    first_moment, second_moment, _ = lax.optimization_barrier(
        (first_moment, second_moment, their_weights)
    )
    their_moments = from_partner((first_moment, second_moment), "expert", swap_bit)
    weights = jnp.where(swapped, their_weights, weights)
    if groups == 2:
        other = lax.ppermute(weights, "dp", [(0, 1), (1, 0)])
        first_half = lax.axis_index("dp") == 0
        whole = jnp.concatenate(
            [jnp.where(first_half, weights, other), jnp.where(first_half, other, weights)],
            axis=1,
        )[0]
    else:
        whole = lax.all_gather(weights, "dp", axis=1, tiled=True)[0]
    w_gate = whole[:, 0, :]
    w_up = whole[:, 1, :]
    w_down = whole[:, 2, :]
    w_both = jnp.concatenate([w_gate, w_up], axis=1)
    pre_gate = jnp.dot(rows, w_gate, preferred_element_type=jnp.float32)
    pre_up = jnp.dot(rows, w_up, preferred_element_type=jnp.float32)
    activated, act_slope = silu_parts(pre_gate)
    hidden = (activated * pre_up).astype(jnp.bfloat16)
    contract_hidden = (((1,), (1,)), ((), ()))
    projected = jnp.dot(grads_in, w_down, preferred_element_type=jnp.float32)
    gate_rows = jnp.sum(hidden.astype(jnp.float32) * projected, axis=1).astype(jnp.bfloat16)
    scaled_grad = (gates[:, None] * grads_in.astype(jnp.float32)).astype(jnp.bfloat16)
    hidden_grad = jnp.dot(scaled_grad, w_down, preferred_element_type=jnp.float32)
    gate_delta = (hidden_grad * pre_up * act_slope).astype(jnp.bfloat16)
    up_delta = (hidden_grad * activated).astype(jnp.bfloat16)
    both_delta = jnp.concatenate([gate_delta, up_delta], axis=1)
    row_grad = lax.dot_general(
        both_delta, w_both, contract_hidden, preferred_element_type=jnp.float32
    )
    row_grad = row_grad.astype(jnp.bfloat16)
    contract_rows = (((0,), (0,)), ((), ()))
    grad_gate = lax.dot_general(rows, gate_delta, contract_rows, preferred_element_type=jnp.float32)
    grad_up = lax.dot_general(rows, up_delta, contract_rows, preferred_element_type=jnp.float32)
    grad_down = lax.dot_general(
        scaled_grad, hidden, contract_rows, preferred_element_type=jnp.float32
    )
    part = jnp.stack([grad_gate, grad_up, grad_down], axis=1).astype(jnp.bfloat16)
    if groups == 2:
        row_half = part.shape[0] // 2
        first_half = lax.axis_index("dp") == 0
        keep = jnp.where(first_half, part[:row_half], part[row_half:])
        give = jnp.where(first_half, part[row_half:], part[:row_half])
        got = lax.ppermute(give, "dp", [(0, 1), (1, 0)])
        grad = (keep.astype(jnp.float32) + got.astype(jnp.float32)) * (1.0 / groups)
    else:
        grad = lax.psum_scatter(
            part, "dp", scatter_dimension=0, tiled=True
        ).astype(jnp.float32) * (1.0 / groups)
    grad = grad[None]
    first_moment = jnp.where(swapped, their_moments[0], first_moment)
    second_moment = jnp.where(swapped, their_moments[1], second_moment)
    new_first = (0.9 * first_moment.astype(jnp.float32) + 0.1 * grad).astype(jnp.bfloat16)
    new_second = (0.95 * second_moment.astype(jnp.float32) + 0.05 * grad * grad).astype(
        jnp.bfloat16
    )

    if two_stage:
        back_all = spread(jnp.concatenate([row_grad, with_tile(gate_rows)], axis=1))
        back_rows = back_all[:, :model_width]
        back_gate = back_all[:, model_width].astype(jnp.float32)
        weight_of = jnp.where(slot_hit, gate2[None, :], 0.0)
        weight_of = jnp.sum(weight_of.reshape(half_axis * chunk, 2 * tok_rows, route_count), axis=2)
        partial = lax.dot_general(
            weight_of,
            back_rows.astype(jnp.float32),
            (((0,), (0,)), ((), ())),
            precision=lax.Precision.HIGHEST,
            preferred_element_type=jnp.float32,
        )
        prob2 = jnp.sum(jnp.where(slot_hit, back_gate[:, None], 0.0), axis=0)
        prob_tile = jnp.concatenate(
            [
                prob2[entry_count:].reshape(tok_rows, route_count),
                jnp.zeros((tok_rows, 128 - route_count), jnp.float32),
            ],
            axis=1,
        )
        p_back = from_partner(
            jnp.concatenate([partial[tok_rows:], prob_tile], axis=1).astype(jnp.bfloat16),
            "expert",
            swap_bit,
        )
        p_partial = p_back[:, :model_width]
        p_prob = p_back[:, model_width : model_width + route_count].reshape(-1)
        token_grad = (partial[:tok_rows] + p_partial.astype(jnp.float32)).astype(jnp.bfloat16)
        prob_grad = jnp.where(
            in_half[:entry_count], prob2[:entry_count], p_prob.astype(jnp.float32)
        )
        prob_grad = prob_grad.astype(jnp.bfloat16).reshape(tok_rows, route_count)
    else:
        back_rows, back_gate = [
            lax.all_to_all(
                part.reshape((axis_width, slot_cap) + part.shape[1:]),
                "expert",
                split_axis=0,
                concat_axis=0,
                tiled=True,
            )
            for part in (row_grad, gate_rows)
        ]
        gathered = back_rows.reshape(slot_count, model_width)[slot_of].astype(jnp.float32)
        token_grad = (
            (gathered * flat_gate[:, None])
            .reshape(tok_rows, route_count, model_width)
            .sum(axis=1)
            .astype(jnp.bfloat16)
        )
        prob_grad = back_gate.reshape(slot_count)[slot_of].reshape(tok_rows, route_count)
    return (token_grad, prob_grad, weights, grad, new_first, new_second)


def solution(mesh):
    in_specs = (
        P(("dp", "expert"), None),
        P(("dp", "expert"), None),
        P(("dp", "expert"), None),
        P(("dp", "expert"), None),
        P("expert", "dp", None, None),
        P("expert", "dp", None, None),
        P("expert", "dp", None, None),
        P(),
    )
    out_specs = (
        P(("dp", "expert"), None),
        P(("dp", "expert"), None),
        P("expert", "dp", None, None),
        P("expert", "dp", None, None),
        P("expert", "dp", None, None),
        P("expert", "dp", None, None),
    )
    return jax.shard_map(
        on_device, mesh=mesh, in_specs=in_specs, out_specs=out_specs, check_vma=False
    )
```
